32 devices in a mesh: mx: 8 (over z, core), my: 2 (over y), vz: 2 (over x).
Axes of the slice: x: 2, y: 2, z: 4, core: 2. Of those that a mesh axis runs over, the one named last changes fastest.
Arguments:
- viscosity: float32 [16, 128, 256], P('vz', 'mx', 'my'), may hold values from 0.1 to 2.5
- friction: float32 [128, 256], P('mx', 'my'), may hold values from 0.3 to 3
- base_velocity: float32 [2, 128, 256], P(None, 'mx', 'my'), may hold values from -6 to 6
- grounded: int32 [128, 256], P('mx', 'my'), may hold values 0 or 1
- ice_free: int32 [128, 256], P('mx', 'my'), may hold values 0 or 1
- direction: float32 [128, 256], P('mx', 'my'), may hold values from -6 to 6
Outputs:
- hess_action: float32 [128, 256], P('mx', 'my')
- velocity_step: float32 [2, 16, 128, 256], P(None, 'vz', 'mx', 'my')
The draws below stay inside these ranges and needn't reach their ends.
All inputs are finite; a program needn't handle non-finite values. No bound on the sum of `grounded` or of `ice_free` on one device may be relied on, other than what follows from the above.
Results may differ from the reference program's by a relative error of at most 0.00002.
Values sent between devices are 32-bit elements; how exact they have to be, the bound alone decides.
No kernel may reach another device: no remote copies, remote signals or barrier semaphores. Data moves between devices by JAX's collectives and lax.ppermute only.
A program may use at most 64 MiB of HBM per device.

```python
import math
import jax
import jax.numpy as jnp

LAYERS = 16
STEPS = 16
SWEEPS = 2
NX = 128
NY = 256


def with_ends(result, key, least, largest):
    place = [jax.random.randint(jax.random.fold_in(key, axis), (), 0, length) for axis, length in enumerate(result.shape)]
    longest = result.shape.index(max(result.shape))
    beside = place[:longest] + [(place[longest] + 1) % result.shape[longest]] + place[longest + 1:]
    return result.at[tuple(place)].set(least).at[tuple(beside)].set(largest)


def block_levels(rng, shape, pieces, smallest, top_value):
    factor_of = 1.0
    for axis_at, blocks in pieces:
        steps = jax.random.uniform(jax.random.fold_in(jax.random.fold_in(rng, 6), axis_at), (blocks,), jnp.float32, smallest / len(pieces), top_value / len(pieces))
        factor_of = factor_of * jnp.repeat(jnp.exp(steps), shape[axis_at] // blocks).reshape((-1,) + (1,) * (len(shape) - 1 - axis_at))
    return factor_of


def scatter_about(rng, extent, scale, reach, pieces=(), kind=jnp.bfloat16):
    gain = block_levels(rng, extent, pieces, -0.22, 0.18) if pieces else 1.0
    result = jax.random.normal(rng, extent, jnp.float32) * scale * gain
    return jnp.minimum(jnp.maximum(result, -reach), reach).astype(kind)


def setup_inputs(seed: int = 0) -> dict:
    key_of = jax.random.split(jax.random.key(seed), 7)
    viscosity = jnp.clip(jnp.exp(math.log(2.5) - 3.218876 * jax.random.uniform(key_of[0], (LAYERS, NX, NY), jnp.float32) ** block_levels(key_of[0], (LAYERS, NX, NY), ((0, 2), (1, 8), (2, 2)), -0.2, 0.2)), 0.1, 2.5)
    friction = jnp.clip(jnp.exp(math.log(3.0) - 2.3025851 * jax.random.uniform(key_of[1], (NX, NY), jnp.float32) ** block_levels(key_of[1], (NX, NY), ((0, 8), (1, 2)), -0.2, 0.2)), 0.3, 3.0)
    base_velocity = scatter_about(key_of[2], (2, NX, NY), 1.0, 6.0, ((1, 8), (2, 2)), jnp.float32)
    grounded = with_ends((jax.random.randint(key_of[3], (NX, NY), 0, 4) < 3).astype(jnp.int32), jax.random.fold_in(key_of[3], 1), 0, 1)
    ice_free = with_ends((jax.random.randint(key_of[4], (NX, NY), 0, 8) < 1).astype(jnp.int32), jax.random.fold_in(key_of[4], 1), 0, 1)
    direction = scatter_about(key_of[5], (NX, NY), 1.0, 6.0, ((0, 8), (1, 2)), jnp.float32)
    return dict(viscosity=viscosity, friction=friction, base_velocity=base_velocity, grounded=grounded, ice_free=ice_free, direction=direction)


weight_z = 128.0
shift_mass = 0.05
theta_center = 1.05
delta_half = 0.95
obs_weight = 200.0
reg_weight = 0.5


def harmonic(left, right):
    return 2.0 * left * right / (left + right)


def reference(viscosity, friction, base_velocity, grounded, ice_free, direction):
    act = (1 - ice_free).astype(jnp.float32)
    ground = grounded.astype(jnp.float32)
    padded_eta = jnp.pad(viscosity, 1)
    core = viscosity
    c_zm = weight_z * harmonic(core, padded_eta[:-2, 1:-1, 1:-1])
    c_zp = weight_z * harmonic(core, padded_eta[2:, 1:-1, 1:-1])
    c_xm = harmonic(core, padded_eta[1:-1, :-2, 1:-1])
    c_xp = harmonic(core, padded_eta[1:-1, 2:, 1:-1])
    c_ym = harmonic(core, padded_eta[1:-1, 1:-1, :-2])
    c_yp = harmonic(core, padded_eta[1:-1, 1:-1, 2:])
    basal = jnp.zeros_like(core).at[0].set(ground * friction)
    diag = c_zm + c_zp + c_xm + c_xp + c_ym + c_yp + shift_mass * core + basal
    jacobi = 1.0 / (act * diag + 1.0 - act)

    def operate(field):
        masked = field * act
        pad = jnp.pad(masked, ((0, 0), (1, 1), (1, 1), (1, 1)))
        beside_all = c_zm * pad[:, :-2, 1:-1, 1:-1] + c_zp * pad[:, 2:, 1:-1, 1:-1]
        beside_all = beside_all + c_xm * pad[:, 1:-1, :-2, 1:-1] + c_xp * pad[:, 1:-1, 2:, 1:-1]
        beside_all = beside_all + c_ym * pad[:, 1:-1, 1:-1, :-2] + c_yp * pad[:, 1:-1, 1:-1, 2:]
        return act * (diag * masked - beside_all) + (1.0 - act) * field

    def chebyshev(rhs):
        sigma = theta_center / delta_half
        iterate = jnp.zeros_like(rhs)
        for sweep in range(SWEEPS):
            resid = rhs if sweep == 0 else rhs - operate(iterate)
            rho = 1.0 / sigma
            step_dir = jacobi * resid / theta_center
            for inner in range(STEPS - 1):
                iterate = iterate + step_dir
                resid = rhs - operate(iterate)
                rho_new = 1.0 / (2.0 * sigma - rho)
                step_dir = (rho_new * rho) * step_dir + (2.0 * rho_new / delta_half) * (jacobi * resid)
                rho = rho_new
            iterate = iterate + step_dir
        return iterate

    forcing = jnp.zeros((2,) + core.shape, jnp.float32)
    forcing = forcing.at[:, 0].set(-(ground * friction * direction)[None] * base_velocity)
    forcing = forcing * act
    velocity_step = chebyshev(forcing)
    column = jnp.sum(velocity_step, axis=1) / LAYERS
    adjoint_rhs = obs_weight * act * jnp.broadcast_to(column[:, None], velocity_step.shape)
    adjoint = chebyshev(adjoint_rhs)
    bed_term = ground * friction * jnp.sum(base_velocity * adjoint[:, 0], axis=0)
    pad_dir = jnp.pad(direction, 1)
    lap = 4.0 * direction - pad_dir[:-2, 1:-1] - pad_dir[2:, 1:-1] - pad_dir[1:-1, :-2] - pad_dir[1:-1, 2:]
    hess_action = -bed_term + reg_weight * lap
    return hess_action, velocity_step
```

```python
import jax
import jax.numpy as jnp
from jax import lax
from jax.sharding import PartitionSpec as P

LAYERS = 16
STEPS = 16
SWEEPS = 2
HALO = 16

weight_z = 128.0
shift_mass = 0.05
theta_center = 1.05
delta_half = 0.95
obs_weight = 200.0
reg_weight = 0.5


def step_constants():
    sigma = theta_center / delta_half
    table = []
    for sweep in range(SWEEPS):
        rho = 1.0 / sigma
        if sweep > 0:
            table.append((None, 1.0 / theta_center))
        for inner in range(STEPS - 1):
            rho_new = 1.0 / (2.0 * sigma - rho)
            table.append((rho_new * rho, 2.0 * rho_new / delta_half))
            rho = rho_new
    return table


def harmonic(left, right):
    total = left + right
    safe = jnp.where(total > 0, total, 1.0)
    return jnp.where(total > 0, 2.0 * left * right / safe, 0.0)


def exchange_rows(ext, k, rows, axis):
    count = lax.axis_size("mx")
    forward = [(i, i + 1) for i in range(count - 1)]
    backward = [(i + 1, i) for i in range(count - 1)]
    own = lax.slice_in_dim(ext, k, k + rows, axis=axis)
    low = lax.ppermute(lax.slice_in_dim(own, rows - k, rows, axis=axis), "mx", forward)
    high = lax.ppermute(lax.slice_in_dim(own, 0, k, axis=axis), "mx", backward)
    return jnp.concatenate([low, own, high], axis=axis)


def shift(a, axis, offset):
    n = a.shape[axis]
    zeros_shape = list(a.shape)
    zeros_shape[axis] = 1
    z = jnp.zeros(zeros_shape, a.dtype)
    if offset > 0:
        return jnp.concatenate([lax.slice_in_dim(a, 1, n, axis=axis), z], axis=axis)
    return jnp.concatenate([z, lax.slice_in_dim(a, 0, n - 1, axis=axis)], axis=axis)


def local(viscosity, friction, base_velocity, grounded, ice_free, direction):
    layers_own, rows, cols_own = viscosity.shape
    if cols_own * lax.axis_size("my") > 256:
        return local_split(viscosity, friction, base_velocity, grounded, ice_free, direction)
    k = min(HALO, rows)
    act = (1 - ice_free).astype(jnp.float32)
    bed_coef = grounded.astype(jnp.float32) * friction
    planes = jnp.stack([act, bed_coef, base_velocity[0], base_velocity[1], direction])
    planes = lax.all_gather(planes, "my", axis=2, tiled=True)
    eta = lax.all_gather(viscosity, "my", axis=2, tiled=True)
    eta = lax.all_gather(eta, "vz", axis=0, tiled=True)
    layers = eta.shape[0]
    joined = jnp.concatenate([eta, planes], axis=0)
    zeros_halo = jnp.zeros(joined.shape[:1] + (k,) + joined.shape[2:], joined.dtype)
    joined = exchange_rows(jnp.concatenate([zeros_halo, joined, zeros_halo], axis=1), k, rows, 1)
    eta = joined[:layers]
    act, bed_coef, bv0, bv1, dir_ext = (joined[layers + i] for i in range(5))
    bv = jnp.stack([bv0, bv1])

    c_zm = weight_z * harmonic(eta, shift(eta, 0, -1))
    c_zp = weight_z * harmonic(eta, shift(eta, 0, 1))
    c_xm = harmonic(eta, shift(eta, 1, -1))
    c_xp = harmonic(eta, shift(eta, 1, 1))
    c_ym = harmonic(eta, shift(eta, 2, -1))
    c_yp = harmonic(eta, shift(eta, 2, 1))
    basal = jnp.zeros_like(eta).at[0].set(bed_coef)
    diag = c_zm + c_zp + c_xm + c_xp + c_ym + c_yp + shift_mass * eta + basal
    jacobi = 1.0 / (act * diag + 1.0 - act)

    def operate(field):
        masked = field * act
        beside_all = c_zm * shift(masked, 1, -1) + c_zp * shift(masked, 1, 1)
        beside_all = beside_all + c_xm * shift(masked, 2, -1) + c_xp * shift(masked, 2, 1)
        beside_all = beside_all + c_ym * shift(masked, 3, -1) + c_yp * shift(masked, 3, 1)
        return act * (diag * masked - beside_all) + (1.0 - act) * field

    table = step_constants()
    keep_table = jnp.array([0.0 if kp is None else kp for kp, _ in table], jnp.float32)
    push_table = jnp.array([ps for _, ps in table], jnp.float32)

    def normal_step(position, state_pair, rhs):
        iterate, step_dir = state_pair
        iterate = iterate + step_dir
        resid = rhs - operate(iterate)
        step_dir = keep_table[position] * step_dir + push_table[position] * (jacobi * resid)
        return (iterate, step_dir)

    def chebyshev(rhs):
        iterate = jnp.zeros_like(rhs)
        step_dir = jacobi * rhs / theta_center
        since = 1
        run = []

        def flush(state_pair):
            if len(run) == 1:
                return normal_step(run[0], state_pair, rhs)
            if run:
                return lax.fori_loop(
                    run[0], run[-1] + 1, lambda i, sp: normal_step(i, sp, rhs), state_pair
                )
            return state_pair

        for position, (keep, push) in enumerate(table):
            if since == k:
                iterate, step_dir = flush((iterate, step_dir))
                run = []
                both = exchange_rows(jnp.stack([iterate, step_dir]), k, rows, 3)
                iterate, step_dir = both[0], both[1]
                since = 0
            if keep is None:
                iterate, step_dir = flush((iterate, step_dir))
                run = []
                iterate = iterate + step_dir
                resid = rhs - operate(iterate)
                step_dir = jacobi * resid / theta_center
            else:
                run.append(position)
            since += 1
        iterate, step_dir = flush((iterate, step_dir))
        return iterate + step_dir

    forcing = jnp.zeros((2,) + eta.shape, jnp.float32)
    forcing = forcing.at[:, 0].set(-(bed_coef * dir_ext)[None] * bv)
    forcing = forcing * act
    velocity_ext = chebyshev(forcing)
    column = jnp.sum(velocity_ext, axis=1) / layers
    column = exchange_rows(column, k, rows, 1)
    adjoint_rhs = obs_weight * act * jnp.broadcast_to(column[:, None], velocity_ext.shape)
    adjoint = chebyshev(adjoint_rhs)

    bed_term = bed_coef * jnp.sum(bv * adjoint[:, 0], axis=0)
    lap = (
        4.0 * dir_ext
        - shift(dir_ext, 0, -1)
        - shift(dir_ext, 0, 1)
        - shift(dir_ext, 1, -1)
        - shift(dir_ext, 1, 1)
    )
    hess_ext = -bed_term + reg_weight * lap
    col0 = lax.axis_index("my") * cols_own
    layer0 = lax.axis_index("vz") * layers_own
    hess_action = lax.dynamic_slice(hess_ext, (k, col0), (rows, cols_own))
    velocity_step = lax.dynamic_slice(
        velocity_ext, (0, layer0, k, col0), (2, layers_own, rows, cols_own)
    )
    return (hess_action, velocity_step)


def plain_harmonic(left, right):
    return 2.0 * left * right / (left + right)


def padded(block, sides, width):
    for axis, dim in sides:
        count = lax.axis_size(axis)
        forward = [(i, i + 1) for i in range(count - 1)]
        backward = [(target, source) for source, target in forward]
        low = lax.ppermute(
            lax.slice_in_dim(block, block.shape[dim] - width, None, axis=dim), axis, forward
        )
        high = lax.ppermute(lax.slice_in_dim(block, 0, width, axis=dim), axis, backward)
        block = jnp.concatenate([low, block, high], axis=dim)
    return block


def coefficients(padded_eta):
    core = padded_eta[1:-1, 1:-1, 1:-1]
    coefs = (
        weight_z * plain_harmonic(core, padded_eta[:-2, 1:-1, 1:-1]),
        weight_z * plain_harmonic(core, padded_eta[2:, 1:-1, 1:-1]),
        plain_harmonic(core, padded_eta[1:-1, :-2, 1:-1]),
        plain_harmonic(core, padded_eta[1:-1, 2:, 1:-1]),
        plain_harmonic(core, padded_eta[1:-1, 1:-1, :-2]),
        plain_harmonic(core, padded_eta[1:-1, 1:-1, 2:]),
    )
    return (core, coefs)


def stencil(pad, coefs, diag, masked, act, field):
    beside_all = coefs[0] * pad[:, :-2, 1:-1, 1:-1] + coefs[1] * pad[:, 2:, 1:-1, 1:-1]
    beside_all = beside_all + coefs[2] * pad[:, 1:-1, :-2, 1:-1] + coefs[3] * pad[:, 1:-1, 2:, 1:-1]
    beside_all = beside_all + coefs[4] * pad[:, 1:-1, 1:-1, :-2] + coefs[5] * pad[:, 1:-1, 1:-1, 2:]
    return act * (diag * masked - beside_all) + (1.0 - act) * field


def operate_split(field, coefs, diag, act):
    masked = field * act
    pad = padded(masked, (("mx", 2), ("my", 3), ("vz", 1)), 1)
    return stencil(pad, coefs, diag, masked, act, field)


def chebyshev_split(rhs, operate, jacobi):
    sigma = theta_center / delta_half
    rho = 1.0 / sigma
    keep_list = []
    push_list = []
    for inner in range(STEPS - 1):
        rho_new = 1.0 / (2.0 * sigma - rho)
        keep_list.append(rho_new * rho)
        push_list.append(2.0 * rho_new / delta_half)
        rho = rho_new
    keep_table = jnp.array(keep_list, jnp.float32)
    push_table = jnp.array(push_list, jnp.float32)

    def inner_step(position, state_pair):
        iterate, step_dir = state_pair
        iterate = iterate + step_dir
        resid = rhs - operate(iterate)
        step_dir = keep_table[position] * step_dir + push_table[position] * (jacobi * resid)
        return (iterate, step_dir)

    iterate = jnp.zeros_like(rhs)
    for sweep in range(SWEEPS):
        resid = rhs if sweep == 0 else rhs - operate(iterate)
        step_dir = jacobi * resid / theta_center
        iterate, step_dir = lax.fori_loop(0, STEPS - 1, inner_step, (iterate, step_dir))
        iterate = iterate + step_dir
    return iterate


def local_split(viscosity, friction, base_velocity, grounded, ice_free, direction):
    act = (1 - ice_free).astype(jnp.float32)
    ground = grounded.astype(jnp.float32)
    layer_index = lax.axis_index("vz")
    column_devices = lax.axis_size("vz")
    bed_coef = ground * friction
    padded_eta = padded(viscosity, (("mx", 1), ("my", 2), ("vz", 0)), 1)
    on_bed = jnp.where(layer_index == 0, 1.0, 0.0).astype(jnp.float32)
    core, coefs = coefficients(padded_eta)
    basal = jnp.zeros_like(core).at[0].set(on_bed * bed_coef)
    diag = (
        coefs[0] + coefs[1] + coefs[2] + coefs[3] + coefs[4] + coefs[5] + shift_mass * core + basal
    )
    jacobi = 1.0 / (act * diag + 1.0 - act)
    forcing = jnp.zeros((2,) + core.shape, jnp.float32)
    forcing = forcing.at[:, 0].set(-(on_bed * bed_coef * direction)[None] * base_velocity)
    forcing = forcing * act
    pad_dir = padded(direction, (("mx", 0), ("my", 1)), 1)
    lap = (
        4.0 * direction
        - pad_dir[:-2, 1:-1]
        - pad_dir[2:, 1:-1]
        - pad_dir[1:-1, :-2]
        - pad_dir[1:-1, 2:]
    )

    def operate(field):
        return operate_split(field, coefs, diag, act)

    velocity_step = chebyshev_split(forcing, operate, jacobi)
    column = lax.psum(jnp.sum(velocity_step, axis=1), "vz") / LAYERS
    adjoint_rhs = obs_weight * act * jnp.broadcast_to(column[:, None], velocity_step.shape)
    adjoint = chebyshev_split(adjoint_rhs, operate, jacobi)
    on_top = jnp.where(layer_index == column_devices - 1, 1.0, 0.0).astype(jnp.float32)
    bed_part = on_bed * bed_coef * jnp.sum(base_velocity * adjoint[:, 0], axis=0)
    own_part = on_top * (reg_weight * lap) - bed_part
    hess_action = lax.psum(own_part, "vz")
    return (hess_action, velocity_step)


def solution(mesh):
    return jax.shard_map(
        local,
        mesh=mesh,
        in_specs=(
            P("vz", "mx", "my"),
            P("mx", "my"),
            P(None, "mx", "my"),
            P("mx", "my"),
            P("mx", "my"),
            P("mx", "my"),
        ),
        out_specs=(P("mx", "my"), P(None, "vz", "mx", "my")),
        check_vma=False,
    )
```

```python
import jax
import jax.numpy as jnp
from jax import lax
from jax.experimental import pallas as pl
from jax.experimental.pallas import tpu as pltpu
from jax.sharding import PartitionSpec as P

LAYERS = 16
STEPS = 16
SWEEPS = 2
HALO = 16

weight_z = 128.0
shift_mass = 0.05
theta_center = 1.05
delta_half = 0.95
obs_weight = 200.0
reg_weight = 0.5


def step_constants():
    sigma = theta_center / delta_half
    table = []
    for sweep in range(SWEEPS):
        rho = 1.0 / sigma
        if sweep > 0:
            table.append((None, 1.0 / theta_center))
        for inner in range(STEPS - 1):
            rho_new = 1.0 / (2.0 * sigma - rho)
            table.append((rho_new * rho, 2.0 * rho_new / delta_half))
            rho = rho_new
    return table


def harmonic(left, right):
    total = left + right
    safe = jnp.where(total > 0, total, 1.0)
    return jnp.where(total > 0, 2.0 * left * right / safe, 0.0)


def exchange_rows(ext, k, rows, axis):
    count = lax.axis_size("mx")
    forward = [(i, i + 1) for i in range(count - 1)]
    backward = [(i + 1, i) for i in range(count - 1)]
    own = lax.slice_in_dim(ext, k, k + rows, axis=axis)
    low = lax.ppermute(lax.slice_in_dim(own, rows - k, rows, axis=axis), "mx", forward)
    high = lax.ppermute(lax.slice_in_dim(own, 0, k, axis=axis), "mx", backward)
    return jnp.concatenate([low, own, high], axis=axis)


def shift(a, axis, offset):
    n = a.shape[axis]
    zeros_shape = list(a.shape)
    zeros_shape[axis] = 1
    z = jnp.zeros(zeros_shape, a.dtype)
    if offset > 0:
        return jnp.concatenate([lax.slice_in_dim(a, 1, n, axis=axis), z], axis=axis)
    return jnp.concatenate([z, lax.slice_in_dim(a, 0, n - 1, axis=axis)], axis=axis)


def segment_kernel(steps, op_ref, act_ref, rhs_ref, x_in, d_in, x_ref, d_ref, m_ref):
    comps, layers = rhs_ref.shape[0], rhs_ref.shape[1]
    rows, cols = act_ref.shape
    x_ref[...] = x_in[...]
    d_ref[...] = d_in[...]
    zero = jnp.zeros((rows, cols), jnp.float32)
    for c in range(comps):
        m_ref[c, 0] = zero
        m_ref[c, layers + 1] = zero

    for keep, push in steps:

        def advance(layer, carry):
            for c in range(comps):
                moved = x_ref[c, layer] + d_ref[c, layer]
                x_ref[c, layer] = moved
                m_ref[c, layer + 1] = moved * act_ref[...]
            return carry

        lax.fori_loop(0, layers, advance, 0)

        def update(layer, carry):
            act = act_ref[...]
            for c in range(comps):
                centre = m_ref[c, layer + 1]
                beside = op_ref[0, layer] * m_ref[c, layer] + op_ref[1, layer] * m_ref[c, layer + 2]
                beside = beside + op_ref[2, layer] * pltpu.roll(centre, 1, 0)
                beside = beside + op_ref[3, layer] * pltpu.roll(centre, rows - 1, 0)
                beside = beside + op_ref[4, layer] * pltpu.roll(centre, 1, 1)
                beside = beside + op_ref[5, layer] * pltpu.roll(centre, cols - 1, 1)
                applied = act * (op_ref[6, layer] * centre - beside) + (1.0 - act) * x_ref[c, layer]
                resid = rhs_ref[c, layer] - applied
                if keep is None:
                    d_ref[c, layer] = op_ref[7, layer] * resid / theta_center
                else:
                    d_ref[c, layer] = keep * d_ref[c, layer] + push * (op_ref[7, layer] * resid)
            return carry

        lax.fori_loop(0, layers, update, 0)


def run_segment(steps, op_stack, act, rhs, iterate, step_dir):
    comps, layers, rows, cols = rhs.shape
    vmem = pl.BlockSpec(memory_space=pltpu.VMEM)
    cells = comps * layers * rows * cols
    return pl.pallas_call(
        lambda *refs: segment_kernel(steps, *refs),
        out_shape=(
            jax.ShapeDtypeStruct(rhs.shape, jnp.float32),
            jax.ShapeDtypeStruct(rhs.shape, jnp.float32),
        ),
        in_specs=[vmem] * 5,
        out_specs=(vmem, vmem),
        scratch_shapes=[pltpu.VMEM((comps, layers + 2, rows, cols), jnp.float32)],
        cost_estimate=pl.CostEstimate(
            flops=30 * cells * len(steps), bytes_accessed=4 * cells * 9, transcendentals=0
        ),
    )(op_stack, act, rhs, iterate, step_dir)


def local(viscosity, friction, base_velocity, grounded, ice_free, direction):
    layers_own, rows, cols_own = viscosity.shape
    if cols_own * lax.axis_size("my") > 256:
        return local_split(viscosity, friction, base_velocity, grounded, ice_free, direction)
    k = min(HALO, rows)
    act = (1 - ice_free).astype(jnp.float32)
    bed_coef = grounded.astype(jnp.float32) * friction
    planes = jnp.stack([act, bed_coef, base_velocity[0], base_velocity[1], direction])
    planes = lax.all_gather(planes, "my", axis=2, tiled=True)
    eta = lax.all_gather(viscosity, "my", axis=2, tiled=True)
    eta = lax.all_gather(eta, "vz", axis=0, tiled=True)
    layers = eta.shape[0]
    joined = jnp.concatenate([eta, planes], axis=0)
    zeros_halo = jnp.zeros(joined.shape[:1] + (k,) + joined.shape[2:], joined.dtype)
    joined = exchange_rows(jnp.concatenate([zeros_halo, joined, zeros_halo], axis=1), k, rows, 1)
    eta = joined[:layers]
    act, bed_coef, bv0, bv1, dir_ext = (joined[layers + i] for i in range(5))
    bv = jnp.stack([bv0, bv1])

    c_zm = weight_z * harmonic(eta, shift(eta, 0, -1))
    c_zp = weight_z * harmonic(eta, shift(eta, 0, 1))
    c_xm = harmonic(eta, shift(eta, 1, -1))
    c_xp = harmonic(eta, shift(eta, 1, 1))
    c_ym = harmonic(eta, shift(eta, 2, -1))
    c_yp = harmonic(eta, shift(eta, 2, 1))
    basal = jnp.zeros_like(eta).at[0].set(bed_coef)
    diag = c_zm + c_zp + c_xm + c_xp + c_ym + c_yp + shift_mass * eta + basal
    jacobi = 1.0 / (act * diag + 1.0 - act)

    op_stack = jnp.stack([c_zm, c_zp, c_xm, c_xp, c_ym, c_yp, diag, jacobi])
    table = step_constants()

    def chebyshev(rhs):
        iterate = jnp.zeros_like(rhs)
        step_dir = jacobi * rhs / theta_center
        since = 1
        run = []
        for keep, push in table:
            if since == k:
                iterate, step_dir = run_segment(tuple(run), op_stack, act, rhs, iterate, step_dir)
                run = []
                both = exchange_rows(jnp.stack([iterate, step_dir]), k, rows, 3)
                iterate, step_dir = both[0], both[1]
                since = 0
            run.append((keep, push))
            since += 1
        iterate, step_dir = run_segment(tuple(run), op_stack, act, rhs, iterate, step_dir)
        return iterate + step_dir

    forcing = jnp.zeros((2,) + eta.shape, jnp.float32)
    forcing = forcing.at[:, 0].set(-(bed_coef * dir_ext)[None] * bv)
    forcing = forcing * act
    velocity_ext = chebyshev(forcing)
    column = jnp.sum(velocity_ext, axis=1) / layers
    column = exchange_rows(column, k, rows, 1)
    adjoint_rhs = obs_weight * act * jnp.broadcast_to(column[:, None], velocity_ext.shape)
    adjoint = chebyshev(adjoint_rhs)

    bed_term = bed_coef * jnp.sum(bv * adjoint[:, 0], axis=0)
    lap = (
        4.0 * dir_ext
        - shift(dir_ext, 0, -1)
        - shift(dir_ext, 0, 1)
        - shift(dir_ext, 1, -1)
        - shift(dir_ext, 1, 1)
    )
    hess_ext = -bed_term + reg_weight * lap
    col0 = lax.axis_index("my") * cols_own
    layer0 = lax.axis_index("vz") * layers_own
    hess_action = lax.dynamic_slice(hess_ext, (k, col0), (rows, cols_own))
    velocity_step = lax.dynamic_slice(
        velocity_ext, (0, layer0, k, col0), (2, layers_own, rows, cols_own)
    )
    return (hess_action, velocity_step)


def plain_harmonic(left, right):
    return 2.0 * left * right / (left + right)


def padded(block, sides, width):
    for axis, dim in sides:
        count = lax.axis_size(axis)
        forward = [(i, i + 1) for i in range(count - 1)]
        backward = [(target, source) for source, target in forward]
        low = lax.ppermute(
            lax.slice_in_dim(block, block.shape[dim] - width, None, axis=dim), axis, forward
        )
        high = lax.ppermute(lax.slice_in_dim(block, 0, width, axis=dim), axis, backward)
        block = jnp.concatenate([low, block, high], axis=dim)
    return block


def coefficients(padded_eta):
    core = padded_eta[1:-1, 1:-1, 1:-1]
    coefs = (
        weight_z * plain_harmonic(core, padded_eta[:-2, 1:-1, 1:-1]),
        weight_z * plain_harmonic(core, padded_eta[2:, 1:-1, 1:-1]),
        plain_harmonic(core, padded_eta[1:-1, :-2, 1:-1]),
        plain_harmonic(core, padded_eta[1:-1, 2:, 1:-1]),
        plain_harmonic(core, padded_eta[1:-1, 1:-1, :-2]),
        plain_harmonic(core, padded_eta[1:-1, 1:-1, 2:]),
    )
    return (core, coefs)


def stencil(pad, coefs, diag, masked, act, field):
    beside_all = coefs[0] * pad[:, :-2, 1:-1, 1:-1] + coefs[1] * pad[:, 2:, 1:-1, 1:-1]
    beside_all = beside_all + coefs[2] * pad[:, 1:-1, :-2, 1:-1] + coefs[3] * pad[:, 1:-1, 2:, 1:-1]
    beside_all = beside_all + coefs[4] * pad[:, 1:-1, 1:-1, :-2] + coefs[5] * pad[:, 1:-1, 1:-1, 2:]
    return act * (diag * masked - beside_all) + (1.0 - act) * field


def operate_split(field, coefs, diag, act):
    masked = field * act
    pad = padded(masked, (("mx", 2), ("my", 3), ("vz", 1)), 1)
    return stencil(pad, coefs, diag, masked, act, field)


def chebyshev_split(rhs, operate, jacobi):
    sigma = theta_center / delta_half
    rho = 1.0 / sigma
    keep_list = []
    push_list = []
    for inner in range(STEPS - 1):
        rho_new = 1.0 / (2.0 * sigma - rho)
        keep_list.append(rho_new * rho)
        push_list.append(2.0 * rho_new / delta_half)
        rho = rho_new
    keep_table = jnp.array(keep_list, jnp.float32)
    push_table = jnp.array(push_list, jnp.float32)

    def inner_step(position, state_pair):
        iterate, step_dir = state_pair
        iterate = iterate + step_dir
        resid = rhs - operate(iterate)
        step_dir = keep_table[position] * step_dir + push_table[position] * (jacobi * resid)
        return (iterate, step_dir)

    iterate = jnp.zeros_like(rhs)
    for sweep in range(SWEEPS):
        resid = rhs if sweep == 0 else rhs - operate(iterate)
        step_dir = jacobi * resid / theta_center
        iterate, step_dir = lax.fori_loop(0, STEPS - 1, inner_step, (iterate, step_dir))
        iterate = iterate + step_dir
    return iterate


def local_split(viscosity, friction, base_velocity, grounded, ice_free, direction):
    act = (1 - ice_free).astype(jnp.float32)
    ground = grounded.astype(jnp.float32)
    layer_index = lax.axis_index("vz")
    column_devices = lax.axis_size("vz")
    bed_coef = ground * friction
    padded_eta = padded(viscosity, (("mx", 1), ("my", 2), ("vz", 0)), 1)
    on_bed = jnp.where(layer_index == 0, 1.0, 0.0).astype(jnp.float32)
    core, coefs = coefficients(padded_eta)
    basal = jnp.zeros_like(core).at[0].set(on_bed * bed_coef)
    diag = (
        coefs[0] + coefs[1] + coefs[2] + coefs[3] + coefs[4] + coefs[5] + shift_mass * core + basal
    )
    jacobi = 1.0 / (act * diag + 1.0 - act)
    forcing = jnp.zeros((2,) + core.shape, jnp.float32)
    forcing = forcing.at[:, 0].set(-(on_bed * bed_coef * direction)[None] * base_velocity)
    forcing = forcing * act
    pad_dir = padded(direction, (("mx", 0), ("my", 1)), 1)
    lap = (
        4.0 * direction
        - pad_dir[:-2, 1:-1]
        - pad_dir[2:, 1:-1]
        - pad_dir[1:-1, :-2]
        - pad_dir[1:-1, 2:]
    )

    def operate(field):
        return operate_split(field, coefs, diag, act)

    velocity_step = chebyshev_split(forcing, operate, jacobi)
    column = lax.psum(jnp.sum(velocity_step, axis=1), "vz") / LAYERS
    adjoint_rhs = obs_weight * act * jnp.broadcast_to(column[:, None], velocity_step.shape)
    adjoint = chebyshev_split(adjoint_rhs, operate, jacobi)
    on_top = jnp.where(layer_index == column_devices - 1, 1.0, 0.0).astype(jnp.float32)
    bed_part = on_bed * bed_coef * jnp.sum(base_velocity * adjoint[:, 0], axis=0)
    own_part = on_top * (reg_weight * lap) - bed_part
    hess_action = lax.psum(own_part, "vz")
    return (hess_action, velocity_step)


def solution(mesh):
    return jax.shard_map(
        local,
        mesh=mesh,
        in_specs=(
            P("vz", "mx", "my"),
            P("mx", "my"),
            P(None, "mx", "my"),
            P("mx", "my"),
            P("mx", "my"),
            P("mx", "my"),
        ),
        out_specs=(P("mx", "my"), P(None, "vz", "mx", "my")),
        check_vma=False,
    )
```

```python
import jax
import jax.numpy as jnp
from jax import lax
from jax.experimental import pallas as pl
from jax.experimental.pallas import tpu as pltpu
from jax.sharding import PartitionSpec as P

LAYERS = 16
STEPS = 16
SWEEPS = 2
HALO = 16

weight_z = 128.0
shift_mass = 0.05
theta_center = 1.05
delta_half = 0.95
obs_weight = 200.0
reg_weight = 0.5


def step_constants():
    sigma = theta_center / delta_half
    table = []
    for sweep in range(SWEEPS):
        rho = 1.0 / sigma
        if sweep > 0:
            table.append((None, 1.0 / theta_center))
        for inner in range(STEPS - 1):
            rho_new = 1.0 / (2.0 * sigma - rho)
            table.append((rho_new * rho, 2.0 * rho_new / delta_half))
            rho = rho_new
    return table


def harmonic(left, right):
    total = left + right
    safe = jnp.where(total > 0, total, 1.0)
    return jnp.where(total > 0, 2.0 * left * right / safe, 0.0)


def exchange_rows(ext, k, rows, axis):
    count = lax.axis_size("mx")
    forward = [(i, i + 1) for i in range(count - 1)]
    backward = [(i + 1, i) for i in range(count - 1)]
    own = lax.slice_in_dim(ext, k, k + rows, axis=axis)
    low = lax.ppermute(lax.slice_in_dim(own, rows - k, rows, axis=axis), "mx", forward)
    high = lax.ppermute(lax.slice_in_dim(own, 0, k, axis=axis), "mx", backward)
    return jnp.concatenate([low, own, high], axis=axis)


def shift(a, axis, offset):
    n = a.shape[axis]
    zeros_shape = list(a.shape)
    zeros_shape[axis] = 1
    z = jnp.zeros(zeros_shape, a.dtype)
    if offset > 0:
        return jnp.concatenate([lax.slice_in_dim(a, 1, n, axis=axis), z], axis=axis)
    return jnp.concatenate([z, lax.slice_in_dim(a, 0, n - 1, axis=axis)], axis=axis)


def segment_kernel(steps, op_ref, rhs_ref, x_in, d_in, x_ref, d_ref):
    comps, layers = rhs_ref.shape[0], rhs_ref.shape[1]
    rows, cols = rhs_ref.shape[2], rhs_ref.shape[3]
    x_ref[...] = x_in[...]
    d_ref[...] = d_in[...]

    for keep, push in steps:
        for c in range(comps):
            x_ref[c, 1] = x_ref[c, 1] + d_ref[c, 1]

        def update(layer, carry):
            p = layer + 1
            for c in range(comps):
                x_ref[c, p + 1] = x_ref[c, p + 1] + d_ref[c, p + 1]
                centre = x_ref[c, p]
                beside = op_ref[0, layer] * x_ref[c, p - 1] + op_ref[1, layer] * x_ref[c, p + 1]
                beside = beside + op_ref[2, layer] * pltpu.roll(centre, 1, 0)
                beside = beside + op_ref[3, layer] * pltpu.roll(centre, rows - 1, 0)
                beside = beside + op_ref[4, layer] * pltpu.roll(centre, 1, 1)
                beside = beside + op_ref[5, layer] * pltpu.roll(centre, cols - 1, 1)
                resid = rhs_ref[c, layer] - (op_ref[6, layer] * centre - beside)
                if keep is None:
                    d_ref[c, p] = op_ref[7, layer] * resid / theta_center
                else:
                    d_ref[c, p] = keep * d_ref[c, p] + push * (op_ref[7, layer] * resid)
            return carry

        lax.fori_loop(0, layers, update, 0)


def run_segment(steps, op_stack, rhs, iterate, step_dir):
    comps, layers, rows, cols = rhs.shape
    vmem = pl.BlockSpec(memory_space=pltpu.VMEM)
    cells = comps * layers * rows * cols
    return pl.pallas_call(
        lambda *refs: segment_kernel(steps, *refs),
        out_shape=(
            jax.ShapeDtypeStruct(iterate.shape, jnp.float32),
            jax.ShapeDtypeStruct(iterate.shape, jnp.float32),
        ),
        in_specs=[vmem] * 4,
        out_specs=(vmem, vmem),
        cost_estimate=pl.CostEstimate(
            flops=20 * cells * len(steps), bytes_accessed=4 * cells * 9, transcendentals=0
        ),
    )(op_stack, rhs, iterate, step_dir)


def local(viscosity, friction, base_velocity, grounded, ice_free, direction):
    layers_own, rows, cols_own = viscosity.shape
    if cols_own * lax.axis_size("my") > 256:
        return local_split(viscosity, friction, base_velocity, grounded, ice_free, direction)
    k = min(HALO, rows)
    act = (1 - ice_free).astype(jnp.float32)
    bed_coef = grounded.astype(jnp.float32) * friction
    planes = jnp.stack([act, bed_coef, base_velocity[0], base_velocity[1], direction])
    planes = lax.all_gather(planes, "my", axis=2, tiled=True)
    eta = lax.all_gather(viscosity, "my", axis=2, tiled=True)
    eta = lax.all_gather(eta, "vz", axis=0, tiled=True)
    layers = eta.shape[0]
    joined = jnp.concatenate([eta, planes], axis=0)
    zeros_halo = jnp.zeros(joined.shape[:1] + (k,) + joined.shape[2:], joined.dtype)
    joined = exchange_rows(jnp.concatenate([zeros_halo, joined, zeros_halo], axis=1), k, rows, 1)
    eta = joined[:layers]
    act, bed_coef, bv0, bv1, dir_ext = (joined[layers + i] for i in range(5))
    bv = jnp.stack([bv0, bv1])

    c_zm = weight_z * harmonic(eta, shift(eta, 0, -1))
    c_zp = weight_z * harmonic(eta, shift(eta, 0, 1))
    c_xm = harmonic(eta, shift(eta, 1, -1))
    c_xp = harmonic(eta, shift(eta, 1, 1))
    c_ym = harmonic(eta, shift(eta, 2, -1))
    c_yp = harmonic(eta, shift(eta, 2, 1))
    basal = jnp.zeros_like(eta).at[0].set(bed_coef)
    diag = c_zm + c_zp + c_xm + c_xp + c_ym + c_yp + shift_mass * eta + basal
    jacobi = 1.0 / (act * diag + 1.0 - act)

    on = act > 0
    op_stack = jnp.stack(
        [
            act * c_zm,
            act * c_zp,
            act * c_xm * shift(act, 0, -1),
            act * c_xp * shift(act, 0, 1),
            act * c_ym * shift(act, 1, -1),
            act * c_yp * shift(act, 1, 1),
            jnp.where(on, diag, 1.0),
            jacobi,
        ]
    )
    table = step_constants()
    layer_pad = ((0, 0), (1, 1), (0, 0), (0, 0))

    def chebyshev(rhs):
        iterate = jnp.zeros((2, layers + 2) + rhs.shape[2:], jnp.float32)
        step_dir = jnp.pad(jacobi * rhs / theta_center, layer_pad)
        since = 1
        run = []
        for keep, push in table:
            if since == k:
                iterate, step_dir = run_segment(tuple(run), op_stack, rhs, iterate, step_dir)
                run = []
                both = exchange_rows(jnp.stack([iterate, step_dir]), k, rows, 3)
                iterate, step_dir = both[0], both[1]
                since = 0
            run.append((keep, push))
            since += 1
        iterate, step_dir = run_segment(tuple(run), op_stack, rhs, iterate, step_dir)
        return (iterate + step_dir)[:, 1 : layers + 1]

    forcing = jnp.zeros((2,) + eta.shape, jnp.float32)
    forcing = forcing.at[:, 0].set(-(bed_coef * dir_ext)[None] * bv)
    forcing = forcing * act
    velocity_ext = chebyshev(forcing)
    column = jnp.sum(velocity_ext, axis=1) / layers
    column = exchange_rows(column, k, rows, 1)
    adjoint_rhs = obs_weight * act * jnp.broadcast_to(column[:, None], velocity_ext.shape)
    adjoint = chebyshev(adjoint_rhs)

    bed_term = bed_coef * jnp.sum(bv * adjoint[:, 0], axis=0)
    lap = (
        4.0 * dir_ext
        - shift(dir_ext, 0, -1)
        - shift(dir_ext, 0, 1)
        - shift(dir_ext, 1, -1)
        - shift(dir_ext, 1, 1)
    )
    hess_ext = -bed_term + reg_weight * lap
    col0 = lax.axis_index("my") * cols_own
    layer0 = lax.axis_index("vz") * layers_own
    hess_action = lax.dynamic_slice(hess_ext, (k, col0), (rows, cols_own))
    velocity_step = lax.dynamic_slice(
        velocity_ext, (0, layer0, k, col0), (2, layers_own, rows, cols_own)
    )
    return (hess_action, velocity_step)


def plain_harmonic(left, right):
    return 2.0 * left * right / (left + right)


def padded(block, sides, width):
    for axis, dim in sides:
        count = lax.axis_size(axis)
        forward = [(i, i + 1) for i in range(count - 1)]
        backward = [(target, source) for source, target in forward]
        low = lax.ppermute(
            lax.slice_in_dim(block, block.shape[dim] - width, None, axis=dim), axis, forward
        )
        high = lax.ppermute(lax.slice_in_dim(block, 0, width, axis=dim), axis, backward)
        block = jnp.concatenate([low, block, high], axis=dim)
    return block


def coefficients(padded_eta):
    core = padded_eta[1:-1, 1:-1, 1:-1]
    coefs = (
        weight_z * plain_harmonic(core, padded_eta[:-2, 1:-1, 1:-1]),
        weight_z * plain_harmonic(core, padded_eta[2:, 1:-1, 1:-1]),
        plain_harmonic(core, padded_eta[1:-1, :-2, 1:-1]),
        plain_harmonic(core, padded_eta[1:-1, 2:, 1:-1]),
        plain_harmonic(core, padded_eta[1:-1, 1:-1, :-2]),
        plain_harmonic(core, padded_eta[1:-1, 1:-1, 2:]),
    )
    return (core, coefs)


def stencil(pad, coefs, diag, masked, act, field):
    beside_all = coefs[0] * pad[:, :-2, 1:-1, 1:-1] + coefs[1] * pad[:, 2:, 1:-1, 1:-1]
    beside_all = beside_all + coefs[2] * pad[:, 1:-1, :-2, 1:-1] + coefs[3] * pad[:, 1:-1, 2:, 1:-1]
    beside_all = beside_all + coefs[4] * pad[:, 1:-1, 1:-1, :-2] + coefs[5] * pad[:, 1:-1, 1:-1, 2:]
    return act * (diag * masked - beside_all) + (1.0 - act) * field


def operate_split(field, coefs, diag, act):
    masked = field * act
    pad = padded(masked, (("mx", 2), ("my", 3), ("vz", 1)), 1)
    return stencil(pad, coefs, diag, masked, act, field)


def chebyshev_split(rhs, operate, jacobi):
    sigma = theta_center / delta_half
    rho = 1.0 / sigma
    keep_list = []
    push_list = []
    for inner in range(STEPS - 1):
        rho_new = 1.0 / (2.0 * sigma - rho)
        keep_list.append(rho_new * rho)
        push_list.append(2.0 * rho_new / delta_half)
        rho = rho_new
    keep_table = jnp.array(keep_list, jnp.float32)
    push_table = jnp.array(push_list, jnp.float32)

    def inner_step(position, state_pair):
        iterate, step_dir = state_pair
        iterate = iterate + step_dir
        resid = rhs - operate(iterate)
        step_dir = keep_table[position] * step_dir + push_table[position] * (jacobi * resid)
        return (iterate, step_dir)

    iterate = jnp.zeros_like(rhs)
    for sweep in range(SWEEPS):
        resid = rhs if sweep == 0 else rhs - operate(iterate)
        step_dir = jacobi * resid / theta_center
        iterate, step_dir = lax.fori_loop(0, STEPS - 1, inner_step, (iterate, step_dir))
        iterate = iterate + step_dir
    return iterate


def local_split(viscosity, friction, base_velocity, grounded, ice_free, direction):
    act = (1 - ice_free).astype(jnp.float32)
    ground = grounded.astype(jnp.float32)
    layer_index = lax.axis_index("vz")
    column_devices = lax.axis_size("vz")
    bed_coef = ground * friction
    padded_eta = padded(viscosity, (("mx", 1), ("my", 2), ("vz", 0)), 1)
    on_bed = jnp.where(layer_index == 0, 1.0, 0.0).astype(jnp.float32)
    core, coefs = coefficients(padded_eta)
    basal = jnp.zeros_like(core).at[0].set(on_bed * bed_coef)
    diag = (
        coefs[0] + coefs[1] + coefs[2] + coefs[3] + coefs[4] + coefs[5] + shift_mass * core + basal
    )
    jacobi = 1.0 / (act * diag + 1.0 - act)
    forcing = jnp.zeros((2,) + core.shape, jnp.float32)
    forcing = forcing.at[:, 0].set(-(on_bed * bed_coef * direction)[None] * base_velocity)
    forcing = forcing * act
    pad_dir = padded(direction, (("mx", 0), ("my", 1)), 1)
    lap = (
        4.0 * direction
        - pad_dir[:-2, 1:-1]
        - pad_dir[2:, 1:-1]
        - pad_dir[1:-1, :-2]
        - pad_dir[1:-1, 2:]
    )

    def operate(field):
        return operate_split(field, coefs, diag, act)

    velocity_step = chebyshev_split(forcing, operate, jacobi)
    column = lax.psum(jnp.sum(velocity_step, axis=1), "vz") / LAYERS
    adjoint_rhs = obs_weight * act * jnp.broadcast_to(column[:, None], velocity_step.shape)
    adjoint = chebyshev_split(adjoint_rhs, operate, jacobi)
    on_top = jnp.where(layer_index == column_devices - 1, 1.0, 0.0).astype(jnp.float32)
    bed_part = on_bed * bed_coef * jnp.sum(base_velocity * adjoint[:, 0], axis=0)
    own_part = on_top * (reg_weight * lap) - bed_part
    hess_action = lax.psum(own_part, "vz")
    return (hess_action, velocity_step)


def solution(mesh):
    return jax.shard_map(
        local,
        mesh=mesh,
        in_specs=(
            P("vz", "mx", "my"),
            P("mx", "my"),
            P(None, "mx", "my"),
            P("mx", "my"),
            P("mx", "my"),
            P("mx", "my"),
        ),
        out_specs=(P("mx", "my"), P(None, "vz", "mx", "my")),
        check_vma=False,
    )
```

```python
import jax
import jax.numpy as jnp
from jax import lax
from jax.experimental import pallas as pl
from jax.experimental.pallas import tpu as pltpu
from jax.sharding import PartitionSpec as P

LAYERS = 16
STEPS = 16
SWEEPS = 2
HALO = 16

weight_z = 128.0
shift_mass = 0.05
theta_center = 1.05
delta_half = 0.95
obs_weight = 200.0
reg_weight = 0.5


def step_constants():
    sigma = theta_center / delta_half
    table = []
    for sweep in range(SWEEPS):
        rho = 1.0 / sigma
        if sweep > 0:
            table.append((None, 1.0 / theta_center))
        for inner in range(STEPS - 1):
            rho_new = 1.0 / (2.0 * sigma - rho)
            table.append((rho_new * rho, 2.0 * rho_new / delta_half))
            rho = rho_new
    return table


def harmonic(left, right):
    total = left + right
    safe = jnp.where(total > 0, total, 1.0)
    return jnp.where(total > 0, 2.0 * left * right / safe, 0.0)


def exchange_rows(ext, k, rows, axis):
    count = lax.axis_size("mx")
    forward = [(i, i + 1) for i in range(count - 1)]
    backward = [(i + 1, i) for i in range(count - 1)]
    own = lax.slice_in_dim(ext, k, k + rows, axis=axis)
    low = lax.ppermute(lax.slice_in_dim(own, rows - k, rows, axis=axis), "mx", forward)
    high = lax.ppermute(lax.slice_in_dim(own, 0, k, axis=axis), "mx", backward)
    return jnp.concatenate([low, own, high], axis=axis)


def gather_axis(block, axis, dim):
    count = lax.axis_size(axis)
    me = lax.axis_index(axis)
    seq = [block]
    for s in range(1, count):
        pairs = [(j, (j - s) % count) for j in range(count)]
        seq.append(lax.ppermute(block, axis, pairs))
    size = block.shape[dim]
    doubled = jnp.concatenate(seq + seq, axis=dim)
    return lax.dynamic_slice_in_dim(doubled, ((count - me) % count) * size, count * size, axis=dim)


def shift(a, axis, offset):
    n = a.shape[axis]
    zeros_shape = list(a.shape)
    zeros_shape[axis] = 1
    z = jnp.zeros(zeros_shape, a.dtype)
    if offset > 0:
        return jnp.concatenate([lax.slice_in_dim(a, 1, n, axis=axis), z], axis=axis)
    return jnp.concatenate([z, lax.slice_in_dim(a, 0, n - 1, axis=axis)], axis=axis)


def segment_kernel(steps, op_ref, rhs_ref, x_in, d_in, x_ref, d_ref):
    comps, layers = rhs_ref.shape[0], rhs_ref.shape[1]
    rows, cols = rhs_ref.shape[2], rhs_ref.shape[3]
    x_ref[...] = x_in[...]
    d_ref[...] = d_in[...]

    for keep, push in steps:
        for c in range(comps):
            x_ref[c, 1] = x_ref[c, 1] + d_ref[c, 1]

        def update(layer, carry):
            p = layer + 1
            for c in range(comps):
                x_ref[c, p + 1] = x_ref[c, p + 1] + d_ref[c, p + 1]
                centre = x_ref[c, p]
                beside = op_ref[0, layer] * x_ref[c, p - 1] + op_ref[1, layer] * x_ref[c, p + 1]
                beside = beside + op_ref[2, layer] * pltpu.roll(centre, 1, 0)
                beside = beside + op_ref[3, layer] * pltpu.roll(centre, rows - 1, 0)
                beside = beside + op_ref[4, layer] * pltpu.roll(centre, 1, 1)
                beside = beside + op_ref[5, layer] * pltpu.roll(centre, cols - 1, 1)
                resid = rhs_ref[c, layer] - (op_ref[6, layer] * centre - beside)
                if keep is None:
                    d_ref[c, p] = op_ref[7, layer] * resid / theta_center
                else:
                    d_ref[c, p] = keep * d_ref[c, p] + push * (op_ref[7, layer] * resid)
            return carry

        lax.fori_loop(0, layers, update, 0)


def run_segment(steps, op_stack, rhs, iterate, step_dir):
    comps, layers, rows, cols = rhs.shape
    vmem = pl.BlockSpec(memory_space=pltpu.VMEM)
    cells = comps * layers * rows * cols
    return pl.pallas_call(
        lambda *refs: segment_kernel(steps, *refs),
        out_shape=(
            jax.ShapeDtypeStruct(iterate.shape, jnp.float32),
            jax.ShapeDtypeStruct(iterate.shape, jnp.float32),
        ),
        in_specs=[vmem] * 4,
        out_specs=(vmem, vmem),
        cost_estimate=pl.CostEstimate(
            flops=20 * cells * len(steps), bytes_accessed=4 * cells * 9, transcendentals=0
        ),
    )(op_stack, rhs, iterate, step_dir)


def local(viscosity, friction, base_velocity, grounded, ice_free, direction):
    layers_own, rows, cols_own = viscosity.shape
    if cols_own * lax.axis_size("my") > 256:
        return local_split(viscosity, friction, base_velocity, grounded, ice_free, direction)
    k = min(HALO, rows)
    act = (1 - ice_free).astype(jnp.float32)
    bed_coef = grounded.astype(jnp.float32) * friction
    planes = jnp.stack([act, bed_coef, base_velocity[0], base_velocity[1], direction])
    both = gather_axis(jnp.concatenate([viscosity, planes], axis=0), "my", 2)
    planes = both[layers_own:]
    eta = gather_axis(both[:layers_own], "vz", 0)
    layers = eta.shape[0]
    joined = jnp.concatenate([eta, planes], axis=0)
    zeros_halo = jnp.zeros(joined.shape[:1] + (k,) + joined.shape[2:], joined.dtype)
    joined = exchange_rows(jnp.concatenate([zeros_halo, joined, zeros_halo], axis=1), k, rows, 1)
    eta = joined[:layers]
    act, bed_coef, bv0, bv1, dir_ext = (joined[layers + i] for i in range(5))
    bv = jnp.stack([bv0, bv1])

    c_zm = weight_z * harmonic(eta, shift(eta, 0, -1))
    c_zp = weight_z * harmonic(eta, shift(eta, 0, 1))
    c_xm = harmonic(eta, shift(eta, 1, -1))
    c_xp = harmonic(eta, shift(eta, 1, 1))
    c_ym = harmonic(eta, shift(eta, 2, -1))
    c_yp = harmonic(eta, shift(eta, 2, 1))
    basal = jnp.zeros_like(eta).at[0].set(bed_coef)
    diag = c_zm + c_zp + c_xm + c_xp + c_ym + c_yp + shift_mass * eta + basal
    jacobi = 1.0 / (act * diag + 1.0 - act)

    on = act > 0
    op_stack = jnp.stack(
        [
            act * c_zm,
            act * c_zp,
            act * c_xm * shift(act, 0, -1),
            act * c_xp * shift(act, 0, 1),
            act * c_ym * shift(act, 1, -1),
            act * c_yp * shift(act, 1, 1),
            jnp.where(on, diag, 1.0),
            jacobi,
        ]
    )
    table = step_constants()
    layer_pad = ((0, 0), (1, 1), (0, 0), (0, 0))

    def chebyshev(rhs):
        iterate = jnp.zeros((2, layers + 2) + rhs.shape[2:], jnp.float32)
        step_dir = jnp.pad(jacobi * rhs / theta_center, layer_pad)
        since = 1
        run = []
        for keep, push in table:
            if since == k:
                iterate, step_dir = run_segment(tuple(run), op_stack, rhs, iterate, step_dir)
                run = []
                both = exchange_rows(jnp.stack([iterate, step_dir]), k, rows, 3)
                iterate, step_dir = both[0], both[1]
                since = 0
            run.append((keep, push))
            since += 1
        iterate, step_dir = run_segment(tuple(run), op_stack, rhs, iterate, step_dir)
        return (iterate + step_dir)[:, 1 : layers + 1]

    forcing = jnp.zeros((2,) + eta.shape, jnp.float32)
    forcing = forcing.at[:, 0].set(-(bed_coef * dir_ext)[None] * bv)
    forcing = forcing * act
    velocity_ext = chebyshev(forcing)
    column = jnp.sum(velocity_ext, axis=1) / layers
    column = exchange_rows(column, k, rows, 1)
    adjoint_rhs = obs_weight * act * jnp.broadcast_to(column[:, None], velocity_ext.shape)
    adjoint = chebyshev(adjoint_rhs)

    bed_term = bed_coef * jnp.sum(bv * adjoint[:, 0], axis=0)
    lap = (
        4.0 * dir_ext
        - shift(dir_ext, 0, -1)
        - shift(dir_ext, 0, 1)
        - shift(dir_ext, 1, -1)
        - shift(dir_ext, 1, 1)
    )
    hess_ext = -bed_term + reg_weight * lap
    col0 = lax.axis_index("my") * cols_own
    layer0 = lax.axis_index("vz") * layers_own
    hess_action = lax.dynamic_slice(hess_ext, (k, col0), (rows, cols_own))
    velocity_step = lax.dynamic_slice(
        velocity_ext, (0, layer0, k, col0), (2, layers_own, rows, cols_own)
    )
    return (hess_action, velocity_step)


def plain_harmonic(left, right):
    return 2.0 * left * right / (left + right)


def padded(block, sides, width):
    for axis, dim in sides:
        count = lax.axis_size(axis)
        forward = [(i, i + 1) for i in range(count - 1)]
        backward = [(target, source) for source, target in forward]
        low = lax.ppermute(
            lax.slice_in_dim(block, block.shape[dim] - width, None, axis=dim), axis, forward
        )
        high = lax.ppermute(lax.slice_in_dim(block, 0, width, axis=dim), axis, backward)
        block = jnp.concatenate([low, block, high], axis=dim)
    return block


def coefficients(padded_eta):
    core = padded_eta[1:-1, 1:-1, 1:-1]
    coefs = (
        weight_z * plain_harmonic(core, padded_eta[:-2, 1:-1, 1:-1]),
        weight_z * plain_harmonic(core, padded_eta[2:, 1:-1, 1:-1]),
        plain_harmonic(core, padded_eta[1:-1, :-2, 1:-1]),
        plain_harmonic(core, padded_eta[1:-1, 2:, 1:-1]),
        plain_harmonic(core, padded_eta[1:-1, 1:-1, :-2]),
        plain_harmonic(core, padded_eta[1:-1, 1:-1, 2:]),
    )
    return (core, coefs)


def stencil(pad, coefs, diag, masked, act, field):
    beside_all = coefs[0] * pad[:, :-2, 1:-1, 1:-1] + coefs[1] * pad[:, 2:, 1:-1, 1:-1]
    beside_all = beside_all + coefs[2] * pad[:, 1:-1, :-2, 1:-1] + coefs[3] * pad[:, 1:-1, 2:, 1:-1]
    beside_all = beside_all + coefs[4] * pad[:, 1:-1, 1:-1, :-2] + coefs[5] * pad[:, 1:-1, 1:-1, 2:]
    return act * (diag * masked - beside_all) + (1.0 - act) * field


def operate_split(field, coefs, diag, act):
    masked = field * act
    pad = padded(masked, (("mx", 2), ("my", 3), ("vz", 1)), 1)
    return stencil(pad, coefs, diag, masked, act, field)


def chebyshev_split(rhs, operate, jacobi):
    sigma = theta_center / delta_half
    rho = 1.0 / sigma
    keep_list = []
    push_list = []
    for inner in range(STEPS - 1):
        rho_new = 1.0 / (2.0 * sigma - rho)
        keep_list.append(rho_new * rho)
        push_list.append(2.0 * rho_new / delta_half)
        rho = rho_new
    keep_table = jnp.array(keep_list, jnp.float32)
    push_table = jnp.array(push_list, jnp.float32)

    def inner_step(position, state_pair):
        iterate, step_dir = state_pair
        iterate = iterate + step_dir
        resid = rhs - operate(iterate)
        step_dir = keep_table[position] * step_dir + push_table[position] * (jacobi * resid)
        return (iterate, step_dir)

    iterate = jnp.zeros_like(rhs)
    for sweep in range(SWEEPS):
        resid = rhs if sweep == 0 else rhs - operate(iterate)
        step_dir = jacobi * resid / theta_center
        iterate, step_dir = lax.fori_loop(0, STEPS - 1, inner_step, (iterate, step_dir))
        iterate = iterate + step_dir
    return iterate


def local_split(viscosity, friction, base_velocity, grounded, ice_free, direction):
    act = (1 - ice_free).astype(jnp.float32)
    ground = grounded.astype(jnp.float32)
    layer_index = lax.axis_index("vz")
    column_devices = lax.axis_size("vz")
    bed_coef = ground * friction
    padded_eta = padded(viscosity, (("mx", 1), ("my", 2), ("vz", 0)), 1)
    on_bed = jnp.where(layer_index == 0, 1.0, 0.0).astype(jnp.float32)
    core, coefs = coefficients(padded_eta)
    basal = jnp.zeros_like(core).at[0].set(on_bed * bed_coef)
    diag = (
        coefs[0] + coefs[1] + coefs[2] + coefs[3] + coefs[4] + coefs[5] + shift_mass * core + basal
    )
    jacobi = 1.0 / (act * diag + 1.0 - act)
    forcing = jnp.zeros((2,) + core.shape, jnp.float32)
    forcing = forcing.at[:, 0].set(-(on_bed * bed_coef * direction)[None] * base_velocity)
    forcing = forcing * act
    pad_dir = padded(direction, (("mx", 0), ("my", 1)), 1)
    lap = (
        4.0 * direction
        - pad_dir[:-2, 1:-1]
        - pad_dir[2:, 1:-1]
        - pad_dir[1:-1, :-2]
        - pad_dir[1:-1, 2:]
    )

    def operate(field):
        return operate_split(field, coefs, diag, act)

    velocity_step = chebyshev_split(forcing, operate, jacobi)
    column = lax.psum(jnp.sum(velocity_step, axis=1), "vz") / LAYERS
    adjoint_rhs = obs_weight * act * jnp.broadcast_to(column[:, None], velocity_step.shape)
    adjoint = chebyshev_split(adjoint_rhs, operate, jacobi)
    on_top = jnp.where(layer_index == column_devices - 1, 1.0, 0.0).astype(jnp.float32)
    bed_part = on_bed * bed_coef * jnp.sum(base_velocity * adjoint[:, 0], axis=0)
    own_part = on_top * (reg_weight * lap) - bed_part
    hess_action = lax.psum(own_part, "vz")
    return (hess_action, velocity_step)


def solution(mesh):
    return jax.shard_map(
        local,
        mesh=mesh,
        in_specs=(
            P("vz", "mx", "my"),
            P("mx", "my"),
            P(None, "mx", "my"),
            P("mx", "my"),
            P("mx", "my"),
            P("mx", "my"),
        ),
        out_specs=(P("mx", "my"), P(None, "vz", "mx", "my")),
        check_vma=False,
    )
```

```python
import jax
import jax.numpy as jnp
from jax import lax
from jax.experimental import pallas as pl
from jax.experimental.pallas import tpu as pltpu
from jax.sharding import PartitionSpec as P

LAYERS = 16
STEPS = 16
SWEEPS = 2
HALO = 16

weight_z = 128.0
shift_mass = 0.05
theta_center = 1.05
delta_half = 0.95
obs_weight = 200.0
reg_weight = 0.5


def step_constants():
    sigma = theta_center / delta_half
    table = []
    for sweep in range(SWEEPS):
        rho = 1.0 / sigma
        if sweep > 0:
            table.append((None, 1.0 / theta_center))
        for inner in range(STEPS - 1):
            rho_new = 1.0 / (2.0 * sigma - rho)
            table.append((rho_new * rho, 2.0 * rho_new / delta_half))
            rho = rho_new
    return table


def harmonic(left, right):
    total = left + right
    safe = jnp.where(total > 0, total, 1.0)
    return jnp.where(total > 0, 2.0 * left * right / safe, 0.0)


def exchange_rows(ext, k, rows, axis):
    count = lax.axis_size("mx")
    forward = [(i, i + 1) for i in range(count - 1)]
    backward = [(i + 1, i) for i in range(count - 1)]
    own = lax.slice_in_dim(ext, k, k + rows, axis=axis)
    low = lax.ppermute(lax.slice_in_dim(own, rows - k, rows, axis=axis), "mx", forward)
    high = lax.ppermute(lax.slice_in_dim(own, 0, k, axis=axis), "mx", backward)
    return jnp.concatenate([low, own, high], axis=axis)


def gather_axis(block, axis, dim):
    count = lax.axis_size(axis)
    me = lax.axis_index(axis)
    seq = [block]
    for s in range(1, count):
        pairs = [(j, (j - s) % count) for j in range(count)]
        seq.append(lax.ppermute(block, axis, pairs))
    size = block.shape[dim]
    doubled = jnp.concatenate(seq + seq, axis=dim)
    return lax.dynamic_slice_in_dim(doubled, ((count - me) % count) * size, count * size, axis=dim)


def shift(a, axis, offset):
    n = a.shape[axis]
    zeros_shape = list(a.shape)
    zeros_shape[axis] = 1
    z = jnp.zeros(zeros_shape, a.dtype)
    if offset > 0:
        return jnp.concatenate([lax.slice_in_dim(a, 1, n, axis=axis), z], axis=axis)
    return jnp.concatenate([z, lax.slice_in_dim(a, 0, n - 1, axis=axis)], axis=axis)


def segment_kernel(steps, op_ref, rhs_ref, x_in, d_in, x_ref, d_ref):
    comps, layers = rhs_ref.shape[0], rhs_ref.shape[1]
    rows, cols = rhs_ref.shape[2], rhs_ref.shape[3]
    x_ref[...] = x_in[...]
    d_ref[...] = d_in[...]

    for keep, push in steps:
        for c in range(comps):
            x_ref[c, 1] = x_ref[c, 1] + d_ref[c, 1]

        def update(layer, carry):
            p = layer + 1
            for c in range(comps):
                x_ref[c, p + 1] = x_ref[c, p + 1] + d_ref[c, p + 1]
                centre = x_ref[c, p]
                beside = op_ref[0, layer] * x_ref[c, p - 1] + op_ref[1, layer] * x_ref[c, p + 1]
                beside = beside + op_ref[2, layer] * pltpu.roll(centre, 1, 0)
                beside = beside + op_ref[3, layer] * pltpu.roll(centre, rows - 1, 0)
                beside = beside + op_ref[4, layer] * pltpu.roll(centre, 1, 1)
                beside = beside + op_ref[5, layer] * pltpu.roll(centre, cols - 1, 1)
                resid = rhs_ref[c, layer] - (op_ref[6, layer] * centre - beside)
                if keep is None:
                    d_ref[c, p] = op_ref[7, layer] * resid / theta_center
                else:
                    d_ref[c, p] = keep * d_ref[c, p] + push * (op_ref[7, layer] * resid)
            return carry

        lax.fori_loop(0, layers, update, 0)


def run_segment(steps, op_stack, rhs, iterate, step_dir):
    comps, layers, rows, cols = rhs.shape
    vmem = pl.BlockSpec(memory_space=pltpu.VMEM)
    cells = comps * layers * rows * cols
    return pl.pallas_call(
        lambda *refs: segment_kernel(steps, *refs),
        out_shape=(
            jax.ShapeDtypeStruct(iterate.shape, jnp.float32),
            jax.ShapeDtypeStruct(iterate.shape, jnp.float32),
        ),
        in_specs=[vmem] * 4,
        out_specs=(vmem, vmem),
        cost_estimate=pl.CostEstimate(
            flops=20 * cells * len(steps), bytes_accessed=4 * cells * 9, transcendentals=0
        ),
    )(op_stack, rhs, iterate, step_dir)


def local(viscosity, friction, base_velocity, grounded, ice_free, direction):
    layers_own, rows, cols_own = viscosity.shape
    if cols_own * lax.axis_size("my") > 256:
        return local_split(viscosity, friction, base_velocity, grounded, ice_free, direction)
    k = min(HALO, rows)
    act = (1 - ice_free).astype(jnp.float32)
    bed_coef = grounded.astype(jnp.float32) * friction
    planes = jnp.stack([act, bed_coef, base_velocity[0], base_velocity[1], direction])
    both = gather_axis(jnp.concatenate([viscosity, planes], axis=0), "my", 2)
    planes = both[layers_own:]
    eta = gather_axis(both[:layers_own], "vz", 0)
    layers = eta.shape[0]
    joined = jnp.concatenate([eta, planes], axis=0)
    zeros_halo = jnp.zeros(joined.shape[:1] + (k,) + joined.shape[2:], joined.dtype)
    joined = exchange_rows(jnp.concatenate([zeros_halo, joined, zeros_halo], axis=1), k, rows, 1)
    eta = joined[:layers]
    act, bed_coef, bv0, bv1, dir_ext = (joined[layers + i] for i in range(5))
    bv = jnp.stack([bv0, bv1])

    c_zm = weight_z * harmonic(eta, shift(eta, 0, -1))
    c_zp = weight_z * harmonic(eta, shift(eta, 0, 1))
    c_xm = harmonic(eta, shift(eta, 1, -1))
    c_xp = harmonic(eta, shift(eta, 1, 1))
    c_ym = harmonic(eta, shift(eta, 2, -1))
    c_yp = harmonic(eta, shift(eta, 2, 1))
    basal = jnp.zeros_like(eta).at[0].set(bed_coef)
    diag = c_zm + c_zp + c_xm + c_xp + c_ym + c_yp + shift_mass * eta + basal
    jacobi = 1.0 / (act * diag + 1.0 - act)

    on = act > 0
    op_stack = jnp.stack(
        [
            act * c_zm,
            act * c_zp,
            act * c_xm * shift(act, 0, -1),
            act * c_xp * shift(act, 0, 1),
            act * c_ym * shift(act, 1, -1),
            act * c_yp * shift(act, 1, 1),
            jnp.where(on, diag, 1.0),
            jacobi,
        ]
    )
    table = step_constants()
    layer_pad = ((0, 0), (1, 1), (0, 0), (0, 0))

    def exchange_state(iterate, step_dir):
        inner = jnp.stack([iterate, step_dir])[:, :, 1 : layers + 1]
        both = jnp.pad(exchange_rows(inner, k, rows, 3), ((0, 0),) + layer_pad)
        return both[0], both[1]

    def chebyshev(rhs_list):
        states = [
            (
                jnp.zeros((1, layers + 2) + rhs.shape[2:], jnp.float32),
                jnp.pad(jacobi * rhs / theta_center, layer_pad),
            )
            for rhs in rhs_list
        ]
        since = 1
        run = []
        for keep, push in table:
            if since == k:
                states = [
                    exchange_state(*run_segment(tuple(run), op_stack, rhs, *state))
                    for rhs, state in zip(rhs_list, states)
                ]
                run = []
                since = 0
            run.append((keep, push))
            since += 1
        finals = []
        for rhs, state in zip(rhs_list, states):
            iterate, step_dir = run_segment(tuple(run), op_stack, rhs, *state)
            finals.append((iterate + step_dir)[:, 1 : layers + 1])
        return finals

    forcing = jnp.zeros((2,) + eta.shape, jnp.float32)
    forcing = forcing.at[:, 0].set(-(bed_coef * dir_ext)[None] * bv)
    forcing = forcing * act
    velocity_parts = chebyshev([forcing[0:1], forcing[1:2]])
    adjoint_rhs = []
    for part in velocity_parts:
        column = jnp.sum(part, axis=1) / layers
        column = exchange_rows(column, k, rows, 1)
        adjoint_rhs.append(obs_weight * act * jnp.broadcast_to(column[:, None], part.shape))
    adjoint = jnp.concatenate(chebyshev(adjoint_rhs), axis=0)
    velocity_ext = jnp.concatenate(velocity_parts, axis=0)

    bed_term = bed_coef * jnp.sum(bv * adjoint[:, 0], axis=0)
    lap = (
        4.0 * dir_ext
        - shift(dir_ext, 0, -1)
        - shift(dir_ext, 0, 1)
        - shift(dir_ext, 1, -1)
        - shift(dir_ext, 1, 1)
    )
    hess_ext = -bed_term + reg_weight * lap
    col0 = lax.axis_index("my") * cols_own
    layer0 = lax.axis_index("vz") * layers_own
    hess_action = lax.dynamic_slice(hess_ext, (k, col0), (rows, cols_own))
    velocity_step = lax.dynamic_slice(
        velocity_ext, (0, layer0, k, col0), (2, layers_own, rows, cols_own)
    )
    return (hess_action, velocity_step)


def plain_harmonic(left, right):
    return 2.0 * left * right / (left + right)


def padded(block, sides, width):
    for axis, dim in sides:
        count = lax.axis_size(axis)
        forward = [(i, i + 1) for i in range(count - 1)]
        backward = [(target, source) for source, target in forward]
        low = lax.ppermute(
            lax.slice_in_dim(block, block.shape[dim] - width, None, axis=dim), axis, forward
        )
        high = lax.ppermute(lax.slice_in_dim(block, 0, width, axis=dim), axis, backward)
        block = jnp.concatenate([low, block, high], axis=dim)
    return block


def coefficients(padded_eta):
    core = padded_eta[1:-1, 1:-1, 1:-1]
    coefs = (
        weight_z * plain_harmonic(core, padded_eta[:-2, 1:-1, 1:-1]),
        weight_z * plain_harmonic(core, padded_eta[2:, 1:-1, 1:-1]),
        plain_harmonic(core, padded_eta[1:-1, :-2, 1:-1]),
        plain_harmonic(core, padded_eta[1:-1, 2:, 1:-1]),
        plain_harmonic(core, padded_eta[1:-1, 1:-1, :-2]),
        plain_harmonic(core, padded_eta[1:-1, 1:-1, 2:]),
    )
    return (core, coefs)


def stencil(pad, coefs, diag, masked, act, field):
    beside_all = coefs[0] * pad[:, :-2, 1:-1, 1:-1] + coefs[1] * pad[:, 2:, 1:-1, 1:-1]
    beside_all = beside_all + coefs[2] * pad[:, 1:-1, :-2, 1:-1] + coefs[3] * pad[:, 1:-1, 2:, 1:-1]
    beside_all = beside_all + coefs[4] * pad[:, 1:-1, 1:-1, :-2] + coefs[5] * pad[:, 1:-1, 1:-1, 2:]
    return act * (diag * masked - beside_all) + (1.0 - act) * field


def operate_split(field, coefs, diag, act):
    masked = field * act
    pad = padded(masked, (("mx", 2), ("my", 3), ("vz", 1)), 1)
    return stencil(pad, coefs, diag, masked, act, field)


def chebyshev_split(rhs, operate, jacobi):
    sigma = theta_center / delta_half
    rho = 1.0 / sigma
    keep_list = []
    push_list = []
    for inner in range(STEPS - 1):
        rho_new = 1.0 / (2.0 * sigma - rho)
        keep_list.append(rho_new * rho)
        push_list.append(2.0 * rho_new / delta_half)
        rho = rho_new
    keep_table = jnp.array(keep_list, jnp.float32)
    push_table = jnp.array(push_list, jnp.float32)

    def inner_step(position, state_pair):
        iterate, step_dir = state_pair
        iterate = iterate + step_dir
        resid = rhs - operate(iterate)
        step_dir = keep_table[position] * step_dir + push_table[position] * (jacobi * resid)
        return (iterate, step_dir)

    iterate = jnp.zeros_like(rhs)
    for sweep in range(SWEEPS):
        resid = rhs if sweep == 0 else rhs - operate(iterate)
        step_dir = jacobi * resid / theta_center
        iterate, step_dir = lax.fori_loop(0, STEPS - 1, inner_step, (iterate, step_dir))
        iterate = iterate + step_dir
    return iterate


def local_split(viscosity, friction, base_velocity, grounded, ice_free, direction):
    act = (1 - ice_free).astype(jnp.float32)
    ground = grounded.astype(jnp.float32)
    layer_index = lax.axis_index("vz")
    column_devices = lax.axis_size("vz")
    bed_coef = ground * friction
    padded_eta = padded(viscosity, (("mx", 1), ("my", 2), ("vz", 0)), 1)
    on_bed = jnp.where(layer_index == 0, 1.0, 0.0).astype(jnp.float32)
    core, coefs = coefficients(padded_eta)
    basal = jnp.zeros_like(core).at[0].set(on_bed * bed_coef)
    diag = (
        coefs[0] + coefs[1] + coefs[2] + coefs[3] + coefs[4] + coefs[5] + shift_mass * core + basal
    )
    jacobi = 1.0 / (act * diag + 1.0 - act)
    forcing = jnp.zeros((2,) + core.shape, jnp.float32)
    forcing = forcing.at[:, 0].set(-(on_bed * bed_coef * direction)[None] * base_velocity)
    forcing = forcing * act
    pad_dir = padded(direction, (("mx", 0), ("my", 1)), 1)
    lap = (
        4.0 * direction
        - pad_dir[:-2, 1:-1]
        - pad_dir[2:, 1:-1]
        - pad_dir[1:-1, :-2]
        - pad_dir[1:-1, 2:]
    )

    def operate(field):
        return operate_split(field, coefs, diag, act)

    velocity_step = chebyshev_split(forcing, operate, jacobi)
    column = lax.psum(jnp.sum(velocity_step, axis=1), "vz") / LAYERS
    adjoint_rhs = obs_weight * act * jnp.broadcast_to(column[:, None], velocity_step.shape)
    adjoint = chebyshev_split(adjoint_rhs, operate, jacobi)
    on_top = jnp.where(layer_index == column_devices - 1, 1.0, 0.0).astype(jnp.float32)
    bed_part = on_bed * bed_coef * jnp.sum(base_velocity * adjoint[:, 0], axis=0)
    own_part = on_top * (reg_weight * lap) - bed_part
    hess_action = lax.psum(own_part, "vz")
    return (hess_action, velocity_step)


def solution(mesh):
    return jax.shard_map(
        local,
        mesh=mesh,
        in_specs=(
            P("vz", "mx", "my"),
            P("mx", "my"),
            P(None, "mx", "my"),
            P("mx", "my"),
            P("mx", "my"),
            P("mx", "my"),
        ),
        out_specs=(P("mx", "my"), P(None, "vz", "mx", "my")),
        check_vma=False,
    )
```

```python
import jax
import jax.numpy as jnp
from jax import lax
from jax.experimental import pallas as pl
from jax.experimental.pallas import tpu as pltpu
from jax.sharding import PartitionSpec as P

LAYERS = 16
STEPS = 16
SWEEPS = 2
HALO = 16

weight_z = 128.0
shift_mass = 0.05
theta_center = 1.05
delta_half = 0.95
obs_weight = 200.0
reg_weight = 0.5


def step_constants():
    sigma = theta_center / delta_half
    table = []
    for sweep in range(SWEEPS):
        rho = 1.0 / sigma
        if sweep > 0:
            table.append((None, 1.0 / theta_center))
        for inner in range(STEPS - 1):
            rho_new = 1.0 / (2.0 * sigma - rho)
            table.append((rho_new * rho, 2.0 * rho_new / delta_half))
            rho = rho_new
    return table


def harmonic(left, right):
    total = left + right
    safe = jnp.where(total > 0, total, 1.0)
    return jnp.where(total > 0, 2.0 * left * right / safe, 0.0)


def exchange_rows(ext, k, rows, axis):
    count = lax.axis_size("mx")
    forward = [(i, i + 1) for i in range(count - 1)]
    backward = [(i + 1, i) for i in range(count - 1)]
    own = lax.slice_in_dim(ext, k, k + rows, axis=axis)
    low = lax.ppermute(lax.slice_in_dim(own, rows - k, rows, axis=axis), "mx", forward)
    high = lax.ppermute(lax.slice_in_dim(own, 0, k, axis=axis), "mx", backward)
    return jnp.concatenate([low, own, high], axis=axis)


def gather_axis(block, axis, dim):
    count = lax.axis_size(axis)
    me = lax.axis_index(axis)
    seq = [block]
    for s in range(1, count):
        pairs = [(j, (j - s) % count) for j in range(count)]
        seq.append(lax.ppermute(block, axis, pairs))
    size = block.shape[dim]
    doubled = jnp.concatenate(seq + seq, axis=dim)
    return lax.dynamic_slice_in_dim(doubled, ((count - me) % count) * size, count * size, axis=dim)


def shift(a, axis, offset):
    n = a.shape[axis]
    zeros_shape = list(a.shape)
    zeros_shape[axis] = 1
    z = jnp.zeros(zeros_shape, a.dtype)
    if offset > 0:
        return jnp.concatenate([lax.slice_in_dim(a, 1, n, axis=axis), z], axis=axis)
    return jnp.concatenate([z, lax.slice_in_dim(a, 0, n - 1, axis=axis)], axis=axis)


def segment_kernel(steps, start_valid, op_ref, rhs_ref, x_in, d_in, x_ref, d_ref):
    comps, layers = rhs_ref.shape[0], rhs_ref.shape[1]
    rows, cols = rhs_ref.shape[2], rhs_ref.shape[3]
    x_ref[...] = x_in[...]
    d_ref[...] = d_in[...]

    for j, (keep, push) in enumerate(steps):
        lo = min(8 * ((start_valid + j) // 8), rows // 2 - 8)
        lo = max(lo, 0)
        span = pl.ds(lo, rows - 2 * lo)
        height = rows - 2 * lo
        for c in range(comps):
            x_ref[c, 1, span] = x_ref[c, 1, span] + d_ref[c, 1, span]

        def update(layer, carry):
            p = layer + 1
            c_xm = op_ref[2, layer, span]
            c_ym = op_ref[3, layer, span]
            c_xp = pltpu.roll(c_xm, height - 1, 0)
            c_yp = pltpu.roll(c_ym, cols - 1, 1)
            for c in range(comps):
                above = x_ref[c, p + 1, span] + d_ref[c, p + 1, span]
                x_ref[c, p + 1, span] = above
                centre = x_ref[c, p, span]
                beside = op_ref[0, layer, span] * x_ref[c, p - 1, span] + op_ref[1, layer, span] * above
                beside = beside + c_xm * pltpu.roll(centre, 1, 0)
                beside = beside + c_xp * pltpu.roll(centre, height - 1, 0)
                beside = beside + c_ym * pltpu.roll(centre, 1, 1)
                beside = beside + c_yp * pltpu.roll(centre, cols - 1, 1)
                resid = rhs_ref[c, layer, span] - (op_ref[4, layer, span] * centre - beside)
                if keep is None:
                    d_ref[c, p, span] = op_ref[5, layer, span] * resid / theta_center
                else:
                    d_ref[c, p, span] = keep * d_ref[c, p, span] + push * (op_ref[5, layer, span] * resid)
            return carry

        lax.fori_loop(0, layers, update, 0)


def run_segment(steps, start_valid, op_stack, rhs, iterate, step_dir):
    comps, layers, rows, cols = rhs.shape
    vmem = pl.BlockSpec(memory_space=pltpu.VMEM)
    cells = comps * layers * rows * cols
    return pl.pallas_call(
        lambda *refs: segment_kernel(steps, start_valid, *refs),
        out_shape=(
            jax.ShapeDtypeStruct(iterate.shape, jnp.float32),
            jax.ShapeDtypeStruct(iterate.shape, jnp.float32),
        ),
        in_specs=[vmem] * 4,
        out_specs=(vmem, vmem),
        cost_estimate=pl.CostEstimate(
            flops=20 * cells * len(steps), bytes_accessed=4 * cells * 9, transcendentals=0
        ),
    )(op_stack, rhs, iterate, step_dir)


def local(viscosity, friction, base_velocity, grounded, ice_free, direction):
    layers_own, rows, cols_own = viscosity.shape
    if cols_own * lax.axis_size("my") > 256:
        return local_split(viscosity, friction, base_velocity, grounded, ice_free, direction)
    k = min(HALO, rows)
    act = (1 - ice_free).astype(jnp.float32)
    bed_coef = grounded.astype(jnp.float32) * friction
    planes = jnp.stack([act, bed_coef, base_velocity[0], base_velocity[1], direction])
    both = gather_axis(jnp.concatenate([viscosity, planes], axis=0), "my", 2)
    planes = both[layers_own:]
    eta = gather_axis(both[:layers_own], "vz", 0)
    layers = eta.shape[0]
    joined = jnp.concatenate([eta, planes], axis=0)
    zeros_halo = jnp.zeros(joined.shape[:1] + (k,) + joined.shape[2:], joined.dtype)
    joined = exchange_rows(jnp.concatenate([zeros_halo, joined, zeros_halo], axis=1), k, rows, 1)
    eta = joined[:layers]
    act, bed_coef, bv0, bv1, dir_ext = (joined[layers + i] for i in range(5))
    bv = jnp.stack([bv0, bv1])

    c_zm = weight_z * harmonic(eta, shift(eta, 0, -1))
    c_zp = weight_z * harmonic(eta, shift(eta, 0, 1))
    c_xm = harmonic(eta, shift(eta, 1, -1))
    c_xp = harmonic(eta, shift(eta, 1, 1))
    c_ym = harmonic(eta, shift(eta, 2, -1))
    c_yp = harmonic(eta, shift(eta, 2, 1))
    basal = jnp.zeros_like(eta).at[0].set(bed_coef)
    diag = c_zm + c_zp + c_xm + c_xp + c_ym + c_yp + shift_mass * eta + basal
    jacobi = 1.0 / (act * diag + 1.0 - act)

    on = act > 0
    op_stack = jnp.stack(
        [
            act * c_zm,
            act * c_zp,
            act * c_xm * shift(act, 0, -1),
            act * c_ym * shift(act, 1, -1),
            jnp.where(on, diag, 1.0),
            jacobi,
        ]
    )
    table = step_constants()
    layer_pad = ((0, 0), (1, 1), (0, 0), (0, 0))

    def chebyshev(rhs):
        iterate = jnp.zeros((2, layers + 2) + rhs.shape[2:], jnp.float32)
        step_dir = jnp.pad(jacobi * rhs / theta_center, layer_pad)
        since = 1
        start_valid = 1
        run = []
        for keep, push in table:
            if since == k:
                iterate, step_dir = run_segment(tuple(run), start_valid, op_stack, rhs, iterate, step_dir)
                run = []
                start_valid = 0
                both = exchange_rows(jnp.stack([iterate, step_dir]), k, rows, 3)
                iterate, step_dir = both[0], both[1]
                since = 0
            run.append((keep, push))
            since += 1
        iterate, step_dir = run_segment(tuple(run), start_valid, op_stack, rhs, iterate, step_dir)
        return (iterate + step_dir)[:, 1 : layers + 1]

    forcing = jnp.zeros((2,) + eta.shape, jnp.float32)
    forcing = forcing.at[:, 0].set(-(bed_coef * dir_ext)[None] * bv)
    forcing = forcing * act
    velocity_ext = chebyshev(forcing)
    column = jnp.sum(velocity_ext, axis=1) / layers
    column = exchange_rows(column, k, rows, 1)
    adjoint_rhs = obs_weight * act * jnp.broadcast_to(column[:, None], velocity_ext.shape)
    adjoint = chebyshev(adjoint_rhs)

    bed_term = bed_coef * jnp.sum(bv * adjoint[:, 0], axis=0)
    lap = (
        4.0 * dir_ext
        - shift(dir_ext, 0, -1)
        - shift(dir_ext, 0, 1)
        - shift(dir_ext, 1, -1)
        - shift(dir_ext, 1, 1)
    )
    hess_ext = -bed_term + reg_weight * lap
    col0 = lax.axis_index("my") * cols_own
    layer0 = lax.axis_index("vz") * layers_own
    hess_action = lax.dynamic_slice(hess_ext, (k, col0), (rows, cols_own))
    velocity_step = lax.dynamic_slice(
        velocity_ext, (0, layer0, k, col0), (2, layers_own, rows, cols_own)
    )
    return (hess_action, velocity_step)


def plain_harmonic(left, right):
    return 2.0 * left * right / (left + right)


def padded(block, sides, width):
    for axis, dim in sides:
        count = lax.axis_size(axis)
        forward = [(i, i + 1) for i in range(count - 1)]
        backward = [(target, source) for source, target in forward]
        low = lax.ppermute(
            lax.slice_in_dim(block, block.shape[dim] - width, None, axis=dim), axis, forward
        )
        high = lax.ppermute(lax.slice_in_dim(block, 0, width, axis=dim), axis, backward)
        block = jnp.concatenate([low, block, high], axis=dim)
    return block


def coefficients(padded_eta):
    core = padded_eta[1:-1, 1:-1, 1:-1]
    coefs = (
        weight_z * plain_harmonic(core, padded_eta[:-2, 1:-1, 1:-1]),
        weight_z * plain_harmonic(core, padded_eta[2:, 1:-1, 1:-1]),
        plain_harmonic(core, padded_eta[1:-1, :-2, 1:-1]),
        plain_harmonic(core, padded_eta[1:-1, 2:, 1:-1]),
        plain_harmonic(core, padded_eta[1:-1, 1:-1, :-2]),
        plain_harmonic(core, padded_eta[1:-1, 1:-1, 2:]),
    )
    return (core, coefs)


def stencil(pad, coefs, diag, masked, act, field):
    beside_all = coefs[0] * pad[:, :-2, 1:-1, 1:-1] + coefs[1] * pad[:, 2:, 1:-1, 1:-1]
    beside_all = beside_all + coefs[2] * pad[:, 1:-1, :-2, 1:-1] + coefs[3] * pad[:, 1:-1, 2:, 1:-1]
    beside_all = beside_all + coefs[4] * pad[:, 1:-1, 1:-1, :-2] + coefs[5] * pad[:, 1:-1, 1:-1, 2:]
    return act * (diag * masked - beside_all) + (1.0 - act) * field


def operate_split(field, coefs, diag, act):
    masked = field * act
    pad = padded(masked, (("mx", 2), ("my", 3), ("vz", 1)), 1)
    return stencil(pad, coefs, diag, masked, act, field)


def chebyshev_split(rhs, operate, jacobi):
    sigma = theta_center / delta_half
    rho = 1.0 / sigma
    keep_list = []
    push_list = []
    for inner in range(STEPS - 1):
        rho_new = 1.0 / (2.0 * sigma - rho)
        keep_list.append(rho_new * rho)
        push_list.append(2.0 * rho_new / delta_half)
        rho = rho_new
    keep_table = jnp.array(keep_list, jnp.float32)
    push_table = jnp.array(push_list, jnp.float32)

    def inner_step(position, state_pair):
        iterate, step_dir = state_pair
        iterate = iterate + step_dir
        resid = rhs - operate(iterate)
        step_dir = keep_table[position] * step_dir + push_table[position] * (jacobi * resid)
        return (iterate, step_dir)

    iterate = jnp.zeros_like(rhs)
    for sweep in range(SWEEPS):
        resid = rhs if sweep == 0 else rhs - operate(iterate)
        step_dir = jacobi * resid / theta_center
        iterate, step_dir = lax.fori_loop(0, STEPS - 1, inner_step, (iterate, step_dir))
        iterate = iterate + step_dir
    return iterate


def local_split(viscosity, friction, base_velocity, grounded, ice_free, direction):
    act = (1 - ice_free).astype(jnp.float32)
    ground = grounded.astype(jnp.float32)
    layer_index = lax.axis_index("vz")
    column_devices = lax.axis_size("vz")
    bed_coef = ground * friction
    padded_eta = padded(viscosity, (("mx", 1), ("my", 2), ("vz", 0)), 1)
    on_bed = jnp.where(layer_index == 0, 1.0, 0.0).astype(jnp.float32)
    core, coefs = coefficients(padded_eta)
    basal = jnp.zeros_like(core).at[0].set(on_bed * bed_coef)
    diag = (
        coefs[0] + coefs[1] + coefs[2] + coefs[3] + coefs[4] + coefs[5] + shift_mass * core + basal
    )
    jacobi = 1.0 / (act * diag + 1.0 - act)
    forcing = jnp.zeros((2,) + core.shape, jnp.float32)
    forcing = forcing.at[:, 0].set(-(on_bed * bed_coef * direction)[None] * base_velocity)
    forcing = forcing * act
    pad_dir = padded(direction, (("mx", 0), ("my", 1)), 1)
    lap = (
        4.0 * direction
        - pad_dir[:-2, 1:-1]
        - pad_dir[2:, 1:-1]
        - pad_dir[1:-1, :-2]
        - pad_dir[1:-1, 2:]
    )

    def operate(field):
        return operate_split(field, coefs, diag, act)

    velocity_step = chebyshev_split(forcing, operate, jacobi)
    column = lax.psum(jnp.sum(velocity_step, axis=1), "vz") / LAYERS
    adjoint_rhs = obs_weight * act * jnp.broadcast_to(column[:, None], velocity_step.shape)
    adjoint = chebyshev_split(adjoint_rhs, operate, jacobi)
    on_top = jnp.where(layer_index == column_devices - 1, 1.0, 0.0).astype(jnp.float32)
    bed_part = on_bed * bed_coef * jnp.sum(base_velocity * adjoint[:, 0], axis=0)
    own_part = on_top * (reg_weight * lap) - bed_part
    hess_action = lax.psum(own_part, "vz")
    return (hess_action, velocity_step)


def solution(mesh):
    return jax.shard_map(
        local,
        mesh=mesh,
        in_specs=(
            P("vz", "mx", "my"),
            P("mx", "my"),
            P(None, "mx", "my"),
            P("mx", "my"),
            P("mx", "my"),
            P("mx", "my"),
        ),
        out_specs=(P("mx", "my"), P(None, "vz", "mx", "my")),
        check_vma=False,
    )
```

```python
import jax
import jax.numpy as jnp
from jax import lax
from jax.experimental import pallas as pl
from jax.experimental.pallas import tpu as pltpu
from jax.sharding import PartitionSpec as P

LAYERS = 16
STEPS = 16
SWEEPS = 2
HALO = 16

weight_z = 128.0
shift_mass = 0.05
theta_center = 1.05
delta_half = 0.95
obs_weight = 200.0
reg_weight = 0.5


def step_constants():
    sigma = theta_center / delta_half
    table = []
    for sweep in range(SWEEPS):
        rho = 1.0 / sigma
        if sweep > 0:
            table.append((None, 1.0 / theta_center))
        for inner in range(STEPS - 1):
            rho_new = 1.0 / (2.0 * sigma - rho)
            table.append((rho_new * rho, 2.0 * rho_new / delta_half))
            rho = rho_new
    return table


def harmonic(left, right):
    total = left + right
    safe = jnp.where(total > 0, total, 1.0)
    return jnp.where(total > 0, 2.0 * left * right / safe, 0.0)


def exchange_rows(ext, k, rows, axis):
    count = lax.axis_size("mx")
    forward = [(i, i + 1) for i in range(count - 1)]
    backward = [(i + 1, i) for i in range(count - 1)]
    own = lax.slice_in_dim(ext, k, k + rows, axis=axis)
    low = lax.ppermute(lax.slice_in_dim(own, rows - k, rows, axis=axis), "mx", forward)
    high = lax.ppermute(lax.slice_in_dim(own, 0, k, axis=axis), "mx", backward)
    return jnp.concatenate([low, own, high], axis=axis)


def gather_axis(block, axis, dim):
    count = lax.axis_size(axis)
    me = lax.axis_index(axis)
    seq = [block]
    for s in range(1, count):
        pairs = [(j, (j - s) % count) for j in range(count)]
        seq.append(lax.ppermute(block, axis, pairs))
    size = block.shape[dim]
    doubled = jnp.concatenate(seq + seq, axis=dim)
    return lax.dynamic_slice_in_dim(doubled, ((count - me) % count) * size, count * size, axis=dim)


def shift(a, axis, offset):
    n = a.shape[axis]
    zeros_shape = list(a.shape)
    zeros_shape[axis] = 1
    z = jnp.zeros(zeros_shape, a.dtype)
    if offset > 0:
        return jnp.concatenate([lax.slice_in_dim(a, 1, n, axis=axis), z], axis=axis)
    return jnp.concatenate([z, lax.slice_in_dim(a, 0, n - 1, axis=axis)], axis=axis)


def segment_kernel(steps, start_valid, op_ref, rhs_ref, x_in, d_in, x_ref, d_ref):
    comps, layers = rhs_ref.shape[0], rhs_ref.shape[1]
    rows, cols = rhs_ref.shape[2], rhs_ref.shape[3]
    x_ref[...] = x_in[...]
    d_ref[...] = d_in[...]

    for j, (keep, push) in enumerate(steps):
        lo = min(8 * ((start_valid + j) // 8), rows // 2 - 8)
        lo = max(lo, 0)
        span = pl.ds(lo, rows - 2 * lo)
        height = rows - 2 * lo
        for c in range(comps):
            x_ref[c, 1, span] = x_ref[c, 1, span] + d_ref[c, 1, span]

        def update(layer, carry):
            p = layer + 1
            c_xm = op_ref[2, layer, span]
            c_ym = op_ref[3, layer, span]
            c_xp = pltpu.roll(c_xm, height - 1, 0)
            c_yp = pltpu.roll(c_ym, cols - 1, 1)
            for c in range(comps):
                above = x_ref[c, p + 1, span] + d_ref[c, p + 1, span]
                x_ref[c, p + 1, span] = above
                centre = x_ref[c, p, span]
                beside = op_ref[0, layer, span] * x_ref[c, p - 1, span] + op_ref[1, layer, span] * above
                beside = beside + c_xm * pltpu.roll(centre, 1, 0)
                beside = beside + c_xp * pltpu.roll(centre, height - 1, 0)
                beside = beside + c_ym * pltpu.roll(centre, 1, 1)
                beside = beside + c_yp * pltpu.roll(centre, cols - 1, 1)
                resid = rhs_ref[c, layer, span] - (op_ref[4, layer, span] * centre - beside)
                if keep is None:
                    d_ref[c, p, span] = op_ref[5, layer, span] * resid / theta_center
                else:
                    d_ref[c, p, span] = keep * d_ref[c, p, span] + push * (op_ref[5, layer, span] * resid)
            return carry

        lax.fori_loop(0, layers, update, 0, unroll=4)


def run_segment(steps, start_valid, op_stack, rhs, iterate, step_dir):
    comps, layers, rows, cols = rhs.shape
    vmem = pl.BlockSpec(memory_space=pltpu.VMEM)
    cells = comps * layers * rows * cols
    return pl.pallas_call(
        lambda *refs: segment_kernel(steps, start_valid, *refs),
        out_shape=(
            jax.ShapeDtypeStruct(iterate.shape, jnp.float32),
            jax.ShapeDtypeStruct(iterate.shape, jnp.float32),
        ),
        in_specs=[vmem] * 4,
        out_specs=(vmem, vmem),
        cost_estimate=pl.CostEstimate(
            flops=20 * cells * len(steps), bytes_accessed=4 * cells * 9, transcendentals=0
        ),
    )(op_stack, rhs, iterate, step_dir)


def local(viscosity, friction, base_velocity, grounded, ice_free, direction):
    layers_own, rows, cols_own = viscosity.shape
    if cols_own * lax.axis_size("my") > 256:
        return local_split(viscosity, friction, base_velocity, grounded, ice_free, direction)
    k = min(HALO, rows)
    act = (1 - ice_free).astype(jnp.float32)
    bed_coef = grounded.astype(jnp.float32) * friction
    planes = jnp.stack([act, bed_coef, base_velocity[0], base_velocity[1], direction])
    both = gather_axis(jnp.concatenate([viscosity, planes], axis=0), "my", 2)
    planes = both[layers_own:]
    eta = gather_axis(both[:layers_own], "vz", 0)
    layers = eta.shape[0]
    joined = jnp.concatenate([eta, planes], axis=0)
    zeros_halo = jnp.zeros(joined.shape[:1] + (k,) + joined.shape[2:], joined.dtype)
    joined = exchange_rows(jnp.concatenate([zeros_halo, joined, zeros_halo], axis=1), k, rows, 1)
    eta = joined[:layers]
    act, bed_coef, bv0, bv1, dir_ext = (joined[layers + i] for i in range(5))
    bv = jnp.stack([bv0, bv1])

    c_zm = weight_z * harmonic(eta, shift(eta, 0, -1))
    c_zp = weight_z * harmonic(eta, shift(eta, 0, 1))
    c_xm = harmonic(eta, shift(eta, 1, -1))
    c_xp = harmonic(eta, shift(eta, 1, 1))
    c_ym = harmonic(eta, shift(eta, 2, -1))
    c_yp = harmonic(eta, shift(eta, 2, 1))
    basal = jnp.zeros_like(eta).at[0].set(bed_coef)
    diag = c_zm + c_zp + c_xm + c_xp + c_ym + c_yp + shift_mass * eta + basal
    jacobi = 1.0 / (act * diag + 1.0 - act)

    on = act > 0
    op_stack = jnp.stack(
        [
            act * c_zm,
            act * c_zp,
            act * c_xm * shift(act, 0, -1),
            act * c_ym * shift(act, 1, -1),
            jnp.where(on, diag, 1.0),
            jacobi,
        ]
    )
    table = step_constants()
    layer_pad = ((0, 0), (1, 1), (0, 0), (0, 0))

    def chebyshev(rhs):
        iterate = jnp.zeros((2, layers + 2) + rhs.shape[2:], jnp.float32)
        step_dir = jnp.pad(jacobi * rhs / theta_center, layer_pad)
        since = 1
        start_valid = 1
        run = []
        for keep, push in table:
            if since == k:
                iterate, step_dir = run_segment(tuple(run), start_valid, op_stack, rhs, iterate, step_dir)
                run = []
                start_valid = 0
                both = exchange_rows(jnp.stack([iterate, step_dir]), k, rows, 3)
                iterate, step_dir = both[0], both[1]
                since = 0
            run.append((keep, push))
            since += 1
        iterate, step_dir = run_segment(tuple(run), start_valid, op_stack, rhs, iterate, step_dir)
        return (iterate + step_dir)[:, 1 : layers + 1]

    forcing = jnp.zeros((2,) + eta.shape, jnp.float32)
    forcing = forcing.at[:, 0].set(-(bed_coef * dir_ext)[None] * bv)
    forcing = forcing * act
    velocity_ext = chebyshev(forcing)
    column = jnp.sum(velocity_ext, axis=1) / layers
    column = exchange_rows(column, k, rows, 1)
    adjoint_rhs = obs_weight * act * jnp.broadcast_to(column[:, None], velocity_ext.shape)
    adjoint = chebyshev(adjoint_rhs)

    bed_term = bed_coef * jnp.sum(bv * adjoint[:, 0], axis=0)
    lap = (
        4.0 * dir_ext
        - shift(dir_ext, 0, -1)
        - shift(dir_ext, 0, 1)
        - shift(dir_ext, 1, -1)
        - shift(dir_ext, 1, 1)
    )
    hess_ext = -bed_term + reg_weight * lap
    col0 = lax.axis_index("my") * cols_own
    layer0 = lax.axis_index("vz") * layers_own
    hess_action = lax.dynamic_slice(hess_ext, (k, col0), (rows, cols_own))
    velocity_step = lax.dynamic_slice(
        velocity_ext, (0, layer0, k, col0), (2, layers_own, rows, cols_own)
    )
    return (hess_action, velocity_step)


def plain_harmonic(left, right):
    return 2.0 * left * right / (left + right)


def padded(block, sides, width):
    for axis, dim in sides:
        count = lax.axis_size(axis)
        forward = [(i, i + 1) for i in range(count - 1)]
        backward = [(target, source) for source, target in forward]
        low = lax.ppermute(
            lax.slice_in_dim(block, block.shape[dim] - width, None, axis=dim), axis, forward
        )
        high = lax.ppermute(lax.slice_in_dim(block, 0, width, axis=dim), axis, backward)
        block = jnp.concatenate([low, block, high], axis=dim)
    return block


def coefficients(padded_eta):
    core = padded_eta[1:-1, 1:-1, 1:-1]
    coefs = (
        weight_z * plain_harmonic(core, padded_eta[:-2, 1:-1, 1:-1]),
        weight_z * plain_harmonic(core, padded_eta[2:, 1:-1, 1:-1]),
        plain_harmonic(core, padded_eta[1:-1, :-2, 1:-1]),
        plain_harmonic(core, padded_eta[1:-1, 2:, 1:-1]),
        plain_harmonic(core, padded_eta[1:-1, 1:-1, :-2]),
        plain_harmonic(core, padded_eta[1:-1, 1:-1, 2:]),
    )
    return (core, coefs)


def stencil(pad, coefs, diag, masked, act, field):
    beside_all = coefs[0] * pad[:, :-2, 1:-1, 1:-1] + coefs[1] * pad[:, 2:, 1:-1, 1:-1]
    beside_all = beside_all + coefs[2] * pad[:, 1:-1, :-2, 1:-1] + coefs[3] * pad[:, 1:-1, 2:, 1:-1]
    beside_all = beside_all + coefs[4] * pad[:, 1:-1, 1:-1, :-2] + coefs[5] * pad[:, 1:-1, 1:-1, 2:]
    return act * (diag * masked - beside_all) + (1.0 - act) * field


def operate_split(field, coefs, diag, act):
    masked = field * act
    pad = padded(masked, (("mx", 2), ("my", 3), ("vz", 1)), 1)
    return stencil(pad, coefs, diag, masked, act, field)


def chebyshev_split(rhs, operate, jacobi):
    sigma = theta_center / delta_half
    rho = 1.0 / sigma
    keep_list = []
    push_list = []
    for inner in range(STEPS - 1):
        rho_new = 1.0 / (2.0 * sigma - rho)
        keep_list.append(rho_new * rho)
        push_list.append(2.0 * rho_new / delta_half)
        rho = rho_new
    keep_table = jnp.array(keep_list, jnp.float32)
    push_table = jnp.array(push_list, jnp.float32)

    def inner_step(position, state_pair):
        iterate, step_dir = state_pair
        iterate = iterate + step_dir
        resid = rhs - operate(iterate)
        step_dir = keep_table[position] * step_dir + push_table[position] * (jacobi * resid)
        return (iterate, step_dir)

    iterate = jnp.zeros_like(rhs)
    for sweep in range(SWEEPS):
        resid = rhs if sweep == 0 else rhs - operate(iterate)
        step_dir = jacobi * resid / theta_center
        iterate, step_dir = lax.fori_loop(0, STEPS - 1, inner_step, (iterate, step_dir))
        iterate = iterate + step_dir
    return iterate


def local_split(viscosity, friction, base_velocity, grounded, ice_free, direction):
    act = (1 - ice_free).astype(jnp.float32)
    ground = grounded.astype(jnp.float32)
    layer_index = lax.axis_index("vz")
    column_devices = lax.axis_size("vz")
    bed_coef = ground * friction
    padded_eta = padded(viscosity, (("mx", 1), ("my", 2), ("vz", 0)), 1)
    on_bed = jnp.where(layer_index == 0, 1.0, 0.0).astype(jnp.float32)
    core, coefs = coefficients(padded_eta)
    basal = jnp.zeros_like(core).at[0].set(on_bed * bed_coef)
    diag = (
        coefs[0] + coefs[1] + coefs[2] + coefs[3] + coefs[4] + coefs[5] + shift_mass * core + basal
    )
    jacobi = 1.0 / (act * diag + 1.0 - act)
    forcing = jnp.zeros((2,) + core.shape, jnp.float32)
    forcing = forcing.at[:, 0].set(-(on_bed * bed_coef * direction)[None] * base_velocity)
    forcing = forcing * act
    pad_dir = padded(direction, (("mx", 0), ("my", 1)), 1)
    lap = (
        4.0 * direction
        - pad_dir[:-2, 1:-1]
        - pad_dir[2:, 1:-1]
        - pad_dir[1:-1, :-2]
        - pad_dir[1:-1, 2:]
    )

    def operate(field):
        return operate_split(field, coefs, diag, act)

    velocity_step = chebyshev_split(forcing, operate, jacobi)
    column = lax.psum(jnp.sum(velocity_step, axis=1), "vz") / LAYERS
    adjoint_rhs = obs_weight * act * jnp.broadcast_to(column[:, None], velocity_step.shape)
    adjoint = chebyshev_split(adjoint_rhs, operate, jacobi)
    on_top = jnp.where(layer_index == column_devices - 1, 1.0, 0.0).astype(jnp.float32)
    bed_part = on_bed * bed_coef * jnp.sum(base_velocity * adjoint[:, 0], axis=0)
    own_part = on_top * (reg_weight * lap) - bed_part
    hess_action = lax.psum(own_part, "vz")
    return (hess_action, velocity_step)


def solution(mesh):
    return jax.shard_map(
        local,
        mesh=mesh,
        in_specs=(
            P("vz", "mx", "my"),
            P("mx", "my"),
            P(None, "mx", "my"),
            P("mx", "my"),
            P("mx", "my"),
            P("mx", "my"),
        ),
        out_specs=(P("mx", "my"), P(None, "vz", "mx", "my")),
        check_vma=False,
    )
```

```python
import jax
import jax.numpy as jnp
from jax import lax
from jax.experimental import pallas as pl
from jax.experimental.pallas import tpu as pltpu
from jax.sharding import PartitionSpec as P

LAYERS = 16
STEPS = 16
SWEEPS = 2
HALO = 16

weight_z = 128.0
shift_mass = 0.05
theta_center = 1.05
delta_half = 0.95
obs_weight = 200.0
reg_weight = 0.5


def step_constants():
    sigma = theta_center / delta_half
    table = []
    for sweep in range(SWEEPS):
        rho = 1.0 / sigma
        if sweep > 0:
            table.append((None, 1.0 / theta_center))
        for inner in range(STEPS - 1):
            rho_new = 1.0 / (2.0 * sigma - rho)
            table.append((rho_new * rho, 2.0 * rho_new / delta_half))
            rho = rho_new
    return table


def harmonic(left, right):
    total = left + right
    safe = jnp.where(total > 0, total, 1.0)
    return jnp.where(total > 0, 2.0 * left * right / safe, 0.0)


def exchange_rows(ext, k, rows, axis):
    count = lax.axis_size("mx")
    forward = [(i, i + 1) for i in range(count - 1)]
    backward = [(i + 1, i) for i in range(count - 1)]
    own = lax.slice_in_dim(ext, k, k + rows, axis=axis)
    low = lax.ppermute(lax.slice_in_dim(own, rows - k, rows, axis=axis), "mx", forward)
    high = lax.ppermute(lax.slice_in_dim(own, 0, k, axis=axis), "mx", backward)
    return jnp.concatenate([low, own, high], axis=axis)


def gather_axis(block, axis, dim):
    count = lax.axis_size(axis)
    me = lax.axis_index(axis)
    seq = [block]
    for s in range(1, count):
        pairs = [(j, (j - s) % count) for j in range(count)]
        seq.append(lax.ppermute(block, axis, pairs))
    size = block.shape[dim]
    doubled = jnp.concatenate(seq + seq, axis=dim)
    return lax.dynamic_slice_in_dim(doubled, ((count - me) % count) * size, count * size, axis=dim)


def shift(a, axis, offset):
    n = a.shape[axis]
    zeros_shape = list(a.shape)
    zeros_shape[axis] = 1
    z = jnp.zeros(zeros_shape, a.dtype)
    if offset > 0:
        return jnp.concatenate([lax.slice_in_dim(a, 1, n, axis=axis), z], axis=axis)
    return jnp.concatenate([z, lax.slice_in_dim(a, 0, n - 1, axis=axis)], axis=axis)


def segment_kernel(steps, start_valid, table_ref, op_ref, rhs_ref, x_in, d_in, x_ref, d_ref):
    comps, layers = rhs_ref.shape[0], rhs_ref.shape[1]
    rows, cols = rhs_ref.shape[2], rhs_ref.shape[3]
    x_ref[...] = x_in[...]
    d_ref[...] = d_in[...]

    def one_step(lo, keep, push):
        span = pl.ds(lo, rows - 2 * lo)
        height = rows - 2 * lo
        for c in range(comps):
            x_ref[c, 1, span] = x_ref[c, 1, span] + d_ref[c, 1, span]

        def update(layer, carry):
            p = layer + 1
            c_xm = op_ref[2, layer, span]
            c_ym = op_ref[3, layer, span]
            c_xp = pltpu.roll(c_xm, height - 1, 0)
            c_yp = pltpu.roll(c_ym, cols - 1, 1)
            for c in range(comps):
                above = x_ref[c, p + 1, span] + d_ref[c, p + 1, span]
                x_ref[c, p + 1, span] = above
                centre = x_ref[c, p, span]
                beside = op_ref[0, layer, span] * x_ref[c, p - 1, span] + op_ref[1, layer, span] * above
                beside = beside + c_xm * pltpu.roll(centre, 1, 0)
                beside = beside + c_xp * pltpu.roll(centre, height - 1, 0)
                beside = beside + c_ym * pltpu.roll(centre, 1, 1)
                beside = beside + c_yp * pltpu.roll(centre, cols - 1, 1)
                resid = rhs_ref[c, layer, span] - (op_ref[4, layer, span] * centre - beside)
                if keep is None:
                    d_ref[c, p, span] = op_ref[5, layer, span] * resid / theta_center
                else:
                    d_ref[c, p, span] = keep * d_ref[c, p, span] + push * (op_ref[5, layer, span] * resid)
            return carry

        lax.fori_loop(0, layers, update, 0, unroll=True)

    def row_start(j):
        return max(min(8 * ((start_valid + j) // 8), rows // 2 - 8), 0)

    j = 0
    if steps[0][0] is None:
        one_step(row_start(0), None, None)
        j = 1
    while j < len(steps):
        lo = row_start(j)
        end = j
        while end < len(steps) and row_start(end) == lo:
            end += 1

        def body(i, carry, lo=lo):
            one_step(lo, table_ref[0, i], table_ref[1, i])
            return carry

        lax.fori_loop(j, end, body, 0)
        j = end


def run_segment(steps, start_valid, op_stack, rhs, iterate, step_dir):
    comps, layers, rows, cols = rhs.shape
    vmem = pl.BlockSpec(memory_space=pltpu.VMEM)
    smem = pl.BlockSpec(memory_space=pltpu.SMEM)
    cells = comps * layers * rows * cols
    table = jnp.array(
        [[0.0 if kp is None else kp for kp, _ in steps], [0.0 if kp is None else ps for kp, ps in steps]],
        jnp.float32,
    )
    return pl.pallas_call(
        lambda *refs: segment_kernel(steps, start_valid, *refs),
        out_shape=(
            jax.ShapeDtypeStruct(iterate.shape, jnp.float32),
            jax.ShapeDtypeStruct(iterate.shape, jnp.float32),
        ),
        in_specs=[smem] + [vmem] * 4,
        out_specs=(vmem, vmem),
        cost_estimate=pl.CostEstimate(
            flops=20 * cells * len(steps), bytes_accessed=4 * cells * 9, transcendentals=0
        ),
    )(table, op_stack, rhs, iterate, step_dir)


def local(viscosity, friction, base_velocity, grounded, ice_free, direction):
    layers_own, rows, cols_own = viscosity.shape
    if cols_own * lax.axis_size("my") > 256:
        return local_split(viscosity, friction, base_velocity, grounded, ice_free, direction)
    k = min(HALO, rows)
    act = (1 - ice_free).astype(jnp.float32)
    bed_coef = grounded.astype(jnp.float32) * friction
    planes = jnp.stack([act, bed_coef, base_velocity[0], base_velocity[1], direction])
    both = gather_axis(jnp.concatenate([viscosity, planes], axis=0), "my", 2)
    planes = both[layers_own:]
    eta = gather_axis(both[:layers_own], "vz", 0)
    layers = eta.shape[0]
    joined = jnp.concatenate([eta, planes], axis=0)
    zeros_halo = jnp.zeros(joined.shape[:1] + (k,) + joined.shape[2:], joined.dtype)
    joined = exchange_rows(jnp.concatenate([zeros_halo, joined, zeros_halo], axis=1), k, rows, 1)
    eta = joined[:layers]
    act, bed_coef, bv0, bv1, dir_ext = (joined[layers + i] for i in range(5))
    bv = jnp.stack([bv0, bv1])

    c_zm = weight_z * harmonic(eta, shift(eta, 0, -1))
    c_zp = weight_z * harmonic(eta, shift(eta, 0, 1))
    c_xm = harmonic(eta, shift(eta, 1, -1))
    c_xp = harmonic(eta, shift(eta, 1, 1))
    c_ym = harmonic(eta, shift(eta, 2, -1))
    c_yp = harmonic(eta, shift(eta, 2, 1))
    basal = jnp.zeros_like(eta).at[0].set(bed_coef)
    diag = c_zm + c_zp + c_xm + c_xp + c_ym + c_yp + shift_mass * eta + basal
    jacobi = 1.0 / (act * diag + 1.0 - act)

    on = act > 0
    op_stack = jnp.stack(
        [
            act * c_zm,
            act * c_zp,
            act * c_xm * shift(act, 0, -1),
            act * c_ym * shift(act, 1, -1),
            jnp.where(on, diag, 1.0),
            jacobi,
        ]
    )
    table = step_constants()
    layer_pad = ((0, 0), (1, 1), (0, 0), (0, 0))

    def chebyshev(rhs):
        iterate = jnp.zeros((2, layers + 2) + rhs.shape[2:], jnp.float32)
        step_dir = jnp.pad(jacobi * rhs / theta_center, layer_pad)
        since = 1
        start_valid = 1
        run = []
        for keep, push in table:
            if since == k:
                iterate, step_dir = run_segment(tuple(run), start_valid, op_stack, rhs, iterate, step_dir)
                run = []
                start_valid = 0
                both = exchange_rows(jnp.stack([iterate, step_dir]), k, rows, 3)
                iterate, step_dir = both[0], both[1]
                since = 0
            run.append((keep, push))
            since += 1
        iterate, step_dir = run_segment(tuple(run), start_valid, op_stack, rhs, iterate, step_dir)
        return (iterate + step_dir)[:, 1 : layers + 1]

    forcing = jnp.zeros((2,) + eta.shape, jnp.float32)
    forcing = forcing.at[:, 0].set(-(bed_coef * dir_ext)[None] * bv)
    forcing = forcing * act
    velocity_ext = chebyshev(forcing)
    column = jnp.sum(velocity_ext, axis=1) / layers
    column = exchange_rows(column, k, rows, 1)
    adjoint_rhs = obs_weight * act * jnp.broadcast_to(column[:, None], velocity_ext.shape)
    adjoint = chebyshev(adjoint_rhs)

    bed_term = bed_coef * jnp.sum(bv * adjoint[:, 0], axis=0)
    lap = (
        4.0 * dir_ext
        - shift(dir_ext, 0, -1)
        - shift(dir_ext, 0, 1)
        - shift(dir_ext, 1, -1)
        - shift(dir_ext, 1, 1)
    )
    hess_ext = -bed_term + reg_weight * lap
    col0 = lax.axis_index("my") * cols_own
    layer0 = lax.axis_index("vz") * layers_own
    hess_action = lax.dynamic_slice(hess_ext, (k, col0), (rows, cols_own))
    velocity_step = lax.dynamic_slice(
        velocity_ext, (0, layer0, k, col0), (2, layers_own, rows, cols_own)
    )
    return (hess_action, velocity_step)


def plain_harmonic(left, right):
    return 2.0 * left * right / (left + right)


def padded(block, sides, width):
    for axis, dim in sides:
        count = lax.axis_size(axis)
        forward = [(i, i + 1) for i in range(count - 1)]
        backward = [(target, source) for source, target in forward]
        low = lax.ppermute(
            lax.slice_in_dim(block, block.shape[dim] - width, None, axis=dim), axis, forward
        )
        high = lax.ppermute(lax.slice_in_dim(block, 0, width, axis=dim), axis, backward)
        block = jnp.concatenate([low, block, high], axis=dim)
    return block


def coefficients(padded_eta):
    core = padded_eta[1:-1, 1:-1, 1:-1]
    coefs = (
        weight_z * plain_harmonic(core, padded_eta[:-2, 1:-1, 1:-1]),
        weight_z * plain_harmonic(core, padded_eta[2:, 1:-1, 1:-1]),
        plain_harmonic(core, padded_eta[1:-1, :-2, 1:-1]),
        plain_harmonic(core, padded_eta[1:-1, 2:, 1:-1]),
        plain_harmonic(core, padded_eta[1:-1, 1:-1, :-2]),
        plain_harmonic(core, padded_eta[1:-1, 1:-1, 2:]),
    )
    return (core, coefs)


def stencil(pad, coefs, diag, masked, act, field):
    beside_all = coefs[0] * pad[:, :-2, 1:-1, 1:-1] + coefs[1] * pad[:, 2:, 1:-1, 1:-1]
    beside_all = beside_all + coefs[2] * pad[:, 1:-1, :-2, 1:-1] + coefs[3] * pad[:, 1:-1, 2:, 1:-1]
    beside_all = beside_all + coefs[4] * pad[:, 1:-1, 1:-1, :-2] + coefs[5] * pad[:, 1:-1, 1:-1, 2:]
    return act * (diag * masked - beside_all) + (1.0 - act) * field


def operate_split(field, coefs, diag, act):
    masked = field * act
    pad = padded(masked, (("mx", 2), ("my", 3), ("vz", 1)), 1)
    return stencil(pad, coefs, diag, masked, act, field)


def chebyshev_split(rhs, operate, jacobi):
    sigma = theta_center / delta_half
    rho = 1.0 / sigma
    keep_list = []
    push_list = []
    for inner in range(STEPS - 1):
        rho_new = 1.0 / (2.0 * sigma - rho)
        keep_list.append(rho_new * rho)
        push_list.append(2.0 * rho_new / delta_half)
        rho = rho_new
    keep_table = jnp.array(keep_list, jnp.float32)
    push_table = jnp.array(push_list, jnp.float32)

    def inner_step(position, state_pair):
        iterate, step_dir = state_pair
        iterate = iterate + step_dir
        resid = rhs - operate(iterate)
        step_dir = keep_table[position] * step_dir + push_table[position] * (jacobi * resid)
        return (iterate, step_dir)

    iterate = jnp.zeros_like(rhs)
    for sweep in range(SWEEPS):
        resid = rhs if sweep == 0 else rhs - operate(iterate)
        step_dir = jacobi * resid / theta_center
        iterate, step_dir = lax.fori_loop(0, STEPS - 1, inner_step, (iterate, step_dir))
        iterate = iterate + step_dir
    return iterate


def local_split(viscosity, friction, base_velocity, grounded, ice_free, direction):
    act = (1 - ice_free).astype(jnp.float32)
    ground = grounded.astype(jnp.float32)
    layer_index = lax.axis_index("vz")
    column_devices = lax.axis_size("vz")
    bed_coef = ground * friction
    padded_eta = padded(viscosity, (("mx", 1), ("my", 2), ("vz", 0)), 1)
    on_bed = jnp.where(layer_index == 0, 1.0, 0.0).astype(jnp.float32)
    core, coefs = coefficients(padded_eta)
    basal = jnp.zeros_like(core).at[0].set(on_bed * bed_coef)
    diag = (
        coefs[0] + coefs[1] + coefs[2] + coefs[3] + coefs[4] + coefs[5] + shift_mass * core + basal
    )
    jacobi = 1.0 / (act * diag + 1.0 - act)
    forcing = jnp.zeros((2,) + core.shape, jnp.float32)
    forcing = forcing.at[:, 0].set(-(on_bed * bed_coef * direction)[None] * base_velocity)
    forcing = forcing * act
    pad_dir = padded(direction, (("mx", 0), ("my", 1)), 1)
    lap = (
        4.0 * direction
        - pad_dir[:-2, 1:-1]
        - pad_dir[2:, 1:-1]
        - pad_dir[1:-1, :-2]
        - pad_dir[1:-1, 2:]
    )

    def operate(field):
        return operate_split(field, coefs, diag, act)

    velocity_step = chebyshev_split(forcing, operate, jacobi)
    column = lax.psum(jnp.sum(velocity_step, axis=1), "vz") / LAYERS
    adjoint_rhs = obs_weight * act * jnp.broadcast_to(column[:, None], velocity_step.shape)
    adjoint = chebyshev_split(adjoint_rhs, operate, jacobi)
    on_top = jnp.where(layer_index == column_devices - 1, 1.0, 0.0).astype(jnp.float32)
    bed_part = on_bed * bed_coef * jnp.sum(base_velocity * adjoint[:, 0], axis=0)
    own_part = on_top * (reg_weight * lap) - bed_part
    hess_action = lax.psum(own_part, "vz")
    return (hess_action, velocity_step)


def solution(mesh):
    return jax.shard_map(
        local,
        mesh=mesh,
        in_specs=(
            P("vz", "mx", "my"),
            P("mx", "my"),
            P(None, "mx", "my"),
            P("mx", "my"),
            P("mx", "my"),
            P("mx", "my"),
        ),
        out_specs=(P("mx", "my"), P(None, "vz", "mx", "my")),
        check_vma=False,
    )
```

```python
import jax
import jax.numpy as jnp
from jax import lax
from jax.experimental import pallas as pl
from jax.experimental.pallas import tpu as pltpu
from jax.sharding import PartitionSpec as P

LAYERS = 16
STEPS = 16
SWEEPS = 2
HALO = 16

weight_z = 128.0
shift_mass = 0.05
theta_center = 1.05
delta_half = 0.95
obs_weight = 200.0
reg_weight = 0.5


def step_constants():
    sigma = theta_center / delta_half
    table = []
    for sweep in range(SWEEPS):
        rho = 1.0 / sigma
        if sweep > 0:
            table.append((None, 1.0 / theta_center))
        for inner in range(STEPS - 1):
            rho_new = 1.0 / (2.0 * sigma - rho)
            table.append((rho_new * rho, 2.0 * rho_new / delta_half))
            rho = rho_new
    return table


def harmonic(left, right):
    total = left + right
    safe = jnp.where(total > 0, total, 1.0)
    return jnp.where(total > 0, 2.0 * left * right / safe, 0.0)


def exchange_rows(ext, k, rows, axis):
    count = lax.axis_size("mx")
    forward = [(i, i + 1) for i in range(count - 1)]
    backward = [(i + 1, i) for i in range(count - 1)]
    own = lax.slice_in_dim(ext, k, k + rows, axis=axis)
    low = lax.ppermute(lax.slice_in_dim(own, rows - k, rows, axis=axis), "mx", forward)
    high = lax.ppermute(lax.slice_in_dim(own, 0, k, axis=axis), "mx", backward)
    return jnp.concatenate([low, own, high], axis=axis)


def gather_axis(block, axis, dim):
    count = lax.axis_size(axis)
    me = lax.axis_index(axis)
    seq = [block]
    for s in range(1, count):
        pairs = [(j, (j - s) % count) for j in range(count)]
        seq.append(lax.ppermute(block, axis, pairs))
    size = block.shape[dim]
    doubled = jnp.concatenate(seq + seq, axis=dim)
    return lax.dynamic_slice_in_dim(doubled, ((count - me) % count) * size, count * size, axis=dim)


def shift(a, axis, offset):
    n = a.shape[axis]
    zeros_shape = list(a.shape)
    zeros_shape[axis] = 1
    z = jnp.zeros(zeros_shape, a.dtype)
    if offset > 0:
        return jnp.concatenate([lax.slice_in_dim(a, 1, n, axis=axis), z], axis=axis)
    return jnp.concatenate([z, lax.slice_in_dim(a, 0, n - 1, axis=axis)], axis=axis)


def segment_kernel(steps, start_valid, table_ref, op_ref, rhs_ref, *refs):
    comps, layers = rhs_ref.shape[0], rhs_ref.shape[1]
    rows, cols = rhs_ref.shape[2], rhs_ref.shape[3]
    if len(refs) == 4:
        x_in, d_in, x_ref, d_ref = refs
        x_ref[...] = x_in[...]
        d_ref[...] = d_in[...]
    else:
        x_ref, d_ref = refs
        zero = jnp.zeros((rows, cols), jnp.float32)
        for c in range(comps):
            x_ref[c, 0] = zero
            d_ref[c, 0] = zero
            x_ref[c, layers + 1] = zero
            d_ref[c, layers + 1] = zero

        def start(layer, carry):
            for c in range(comps):
                x_ref[c, layer + 1] = zero
                d_ref[c, layer + 1] = op_ref[5, layer] * rhs_ref[c, layer] / theta_center
            return carry

        lax.fori_loop(0, layers, start, 0)

    def one_step(lo, keep, push):
        span = pl.ds(lo, rows - 2 * lo)
        height = rows - 2 * lo
        for c in range(comps):
            x_ref[c, 1, span] = x_ref[c, 1, span] + d_ref[c, 1, span]

        def update(layer, carry):
            p = layer + 1
            c_xm = op_ref[2, layer, span]
            c_ym = op_ref[3, layer, span]
            c_xp = pltpu.roll(c_xm, height - 1, 0)
            c_yp = pltpu.roll(c_ym, cols - 1, 1)
            for c in range(comps):
                above = x_ref[c, p + 1, span] + d_ref[c, p + 1, span]
                x_ref[c, p + 1, span] = above
                centre = x_ref[c, p, span]
                beside = op_ref[0, layer, span] * x_ref[c, p - 1, span] + op_ref[1, layer, span] * above
                beside = beside + c_xm * pltpu.roll(centre, 1, 0)
                beside = beside + c_xp * pltpu.roll(centre, height - 1, 0)
                beside = beside + c_ym * pltpu.roll(centre, 1, 1)
                beside = beside + c_yp * pltpu.roll(centre, cols - 1, 1)
                resid = rhs_ref[c, layer, span] - (op_ref[4, layer, span] * centre - beside)
                if keep is None:
                    d_ref[c, p, span] = op_ref[5, layer, span] * resid / theta_center
                else:
                    d_ref[c, p, span] = keep * d_ref[c, p, span] + push * (op_ref[5, layer, span] * resid)
            return carry

        lax.fori_loop(0, layers, update, 0, unroll=True)

    def row_start(j):
        return max(min(8 * ((start_valid + j) // 8), rows // 2 - 8), 0)

    j = 0
    if steps[0][0] is None:
        one_step(row_start(0), None, None)
        j = 1
    while j < len(steps):
        lo = row_start(j)
        end = j
        while end < len(steps) and row_start(end) == lo:
            end += 1

        def body(i, carry, lo=lo):
            one_step(lo, table_ref[0, i], table_ref[1, i])
            return carry

        lax.fori_loop(j, end, body, 0)
        j = end


def run_segment(steps, start_valid, op_stack, rhs, iterate, step_dir):
    comps, layers, rows, cols = rhs.shape
    vmem = pl.BlockSpec(memory_space=pltpu.VMEM)
    smem = pl.BlockSpec(memory_space=pltpu.SMEM)
    cells = comps * layers * rows * cols
    table = jnp.array(
        [[0.0 if kp is None else kp for kp, _ in steps], [0.0 if kp is None else ps for kp, ps in steps]],
        jnp.float32,
    )
    state = () if iterate is None else (iterate, step_dir)
    padded_shape = (comps, layers + 2, rows, cols)
    return pl.pallas_call(
        lambda *refs: segment_kernel(steps, start_valid, *refs),
        out_shape=(
            jax.ShapeDtypeStruct(padded_shape, jnp.float32),
            jax.ShapeDtypeStruct(padded_shape, jnp.float32),
        ),
        in_specs=[smem] + [vmem] * (2 + len(state)),
        out_specs=(vmem, vmem),
        cost_estimate=pl.CostEstimate(
            flops=20 * cells * len(steps), bytes_accessed=4 * cells * 9, transcendentals=0
        ),
    )(table, op_stack, rhs, *state)


def local(viscosity, friction, base_velocity, grounded, ice_free, direction):
    layers_own, rows, cols_own = viscosity.shape
    if cols_own * lax.axis_size("my") > 256:
        return local_split(viscosity, friction, base_velocity, grounded, ice_free, direction)
    k = min(HALO, rows)
    act = (1 - ice_free).astype(jnp.float32)
    bed_coef = grounded.astype(jnp.float32) * friction
    planes = jnp.stack([act, bed_coef, base_velocity[0], base_velocity[1], direction])
    both = gather_axis(jnp.concatenate([viscosity, planes], axis=0), "my", 2)
    planes = both[layers_own:]
    eta = gather_axis(both[:layers_own], "vz", 0)
    layers = eta.shape[0]
    joined = jnp.concatenate([eta, planes], axis=0)
    zeros_halo = jnp.zeros(joined.shape[:1] + (k,) + joined.shape[2:], joined.dtype)
    joined = exchange_rows(jnp.concatenate([zeros_halo, joined, zeros_halo], axis=1), k, rows, 1)
    eta = joined[:layers]
    act, bed_coef, bv0, bv1, dir_ext = (joined[layers + i] for i in range(5))
    bv = jnp.stack([bv0, bv1])

    c_zm = weight_z * harmonic(eta, shift(eta, 0, -1))
    c_zp = weight_z * harmonic(eta, shift(eta, 0, 1))
    c_xm = harmonic(eta, shift(eta, 1, -1))
    c_xp = harmonic(eta, shift(eta, 1, 1))
    c_ym = harmonic(eta, shift(eta, 2, -1))
    c_yp = harmonic(eta, shift(eta, 2, 1))
    basal = jnp.zeros_like(eta).at[0].set(bed_coef)
    diag = c_zm + c_zp + c_xm + c_xp + c_ym + c_yp + shift_mass * eta + basal
    jacobi = 1.0 / (act * diag + 1.0 - act)

    on = act > 0
    op_stack = jnp.stack(
        [
            act * c_zm,
            act * c_zp,
            act * c_xm * shift(act, 0, -1),
            act * c_ym * shift(act, 1, -1),
            jnp.where(on, diag, 1.0),
            jacobi,
        ]
    )
    table = step_constants()

    def chebyshev(rhs):
        iterate, step_dir = None, None
        since = 1
        start_valid = 1
        run = []
        for keep, push in table:
            if since == k:
                iterate, step_dir = run_segment(tuple(run), start_valid, op_stack, rhs, iterate, step_dir)
                run = []
                start_valid = 0
                both = exchange_rows(jnp.stack([iterate, step_dir]), k, rows, 3)
                iterate, step_dir = both[0], both[1]
                since = 0
            run.append((keep, push))
            since += 1
        iterate, step_dir = run_segment(tuple(run), start_valid, op_stack, rhs, iterate, step_dir)
        return (iterate + step_dir)[:, 1 : layers + 1]

    forcing = jnp.zeros((2,) + eta.shape, jnp.float32)
    forcing = forcing.at[:, 0].set(-(bed_coef * dir_ext)[None] * bv)
    forcing = forcing * act
    velocity_ext = chebyshev(forcing)
    column = jnp.sum(velocity_ext, axis=1) / layers
    column = exchange_rows(column, k, rows, 1)
    adjoint_rhs = obs_weight * act * jnp.broadcast_to(column[:, None], velocity_ext.shape)
    adjoint = chebyshev(adjoint_rhs)

    bed_term = bed_coef * jnp.sum(bv * adjoint[:, 0], axis=0)
    lap = (
        4.0 * dir_ext
        - shift(dir_ext, 0, -1)
        - shift(dir_ext, 0, 1)
        - shift(dir_ext, 1, -1)
        - shift(dir_ext, 1, 1)
    )
    hess_ext = -bed_term + reg_weight * lap
    col0 = lax.axis_index("my") * cols_own
    layer0 = lax.axis_index("vz") * layers_own
    hess_action = lax.dynamic_slice(hess_ext, (k, col0), (rows, cols_own))
    velocity_step = lax.dynamic_slice(
        velocity_ext, (0, layer0, k, col0), (2, layers_own, rows, cols_own)
    )
    return (hess_action, velocity_step)


def plain_harmonic(left, right):
    return 2.0 * left * right / (left + right)


def padded(block, sides, width):
    for axis, dim in sides:
        count = lax.axis_size(axis)
        forward = [(i, i + 1) for i in range(count - 1)]
        backward = [(target, source) for source, target in forward]
        low = lax.ppermute(
            lax.slice_in_dim(block, block.shape[dim] - width, None, axis=dim), axis, forward
        )
        high = lax.ppermute(lax.slice_in_dim(block, 0, width, axis=dim), axis, backward)
        block = jnp.concatenate([low, block, high], axis=dim)
    return block


def coefficients(padded_eta):
    core = padded_eta[1:-1, 1:-1, 1:-1]
    coefs = (
        weight_z * plain_harmonic(core, padded_eta[:-2, 1:-1, 1:-1]),
        weight_z * plain_harmonic(core, padded_eta[2:, 1:-1, 1:-1]),
        plain_harmonic(core, padded_eta[1:-1, :-2, 1:-1]),
        plain_harmonic(core, padded_eta[1:-1, 2:, 1:-1]),
        plain_harmonic(core, padded_eta[1:-1, 1:-1, :-2]),
        plain_harmonic(core, padded_eta[1:-1, 1:-1, 2:]),
    )
    return (core, coefs)


def stencil(pad, coefs, diag, masked, act, field):
    beside_all = coefs[0] * pad[:, :-2, 1:-1, 1:-1] + coefs[1] * pad[:, 2:, 1:-1, 1:-1]
    beside_all = beside_all + coefs[2] * pad[:, 1:-1, :-2, 1:-1] + coefs[3] * pad[:, 1:-1, 2:, 1:-1]
    beside_all = beside_all + coefs[4] * pad[:, 1:-1, 1:-1, :-2] + coefs[5] * pad[:, 1:-1, 1:-1, 2:]
    return act * (diag * masked - beside_all) + (1.0 - act) * field


def operate_split(field, coefs, diag, act):
    masked = field * act
    pad = padded(masked, (("mx", 2), ("my", 3), ("vz", 1)), 1)
    return stencil(pad, coefs, diag, masked, act, field)


def chebyshev_split(rhs, operate, jacobi):
    sigma = theta_center / delta_half
    rho = 1.0 / sigma
    keep_list = []
    push_list = []
    for inner in range(STEPS - 1):
        rho_new = 1.0 / (2.0 * sigma - rho)
        keep_list.append(rho_new * rho)
        push_list.append(2.0 * rho_new / delta_half)
        rho = rho_new
    keep_table = jnp.array(keep_list, jnp.float32)
    push_table = jnp.array(push_list, jnp.float32)

    def inner_step(position, state_pair):
        iterate, step_dir = state_pair
        iterate = iterate + step_dir
        resid = rhs - operate(iterate)
        step_dir = keep_table[position] * step_dir + push_table[position] * (jacobi * resid)
        return (iterate, step_dir)

    iterate = jnp.zeros_like(rhs)
    for sweep in range(SWEEPS):
        resid = rhs if sweep == 0 else rhs - operate(iterate)
        step_dir = jacobi * resid / theta_center
        iterate, step_dir = lax.fori_loop(0, STEPS - 1, inner_step, (iterate, step_dir))
        iterate = iterate + step_dir
    return iterate


def local_split(viscosity, friction, base_velocity, grounded, ice_free, direction):
    act = (1 - ice_free).astype(jnp.float32)
    ground = grounded.astype(jnp.float32)
    layer_index = lax.axis_index("vz")
    column_devices = lax.axis_size("vz")
    bed_coef = ground * friction
    padded_eta = padded(viscosity, (("mx", 1), ("my", 2), ("vz", 0)), 1)
    on_bed = jnp.where(layer_index == 0, 1.0, 0.0).astype(jnp.float32)
    core, coefs = coefficients(padded_eta)
    basal = jnp.zeros_like(core).at[0].set(on_bed * bed_coef)
    diag = (
        coefs[0] + coefs[1] + coefs[2] + coefs[3] + coefs[4] + coefs[5] + shift_mass * core + basal
    )
    jacobi = 1.0 / (act * diag + 1.0 - act)
    forcing = jnp.zeros((2,) + core.shape, jnp.float32)
    forcing = forcing.at[:, 0].set(-(on_bed * bed_coef * direction)[None] * base_velocity)
    forcing = forcing * act
    pad_dir = padded(direction, (("mx", 0), ("my", 1)), 1)
    lap = (
        4.0 * direction
        - pad_dir[:-2, 1:-1]
        - pad_dir[2:, 1:-1]
        - pad_dir[1:-1, :-2]
        - pad_dir[1:-1, 2:]
    )

    def operate(field):
        return operate_split(field, coefs, diag, act)

    velocity_step = chebyshev_split(forcing, operate, jacobi)
    column = lax.psum(jnp.sum(velocity_step, axis=1), "vz") / LAYERS
    adjoint_rhs = obs_weight * act * jnp.broadcast_to(column[:, None], velocity_step.shape)
    adjoint = chebyshev_split(adjoint_rhs, operate, jacobi)
    on_top = jnp.where(layer_index == column_devices - 1, 1.0, 0.0).astype(jnp.float32)
    bed_part = on_bed * bed_coef * jnp.sum(base_velocity * adjoint[:, 0], axis=0)
    own_part = on_top * (reg_weight * lap) - bed_part
    hess_action = lax.psum(own_part, "vz")
    return (hess_action, velocity_step)


def solution(mesh):
    return jax.shard_map(
        local,
        mesh=mesh,
        in_specs=(
            P("vz", "mx", "my"),
            P("mx", "my"),
            P(None, "mx", "my"),
            P("mx", "my"),
            P("mx", "my"),
            P("mx", "my"),
        ),
        out_specs=(P("mx", "my"), P(None, "vz", "mx", "my")),
        check_vma=False,
    )
```

```python
import jax
import jax.numpy as jnp
from jax import lax
from jax.experimental import pallas as pl
from jax.experimental.pallas import tpu as pltpu
from jax.sharding import PartitionSpec as P

LAYERS = 16
STEPS = 16
SWEEPS = 2
HALO = 16

weight_z = 128.0
shift_mass = 0.05
theta_center = 1.05
delta_half = 0.95
obs_weight = 200.0
reg_weight = 0.5


def step_constants():
    sigma = theta_center / delta_half
    table = []
    for sweep in range(SWEEPS):
        rho = 1.0 / sigma
        if sweep > 0:
            table.append((None, 1.0 / theta_center))
        for inner in range(STEPS - 1):
            rho_new = 1.0 / (2.0 * sigma - rho)
            table.append((rho_new * rho, 2.0 * rho_new / delta_half))
            rho = rho_new
    return table


def harmonic(left, right):
    total = left + right
    safe = jnp.where(total > 0, total, 1.0)
    return jnp.where(total > 0, 2.0 * left * right / safe, 0.0)


def exchange_rows(ext, k, rows, axis):
    count = lax.axis_size("mx")
    forward = [(i, i + 1) for i in range(count - 1)]
    backward = [(i + 1, i) for i in range(count - 1)]
    own = lax.slice_in_dim(ext, k, k + rows, axis=axis)
    low = lax.ppermute(lax.slice_in_dim(own, rows - k, rows, axis=axis), "mx", forward)
    high = lax.ppermute(lax.slice_in_dim(own, 0, k, axis=axis), "mx", backward)
    return jnp.concatenate([low, own, high], axis=axis)


def gather_axis(block, axis, dim):
    count = lax.axis_size(axis)
    me = lax.axis_index(axis)
    seq = [block]
    for s in range(1, count):
        pairs = [(j, (j - s) % count) for j in range(count)]
        seq.append(lax.ppermute(block, axis, pairs))
    size = block.shape[dim]
    doubled = jnp.concatenate(seq + seq, axis=dim)
    return lax.dynamic_slice_in_dim(doubled, ((count - me) % count) * size, count * size, axis=dim)


def shift(a, axis, offset):
    n = a.shape[axis]
    zeros_shape = list(a.shape)
    zeros_shape[axis] = 1
    z = jnp.zeros(zeros_shape, a.dtype)
    if offset > 0:
        return jnp.concatenate([lax.slice_in_dim(a, 1, n, axis=axis), z], axis=axis)
    return jnp.concatenate([z, lax.slice_in_dim(a, 0, n - 1, axis=axis)], axis=axis)


def segment_kernel(steps, start_valid, halo, send, table_ref, op_ref, rhs_ref, *refs):
    comps, layers = rhs_ref.shape[0], rhs_ref.shape[1]
    rows, cols = rhs_ref.shape[2], rhs_ref.shape[3]
    own = rows - 2 * halo
    if send:
        refs, up_ref, down_ref = refs[:-2], refs[-2], refs[-1]
    if len(refs) == 6:
        x_in, d_in, low_in, high_in, x_ref, d_ref = refs
        x_ref[...] = x_in[...]
        d_ref[...] = d_in[...]

        def place(layer, carry):
            for c in range(comps):
                for f, ref in enumerate((x_ref, d_ref)):
                    ref[c, layer + 1, pl.ds(0, halo)] = low_in[f, c, layer]
                    ref[c, layer + 1, pl.ds(halo + own, halo)] = high_in[f, c, layer]
            return carry

        lax.fori_loop(0, layers, place, 0)
    else:
        x_ref, d_ref = refs
        zero = jnp.zeros((rows, cols), jnp.float32)
        for c in range(comps):
            x_ref[c, 0] = zero
            d_ref[c, 0] = zero
            x_ref[c, layers + 1] = zero
            d_ref[c, layers + 1] = zero

        def start(layer, carry):
            for c in range(comps):
                x_ref[c, layer + 1] = zero
                d_ref[c, layer + 1] = op_ref[5, layer] * rhs_ref[c, layer] / theta_center
            return carry

        lax.fori_loop(0, layers, start, 0)

    def one_step(lo, keep, push):
        span = pl.ds(lo, rows - 2 * lo)
        height = rows - 2 * lo
        for c in range(comps):
            x_ref[c, 1, span] = x_ref[c, 1, span] + d_ref[c, 1, span]

        def update(layer, carry):
            p = layer + 1
            c_xm = op_ref[2, layer, span]
            c_ym = op_ref[3, layer, span]
            c_xp = pltpu.roll(c_xm, height - 1, 0)
            c_yp = pltpu.roll(c_ym, cols - 1, 1)
            for c in range(comps):
                above = x_ref[c, p + 1, span] + d_ref[c, p + 1, span]
                x_ref[c, p + 1, span] = above
                centre = x_ref[c, p, span]
                beside = op_ref[0, layer, span] * x_ref[c, p - 1, span] + op_ref[1, layer, span] * above
                beside = beside + c_xm * pltpu.roll(centre, 1, 0)
                beside = beside + c_xp * pltpu.roll(centre, height - 1, 0)
                beside = beside + c_ym * pltpu.roll(centre, 1, 1)
                beside = beside + c_yp * pltpu.roll(centre, cols - 1, 1)
                resid = rhs_ref[c, layer, span] - (op_ref[4, layer, span] * centre - beside)
                if keep is None:
                    d_ref[c, p, span] = op_ref[5, layer, span] * resid / theta_center
                else:
                    d_ref[c, p, span] = keep * d_ref[c, p, span] + push * (op_ref[5, layer, span] * resid)
            return carry

        lax.fori_loop(0, layers, update, 0, unroll=True)

    def row_start(j):
        return max(min(8 * ((start_valid + j) // 8), rows // 2 - 8), 0)

    j = 0
    if steps[0][0] is None:
        one_step(row_start(0), None, None)
        j = 1
    while j < len(steps):
        lo = row_start(j)
        end = j
        while end < len(steps) and row_start(end) == lo:
            end += 1

        def body(i, carry, lo=lo):
            one_step(lo, table_ref[0, i], table_ref[1, i])
            return carry

        lax.fori_loop(j, end, body, 0)
        j = end

    if send:
        def pack(layer, carry):
            for c in range(comps):
                for f, ref in enumerate((x_ref, d_ref)):
                    up_ref[f, c, layer] = ref[c, layer + 1, pl.ds(own, halo)]
                    down_ref[f, c, layer] = ref[c, layer + 1, pl.ds(halo, halo)]
            return carry

        lax.fori_loop(0, layers, pack, 0)


def run_segment(steps, start_valid, halo, send, op_stack, rhs, state):
    comps, layers, rows, cols = rhs.shape
    vmem = pl.BlockSpec(memory_space=pltpu.VMEM)
    smem = pl.BlockSpec(memory_space=pltpu.SMEM)
    cells = comps * layers * rows * cols
    table = jnp.array(
        [[0.0 if kp is None else kp for kp, _ in steps], [0.0 if kp is None else ps for kp, ps in steps]],
        jnp.float32,
    )
    padded_shape = jax.ShapeDtypeStruct((comps, layers + 2, rows, cols), jnp.float32)
    slab_shape = jax.ShapeDtypeStruct((2, comps, layers, halo, cols), jnp.float32)
    out_shape = (padded_shape, padded_shape) + ((slab_shape, slab_shape) if send else ())
    return pl.pallas_call(
        lambda *refs: segment_kernel(steps, start_valid, halo, send, *refs),
        out_shape=out_shape,
        in_specs=[smem] + [vmem] * (2 + len(state)),
        out_specs=tuple(vmem for _ in out_shape),
        cost_estimate=pl.CostEstimate(
            flops=20 * cells * len(steps), bytes_accessed=4 * cells * 9, transcendentals=0
        ),
    )(table, op_stack, rhs, *state)


def local(viscosity, friction, base_velocity, grounded, ice_free, direction):
    layers_own, rows, cols_own = viscosity.shape
    if cols_own * lax.axis_size("my") > 256:
        return local_split(viscosity, friction, base_velocity, grounded, ice_free, direction)
    k = min(HALO, rows)
    act = (1 - ice_free).astype(jnp.float32)
    bed_coef = grounded.astype(jnp.float32) * friction
    planes = jnp.stack([act, bed_coef, base_velocity[0], base_velocity[1], direction])
    both = gather_axis(jnp.concatenate([viscosity, planes], axis=0), "my", 2)
    planes = both[layers_own:]
    eta = gather_axis(both[:layers_own], "vz", 0)
    layers = eta.shape[0]
    joined = jnp.concatenate([eta, planes], axis=0)
    zeros_halo = jnp.zeros(joined.shape[:1] + (k,) + joined.shape[2:], joined.dtype)
    joined = exchange_rows(jnp.concatenate([zeros_halo, joined, zeros_halo], axis=1), k, rows, 1)
    eta = joined[:layers]
    act, bed_coef, bv0, bv1, dir_ext = (joined[layers + i] for i in range(5))
    bv = jnp.stack([bv0, bv1])

    c_zm = weight_z * harmonic(eta, shift(eta, 0, -1))
    c_zp = weight_z * harmonic(eta, shift(eta, 0, 1))
    c_xm = harmonic(eta, shift(eta, 1, -1))
    c_xp = harmonic(eta, shift(eta, 1, 1))
    c_ym = harmonic(eta, shift(eta, 2, -1))
    c_yp = harmonic(eta, shift(eta, 2, 1))
    basal = jnp.zeros_like(eta).at[0].set(bed_coef)
    diag = c_zm + c_zp + c_xm + c_xp + c_ym + c_yp + shift_mass * eta + basal
    jacobi = 1.0 / (act * diag + 1.0 - act)

    on = act > 0
    op_stack = jnp.stack(
        [
            act * c_zm,
            act * c_zp,
            act * c_xm * shift(act, 0, -1),
            act * c_ym * shift(act, 1, -1),
            jnp.where(on, diag, 1.0),
            jacobi,
        ]
    )
    table = step_constants()

    def chebyshev(rhs):
        count = lax.axis_size("mx")
        forward = [(i, i + 1) for i in range(count - 1)]
        backward = [(i + 1, i) for i in range(count - 1)]
        state = ()
        since = 1
        start_valid = 1
        run = []
        for keep, push in table:
            if since == k:
                iterate, step_dir, up, down = run_segment(
                    tuple(run), start_valid, k, True, op_stack, rhs, state
                )
                low = lax.ppermute(up, "mx", forward)
                high = lax.ppermute(down, "mx", backward)
                state = (iterate, step_dir, low, high)
                run = []
                start_valid = 0
                since = 0
            run.append((keep, push))
            since += 1
        iterate, step_dir = run_segment(tuple(run), start_valid, k, False, op_stack, rhs, state)
        return (iterate + step_dir)[:, 1 : layers + 1]

    forcing = jnp.zeros((2,) + eta.shape, jnp.float32)
    forcing = forcing.at[:, 0].set(-(bed_coef * dir_ext)[None] * bv)
    forcing = forcing * act
    velocity_ext = chebyshev(forcing)
    column = jnp.sum(velocity_ext, axis=1) / layers
    column = exchange_rows(column, k, rows, 1)
    adjoint_rhs = obs_weight * act * jnp.broadcast_to(column[:, None], velocity_ext.shape)
    adjoint = chebyshev(adjoint_rhs)

    bed_term = bed_coef * jnp.sum(bv * adjoint[:, 0], axis=0)
    lap = (
        4.0 * dir_ext
        - shift(dir_ext, 0, -1)
        - shift(dir_ext, 0, 1)
        - shift(dir_ext, 1, -1)
        - shift(dir_ext, 1, 1)
    )
    hess_ext = -bed_term + reg_weight * lap
    col0 = lax.axis_index("my") * cols_own
    layer0 = lax.axis_index("vz") * layers_own
    hess_action = lax.dynamic_slice(hess_ext, (k, col0), (rows, cols_own))
    velocity_step = lax.dynamic_slice(
        velocity_ext, (0, layer0, k, col0), (2, layers_own, rows, cols_own)
    )
    return (hess_action, velocity_step)


def plain_harmonic(left, right):
    return 2.0 * left * right / (left + right)


def padded(block, sides, width):
    for axis, dim in sides:
        count = lax.axis_size(axis)
        forward = [(i, i + 1) for i in range(count - 1)]
        backward = [(target, source) for source, target in forward]
        low = lax.ppermute(
            lax.slice_in_dim(block, block.shape[dim] - width, None, axis=dim), axis, forward
        )
        high = lax.ppermute(lax.slice_in_dim(block, 0, width, axis=dim), axis, backward)
        block = jnp.concatenate([low, block, high], axis=dim)
    return block


def coefficients(padded_eta):
    core = padded_eta[1:-1, 1:-1, 1:-1]
    coefs = (
        weight_z * plain_harmonic(core, padded_eta[:-2, 1:-1, 1:-1]),
        weight_z * plain_harmonic(core, padded_eta[2:, 1:-1, 1:-1]),
        plain_harmonic(core, padded_eta[1:-1, :-2, 1:-1]),
        plain_harmonic(core, padded_eta[1:-1, 2:, 1:-1]),
        plain_harmonic(core, padded_eta[1:-1, 1:-1, :-2]),
        plain_harmonic(core, padded_eta[1:-1, 1:-1, 2:]),
    )
    return (core, coefs)


def stencil(pad, coefs, diag, masked, act, field):
    beside_all = coefs[0] * pad[:, :-2, 1:-1, 1:-1] + coefs[1] * pad[:, 2:, 1:-1, 1:-1]
    beside_all = beside_all + coefs[2] * pad[:, 1:-1, :-2, 1:-1] + coefs[3] * pad[:, 1:-1, 2:, 1:-1]
    beside_all = beside_all + coefs[4] * pad[:, 1:-1, 1:-1, :-2] + coefs[5] * pad[:, 1:-1, 1:-1, 2:]
    return act * (diag * masked - beside_all) + (1.0 - act) * field


def operate_split(field, coefs, diag, act):
    masked = field * act
    pad = padded(masked, (("mx", 2), ("my", 3), ("vz", 1)), 1)
    return stencil(pad, coefs, diag, masked, act, field)


def chebyshev_split(rhs, operate, jacobi):
    sigma = theta_center / delta_half
    rho = 1.0 / sigma
    keep_list = []
    push_list = []
    for inner in range(STEPS - 1):
        rho_new = 1.0 / (2.0 * sigma - rho)
        keep_list.append(rho_new * rho)
        push_list.append(2.0 * rho_new / delta_half)
        rho = rho_new
    keep_table = jnp.array(keep_list, jnp.float32)
    push_table = jnp.array(push_list, jnp.float32)

    def inner_step(position, state_pair):
        iterate, step_dir = state_pair
        iterate = iterate + step_dir
        resid = rhs - operate(iterate)
        step_dir = keep_table[position] * step_dir + push_table[position] * (jacobi * resid)
        return (iterate, step_dir)

    iterate = jnp.zeros_like(rhs)
    for sweep in range(SWEEPS):
        resid = rhs if sweep == 0 else rhs - operate(iterate)
        step_dir = jacobi * resid / theta_center
        iterate, step_dir = lax.fori_loop(0, STEPS - 1, inner_step, (iterate, step_dir))
        iterate = iterate + step_dir
    return iterate


def local_split(viscosity, friction, base_velocity, grounded, ice_free, direction):
    act = (1 - ice_free).astype(jnp.float32)
    ground = grounded.astype(jnp.float32)
    layer_index = lax.axis_index("vz")
    column_devices = lax.axis_size("vz")
    bed_coef = ground * friction
    padded_eta = padded(viscosity, (("mx", 1), ("my", 2), ("vz", 0)), 1)
    on_bed = jnp.where(layer_index == 0, 1.0, 0.0).astype(jnp.float32)
    core, coefs = coefficients(padded_eta)
    basal = jnp.zeros_like(core).at[0].set(on_bed * bed_coef)
    diag = (
        coefs[0] + coefs[1] + coefs[2] + coefs[3] + coefs[4] + coefs[5] + shift_mass * core + basal
    )
    jacobi = 1.0 / (act * diag + 1.0 - act)
    forcing = jnp.zeros((2,) + core.shape, jnp.float32)
    forcing = forcing.at[:, 0].set(-(on_bed * bed_coef * direction)[None] * base_velocity)
    forcing = forcing * act
    pad_dir = padded(direction, (("mx", 0), ("my", 1)), 1)
    lap = (
        4.0 * direction
        - pad_dir[:-2, 1:-1]
        - pad_dir[2:, 1:-1]
        - pad_dir[1:-1, :-2]
        - pad_dir[1:-1, 2:]
    )

    def operate(field):
        return operate_split(field, coefs, diag, act)

    velocity_step = chebyshev_split(forcing, operate, jacobi)
    column = lax.psum(jnp.sum(velocity_step, axis=1), "vz") / LAYERS
    adjoint_rhs = obs_weight * act * jnp.broadcast_to(column[:, None], velocity_step.shape)
    adjoint = chebyshev_split(adjoint_rhs, operate, jacobi)
    on_top = jnp.where(layer_index == column_devices - 1, 1.0, 0.0).astype(jnp.float32)
    bed_part = on_bed * bed_coef * jnp.sum(base_velocity * adjoint[:, 0], axis=0)
    own_part = on_top * (reg_weight * lap) - bed_part
    hess_action = lax.psum(own_part, "vz")
    return (hess_action, velocity_step)


def solution(mesh):
    return jax.shard_map(
        local,
        mesh=mesh,
        in_specs=(
            P("vz", "mx", "my"),
            P("mx", "my"),
            P(None, "mx", "my"),
            P("mx", "my"),
            P("mx", "my"),
            P("mx", "my"),
        ),
        out_specs=(P("mx", "my"), P(None, "vz", "mx", "my")),
        check_vma=False,
    )
```

```python
import jax
import jax.numpy as jnp
from jax import lax
from jax.experimental import pallas as pl
from jax.experimental.pallas import tpu as pltpu
from jax.sharding import PartitionSpec as P

LAYERS = 16
STEPS = 16
SWEEPS = 2
HALO = 16

weight_z = 128.0
shift_mass = 0.05
theta_center = 1.05
delta_half = 0.95
obs_weight = 200.0
reg_weight = 0.5


def step_constants():
    sigma = theta_center / delta_half
    table = []
    for sweep in range(SWEEPS):
        rho = 1.0 / sigma
        if sweep > 0:
            table.append((None, 1.0 / theta_center))
        for inner in range(STEPS - 1):
            rho_new = 1.0 / (2.0 * sigma - rho)
            table.append((rho_new * rho, 2.0 * rho_new / delta_half))
            rho = rho_new
    return table


def harmonic(left, right):
    total = left + right
    safe = jnp.where(total > 0, total, 1.0)
    return jnp.where(total > 0, 2.0 * left * right / safe, 0.0)


def exchange_rows(ext, k, rows, axis):
    count = lax.axis_size("mx")
    forward = [(i, i + 1) for i in range(count - 1)]
    backward = [(i + 1, i) for i in range(count - 1)]
    own = lax.slice_in_dim(ext, k, k + rows, axis=axis)
    low = lax.ppermute(lax.slice_in_dim(own, rows - k, rows, axis=axis), "mx", forward)
    high = lax.ppermute(lax.slice_in_dim(own, 0, k, axis=axis), "mx", backward)
    return jnp.concatenate([low, own, high], axis=axis)


def gather_axis(block, axis, dim):
    count = lax.axis_size(axis)
    me = lax.axis_index(axis)
    seq = [block]
    for s in range(1, count):
        pairs = [(j, (j - s) % count) for j in range(count)]
        seq.append(lax.ppermute(block, axis, pairs))
    size = block.shape[dim]
    doubled = jnp.concatenate(seq + seq, axis=dim)
    return lax.dynamic_slice_in_dim(doubled, ((count - me) % count) * size, count * size, axis=dim)


def shift(a, axis, offset):
    n = a.shape[axis]
    zeros_shape = list(a.shape)
    zeros_shape[axis] = 1
    z = jnp.zeros(zeros_shape, a.dtype)
    if offset > 0:
        return jnp.concatenate([lax.slice_in_dim(a, 1, n, axis=axis), z], axis=axis)
    return jnp.concatenate([z, lax.slice_in_dim(a, 0, n - 1, axis=axis)], axis=axis)


def segment_kernel(steps, start_valid, halo, send, table_ref, op_ref, rhs_ref, *refs):
    comps, layers = rhs_ref.shape[0], rhs_ref.shape[1]
    rows, cols = rhs_ref.shape[2], rhs_ref.shape[3]
    own = rows - 2 * halo
    if send:
        refs, up_ref, down_ref = refs[:-2], refs[-2], refs[-1]
    if len(refs) == 6:
        x_in, d_in, low_in, high_in, x_ref, d_ref = refs
        x_ref[...] = x_in[...]
        d_ref[...] = d_in[...]

        def place(layer, carry):
            for c in range(comps):
                for f, ref in enumerate((x_ref, d_ref)):
                    ref[c, layer + 1, pl.ds(0, halo)] = low_in[f, c, layer]
                    ref[c, layer + 1, pl.ds(halo + own, halo)] = high_in[f, c, layer]
            return carry

        lax.fori_loop(0, layers, place, 0)
    else:
        x_ref, d_ref = refs
        zero = jnp.zeros((rows, cols), jnp.float32)
        for c in range(comps):
            x_ref[c, 0] = zero
            d_ref[c, 0] = zero
            x_ref[c, layers + 1] = zero
            d_ref[c, layers + 1] = zero

        def start(layer, carry):
            for c in range(comps):
                x_ref[c, layer + 1] = zero
                d_ref[c, layer + 1] = op_ref[5, layer] * rhs_ref[c, layer] / theta_center
            return carry

        lax.fori_loop(0, layers, start, 0)

    def one_step(lo, keep, push):
        span = pl.ds(lo, rows - 2 * lo)
        height = rows - 2 * lo
        for c in range(comps):
            x_ref[c, 1, span] = x_ref[c, 1, span] + d_ref[c, 1, span]

        def update(layer, carry):
            p = layer + 1
            c_xm = op_ref[2, layer, span]
            c_ym = op_ref[3, layer, span]
            c_xp = pltpu.roll(c_xm, height - 1, 0)
            c_yp = pltpu.roll(c_ym, cols - 1, 1)
            for c in range(comps):
                above = x_ref[c, p + 1, span] + d_ref[c, p + 1, span]
                x_ref[c, p + 1, span] = above
                centre = x_ref[c, p, span]
                beside = op_ref[0, layer, span] * x_ref[c, p - 1, span] + op_ref[1, layer, span] * above
                beside = beside + c_xm * pltpu.roll(centre, 1, 0)
                beside = beside + c_xp * pltpu.roll(centre, height - 1, 0)
                beside = beside + c_ym * pltpu.roll(centre, 1, 1)
                beside = beside + c_yp * pltpu.roll(centre, cols - 1, 1)
                resid = rhs_ref[c, layer, span] - (op_ref[4, layer, span] * centre - beside)
                if keep is None:
                    d_ref[c, p, span] = op_ref[5, layer, span] * resid / theta_center
                else:
                    d_ref[c, p, span] = keep * d_ref[c, p, span] + push * (op_ref[5, layer, span] * resid)
            return carry

        lax.fori_loop(0, layers, update, 0, unroll=True)

    def row_start(j):
        return max(min(8 * ((start_valid + j) // 8), rows // 2 - 8), 0)

    j = 0
    if steps[0][0] is None:
        one_step(row_start(0), None, None)
        j = 1
    while j < len(steps):
        lo = row_start(j)
        end = j
        while end < len(steps) and row_start(end) == lo:
            end += 1

        def body(i, carry, lo=lo):
            one_step(lo, table_ref[0, i], table_ref[1, i])
            return carry

        lax.fori_loop(j, end, body, 0)
        j = end

    if send:
        def pack(layer, carry):
            for c in range(comps):
                for f, ref in enumerate((x_ref, d_ref)):
                    up_ref[f, c, layer] = ref[c, layer + 1, pl.ds(own, halo)]
                    down_ref[f, c, layer] = ref[c, layer + 1, pl.ds(halo, halo)]
            return carry

        lax.fori_loop(0, layers, pack, 0)


def run_segment(steps, start_valid, halo, send, op_stack, rhs, state):
    comps, layers, rows, cols = rhs.shape
    vmem = pl.BlockSpec(memory_space=pltpu.VMEM)
    smem = pl.BlockSpec(memory_space=pltpu.SMEM)
    cells = comps * layers * rows * cols
    table = jnp.array(
        [[0.0 if kp is None else kp for kp, _ in steps], [0.0 if kp is None else ps for kp, ps in steps]],
        jnp.float32,
    )
    padded_shape = jax.ShapeDtypeStruct((comps, layers + 2, rows, cols), jnp.float32)
    slab_shape = jax.ShapeDtypeStruct((2, comps, layers, halo, cols), jnp.float32)
    out_shape = (padded_shape, padded_shape) + ((slab_shape, slab_shape) if send else ())
    return pl.pallas_call(
        lambda *refs: segment_kernel(steps, start_valid, halo, send, *refs),
        out_shape=out_shape,
        in_specs=[smem] + [vmem] * (2 + len(state)),
        out_specs=tuple(vmem for _ in out_shape),
        cost_estimate=pl.CostEstimate(
            flops=20 * cells * len(steps), bytes_accessed=4 * cells * 9, transcendentals=0
        ),
    )(table, op_stack, rhs, *state)


def local(viscosity, friction, base_velocity, grounded, ice_free, direction):
    layers_own, rows, cols_own = viscosity.shape
    if cols_own * lax.axis_size("my") > 256:
        return local_split(viscosity, friction, base_velocity, grounded, ice_free, direction)
    k = min(HALO, rows)
    act = (1 - ice_free).astype(jnp.float32)
    bed_coef = grounded.astype(jnp.float32) * friction
    local_stack = jnp.concatenate(
        [viscosity, act[None], bed_coef[None], base_velocity, direction[None]], axis=0
    )
    if lax.axis_size("vz") == 2 and lax.axis_size("my") == 2:
        swap = [(0, 1), (1, 0)]
        across_my = lax.ppermute(local_stack, "my", swap)
        across_vz = lax.ppermute(viscosity, "vz", swap)
        diagonal = lax.ppermute(viscosity, ("my", "vz"), [(i, 3 - i) for i in range(4)])
        first_my = lax.axis_index("my") == 0
        first_vz = lax.axis_index("vz") == 0

        def by_my(mine, other):
            return jnp.where(first_my, jnp.concatenate([mine, other], axis=2), jnp.concatenate([other, mine], axis=2))

        both = by_my(local_stack, across_my)
        other_half = by_my(across_vz, diagonal)
        mine_half = both[:layers_own]
        eta = jnp.where(
            first_vz,
            jnp.concatenate([mine_half, other_half], axis=0),
            jnp.concatenate([other_half, mine_half], axis=0),
        )
    else:
        both = gather_axis(local_stack, "my", 2)
        eta = gather_axis(both[:layers_own], "vz", 0)
    planes = both[layers_own:]
    layers = eta.shape[0]
    joined = jnp.concatenate([eta, planes], axis=0)
    zeros_halo = jnp.zeros(joined.shape[:1] + (k,) + joined.shape[2:], joined.dtype)
    joined = exchange_rows(jnp.concatenate([zeros_halo, joined, zeros_halo], axis=1), k, rows, 1)
    eta = joined[:layers]
    act, bed_coef, bv0, bv1, dir_ext = (joined[layers + i] for i in range(5))
    bv = jnp.stack([bv0, bv1])

    c_zm = weight_z * harmonic(eta, shift(eta, 0, -1))
    c_zp = weight_z * harmonic(eta, shift(eta, 0, 1))
    c_xm = harmonic(eta, shift(eta, 1, -1))
    c_xp = harmonic(eta, shift(eta, 1, 1))
    c_ym = harmonic(eta, shift(eta, 2, -1))
    c_yp = harmonic(eta, shift(eta, 2, 1))
    basal = jnp.zeros_like(eta).at[0].set(bed_coef)
    diag = c_zm + c_zp + c_xm + c_xp + c_ym + c_yp + shift_mass * eta + basal
    jacobi = 1.0 / (act * diag + 1.0 - act)

    on = act > 0
    op_stack = jnp.stack(
        [
            act * c_zm,
            act * c_zp,
            act * c_xm * shift(act, 0, -1),
            act * c_ym * shift(act, 1, -1),
            jnp.where(on, diag, 1.0),
            jacobi,
        ]
    )
    table = step_constants()

    def chebyshev(rhs):
        count = lax.axis_size("mx")
        forward = [(i, i + 1) for i in range(count - 1)]
        backward = [(i + 1, i) for i in range(count - 1)]
        state = ()
        since = 1
        start_valid = 1
        run = []
        for keep, push in table:
            if since == k:
                iterate, step_dir, up, down = run_segment(
                    tuple(run), start_valid, k, True, op_stack, rhs, state
                )
                low = lax.ppermute(up, "mx", forward)
                high = lax.ppermute(down, "mx", backward)
                state = (iterate, step_dir, low, high)
                run = []
                start_valid = 0
                since = 0
            run.append((keep, push))
            since += 1
        iterate, step_dir = run_segment(tuple(run), start_valid, k, False, op_stack, rhs, state)
        return (iterate + step_dir)[:, 1 : layers + 1]

    forcing = jnp.zeros((2,) + eta.shape, jnp.float32)
    forcing = forcing.at[:, 0].set(-(bed_coef * dir_ext)[None] * bv)
    forcing = forcing * act
    velocity_ext = chebyshev(forcing)
    column = jnp.sum(velocity_ext, axis=1) / layers
    column = exchange_rows(column, k, rows, 1)
    adjoint_rhs = obs_weight * act * jnp.broadcast_to(column[:, None], velocity_ext.shape)
    adjoint = chebyshev(adjoint_rhs)

    bed_term = bed_coef * jnp.sum(bv * adjoint[:, 0], axis=0)
    lap = (
        4.0 * dir_ext
        - shift(dir_ext, 0, -1)
        - shift(dir_ext, 0, 1)
        - shift(dir_ext, 1, -1)
        - shift(dir_ext, 1, 1)
    )
    hess_ext = -bed_term + reg_weight * lap
    col0 = lax.axis_index("my") * cols_own
    layer0 = lax.axis_index("vz") * layers_own
    hess_action = lax.dynamic_slice(hess_ext, (k, col0), (rows, cols_own))
    velocity_step = lax.dynamic_slice(
        velocity_ext, (0, layer0, k, col0), (2, layers_own, rows, cols_own)
    )
    return (hess_action, velocity_step)


def plain_harmonic(left, right):
    return 2.0 * left * right / (left + right)


def padded(block, sides, width):
    for axis, dim in sides:
        count = lax.axis_size(axis)
        forward = [(i, i + 1) for i in range(count - 1)]
        backward = [(target, source) for source, target in forward]
        low = lax.ppermute(
            lax.slice_in_dim(block, block.shape[dim] - width, None, axis=dim), axis, forward
        )
        high = lax.ppermute(lax.slice_in_dim(block, 0, width, axis=dim), axis, backward)
        block = jnp.concatenate([low, block, high], axis=dim)
    return block


def coefficients(padded_eta):
    core = padded_eta[1:-1, 1:-1, 1:-1]
    coefs = (
        weight_z * plain_harmonic(core, padded_eta[:-2, 1:-1, 1:-1]),
        weight_z * plain_harmonic(core, padded_eta[2:, 1:-1, 1:-1]),
        plain_harmonic(core, padded_eta[1:-1, :-2, 1:-1]),
        plain_harmonic(core, padded_eta[1:-1, 2:, 1:-1]),
        plain_harmonic(core, padded_eta[1:-1, 1:-1, :-2]),
        plain_harmonic(core, padded_eta[1:-1, 1:-1, 2:]),
    )
    return (core, coefs)


def stencil(pad, coefs, diag, masked, act, field):
    beside_all = coefs[0] * pad[:, :-2, 1:-1, 1:-1] + coefs[1] * pad[:, 2:, 1:-1, 1:-1]
    beside_all = beside_all + coefs[2] * pad[:, 1:-1, :-2, 1:-1] + coefs[3] * pad[:, 1:-1, 2:, 1:-1]
    beside_all = beside_all + coefs[4] * pad[:, 1:-1, 1:-1, :-2] + coefs[5] * pad[:, 1:-1, 1:-1, 2:]
    return act * (diag * masked - beside_all) + (1.0 - act) * field


def operate_split(field, coefs, diag, act):
    masked = field * act
    pad = padded(masked, (("mx", 2), ("my", 3), ("vz", 1)), 1)
    return stencil(pad, coefs, diag, masked, act, field)


def chebyshev_split(rhs, operate, jacobi):
    sigma = theta_center / delta_half
    rho = 1.0 / sigma
    keep_list = []
    push_list = []
    for inner in range(STEPS - 1):
        rho_new = 1.0 / (2.0 * sigma - rho)
        keep_list.append(rho_new * rho)
        push_list.append(2.0 * rho_new / delta_half)
        rho = rho_new
    keep_table = jnp.array(keep_list, jnp.float32)
    push_table = jnp.array(push_list, jnp.float32)

    def inner_step(position, state_pair):
        iterate, step_dir = state_pair
        iterate = iterate + step_dir
        resid = rhs - operate(iterate)
        step_dir = keep_table[position] * step_dir + push_table[position] * (jacobi * resid)
        return (iterate, step_dir)

    iterate = jnp.zeros_like(rhs)
    for sweep in range(SWEEPS):
        resid = rhs if sweep == 0 else rhs - operate(iterate)
        step_dir = jacobi * resid / theta_center
        iterate, step_dir = lax.fori_loop(0, STEPS - 1, inner_step, (iterate, step_dir))
        iterate = iterate + step_dir
    return iterate


def local_split(viscosity, friction, base_velocity, grounded, ice_free, direction):
    act = (1 - ice_free).astype(jnp.float32)
    ground = grounded.astype(jnp.float32)
    layer_index = lax.axis_index("vz")
    column_devices = lax.axis_size("vz")
    bed_coef = ground * friction
    padded_eta = padded(viscosity, (("mx", 1), ("my", 2), ("vz", 0)), 1)
    on_bed = jnp.where(layer_index == 0, 1.0, 0.0).astype(jnp.float32)
    core, coefs = coefficients(padded_eta)
    basal = jnp.zeros_like(core).at[0].set(on_bed * bed_coef)
    diag = (
        coefs[0] + coefs[1] + coefs[2] + coefs[3] + coefs[4] + coefs[5] + shift_mass * core + basal
    )
    jacobi = 1.0 / (act * diag + 1.0 - act)
    forcing = jnp.zeros((2,) + core.shape, jnp.float32)
    forcing = forcing.at[:, 0].set(-(on_bed * bed_coef * direction)[None] * base_velocity)
    forcing = forcing * act
    pad_dir = padded(direction, (("mx", 0), ("my", 1)), 1)
    lap = (
        4.0 * direction
        - pad_dir[:-2, 1:-1]
        - pad_dir[2:, 1:-1]
        - pad_dir[1:-1, :-2]
        - pad_dir[1:-1, 2:]
    )

    def operate(field):
        return operate_split(field, coefs, diag, act)

    velocity_step = chebyshev_split(forcing, operate, jacobi)
    column = lax.psum(jnp.sum(velocity_step, axis=1), "vz") / LAYERS
    adjoint_rhs = obs_weight * act * jnp.broadcast_to(column[:, None], velocity_step.shape)
    adjoint = chebyshev_split(adjoint_rhs, operate, jacobi)
    on_top = jnp.where(layer_index == column_devices - 1, 1.0, 0.0).astype(jnp.float32)
    bed_part = on_bed * bed_coef * jnp.sum(base_velocity * adjoint[:, 0], axis=0)
    own_part = on_top * (reg_weight * lap) - bed_part
    hess_action = lax.psum(own_part, "vz")
    return (hess_action, velocity_step)


def solution(mesh):
    return jax.shard_map(
        local,
        mesh=mesh,
        in_specs=(
            P("vz", "mx", "my"),
            P("mx", "my"),
            P(None, "mx", "my"),
            P("mx", "my"),
            P("mx", "my"),
            P("mx", "my"),
        ),
        out_specs=(P("mx", "my"), P(None, "vz", "mx", "my")),
        check_vma=False,
    )
```

```python
import functools

import jax
import jax.numpy as jnp
from jax import lax
from jax.experimental import pallas as pl
from jax.experimental.pallas import tpu as pltpu
from jax.sharding import PartitionSpec as P

LAYERS = 16
STEPS = 16
SWEEPS = 2
HALO = 16

weight_z = 128.0
shift_mass = 0.05
theta_center = 1.05
delta_half = 0.95
obs_weight = 200.0
reg_weight = 0.5


def step_constants():
    sigma = theta_center / delta_half
    table = []
    for sweep in range(SWEEPS):
        rho = 1.0 / sigma
        if sweep > 0:
            table.append((None, 1.0 / theta_center))
        for inner in range(STEPS - 1):
            rho_new = 1.0 / (2.0 * sigma - rho)
            table.append((rho_new * rho, 2.0 * rho_new / delta_half))
            rho = rho_new
    return table


def harmonic(left, right):
    total = left + right
    safe = jnp.where(total > 0, total, 1.0)
    return jnp.where(total > 0, 2.0 * left * right / safe, 0.0)


def exchange_rows(ext, k, rows, axis):
    count = lax.axis_size("mx")
    forward = [(i, i + 1) for i in range(count - 1)]
    backward = [(i + 1, i) for i in range(count - 1)]
    own = lax.slice_in_dim(ext, k, k + rows, axis=axis)
    low = lax.ppermute(lax.slice_in_dim(own, rows - k, rows, axis=axis), "mx", forward)
    high = lax.ppermute(lax.slice_in_dim(own, 0, k, axis=axis), "mx", backward)
    return jnp.concatenate([low, own, high], axis=axis)


def gather_axis(block, axis, dim):
    count = lax.axis_size(axis)
    me = lax.axis_index(axis)
    seq = [block]
    for s in range(1, count):
        pairs = [(j, (j - s) % count) for j in range(count)]
        seq.append(lax.ppermute(block, axis, pairs))
    size = block.shape[dim]
    doubled = jnp.concatenate(seq + seq, axis=dim)
    return lax.dynamic_slice_in_dim(doubled, ((count - me) % count) * size, count * size, axis=dim)


def shift(a, axis, offset):
    n = a.shape[axis]
    zeros_shape = list(a.shape)
    zeros_shape[axis] = 1
    z = jnp.zeros(zeros_shape, a.dtype)
    if offset > 0:
        return jnp.concatenate([lax.slice_in_dim(a, 1, n, axis=axis), z], axis=axis)
    return jnp.concatenate([z, lax.slice_in_dim(a, 0, n - 1, axis=axis)], axis=axis)


def segment_kernel(steps, start_valid, halo, send, table_ref, op_ref, rhs_ref, *refs):
    comps, layers = rhs_ref.shape[0], rhs_ref.shape[1]
    rows, cols = rhs_ref.shape[2], rhs_ref.shape[3]
    own = rows - 2 * halo
    if send:
        refs, up_ref, down_ref = refs[:-2], refs[-2], refs[-1]
    if len(refs) == 6:
        x_in, d_in, low_in, high_in, x_ref, d_ref = refs
        x_ref[...] = x_in[...]
        d_ref[...] = d_in[...]

        def place(layer, carry):
            for c in range(comps):
                for f, ref in enumerate((x_ref, d_ref)):
                    ref[c, layer + 1, pl.ds(0, halo)] = low_in[f, c, layer]
                    ref[c, layer + 1, pl.ds(halo + own, halo)] = high_in[f, c, layer]
            return carry

        lax.fori_loop(0, layers, place, 0)
    else:
        x_ref, d_ref = refs
        zero = jnp.zeros((rows, cols), jnp.float32)
        for c in range(comps):
            x_ref[c, 0] = zero
            d_ref[c, 0] = zero
            x_ref[c, layers + 1] = zero
            d_ref[c, layers + 1] = zero

        def start(layer, carry):
            for c in range(comps):
                x_ref[c, layer + 1] = zero
                d_ref[c, layer + 1] = op_ref[5, layer] * rhs_ref[c, layer] / theta_center
            return carry

        lax.fori_loop(0, layers, start, 0)

    def one_step(lo, keep, push):
        span = pl.ds(lo, rows - 2 * lo)
        height = rows - 2 * lo
        for c in range(comps):
            x_ref[c, 1, span] = x_ref[c, 1, span] + d_ref[c, 1, span]

        def update(c, layer, carry):
            p = layer + 1
            c_xm = op_ref[2, layer, span]
            c_ym = op_ref[3, layer, span]
            c_xp = pltpu.roll(c_xm, height - 1, 0)
            c_yp = pltpu.roll(c_ym, cols - 1, 1)
            if True:
                above = x_ref[c, p + 1, span] + d_ref[c, p + 1, span]
                x_ref[c, p + 1, span] = above
                centre = x_ref[c, p, span]
                beside = op_ref[0, layer, span] * x_ref[c, p - 1, span] + op_ref[1, layer, span] * above
                beside = beside + c_xm * pltpu.roll(centre, 1, 0)
                beside = beside + c_xp * pltpu.roll(centre, height - 1, 0)
                beside = beside + c_ym * pltpu.roll(centre, 1, 1)
                beside = beside + c_yp * pltpu.roll(centre, cols - 1, 1)
                resid = rhs_ref[c, layer, span] - (op_ref[4, layer, span] * centre - beside)
                if keep is None:
                    d_ref[c, p, span] = op_ref[5, layer, span] * resid / theta_center
                else:
                    d_ref[c, p, span] = keep * d_ref[c, p, span] + push * (op_ref[5, layer, span] * resid)
            return carry

        for c in range(comps):
            lax.fori_loop(0, layers, functools.partial(update, c), 0, unroll=True)

    def row_start(j):
        return max(min(8 * ((start_valid + j) // 8), rows // 2 - 8), 0)

    j = 0
    if steps[0][0] is None:
        one_step(row_start(0), None, None)
        j = 1
    while j < len(steps):
        lo = row_start(j)
        end = j
        while end < len(steps) and row_start(end) == lo:
            end += 1

        def body(i, carry, lo=lo):
            one_step(lo, table_ref[0, i], table_ref[1, i])
            return carry

        lax.fori_loop(j, end, body, 0)
        j = end

    if send:
        def pack(layer, carry):
            for c in range(comps):
                for f, ref in enumerate((x_ref, d_ref)):
                    up_ref[f, c, layer] = ref[c, layer + 1, pl.ds(own, halo)]
                    down_ref[f, c, layer] = ref[c, layer + 1, pl.ds(halo, halo)]
            return carry

        lax.fori_loop(0, layers, pack, 0)


def run_segment(steps, start_valid, halo, send, op_stack, rhs, state):
    comps, layers, rows, cols = rhs.shape
    vmem = pl.BlockSpec(memory_space=pltpu.VMEM)
    smem = pl.BlockSpec(memory_space=pltpu.SMEM)
    cells = comps * layers * rows * cols
    table = jnp.array(
        [[0.0 if kp is None else kp for kp, _ in steps], [0.0 if kp is None else ps for kp, ps in steps]],
        jnp.float32,
    )
    padded_shape = jax.ShapeDtypeStruct((comps, layers + 2, rows, cols), jnp.float32)
    slab_shape = jax.ShapeDtypeStruct((2, comps, layers, halo, cols), jnp.float32)
    out_shape = (padded_shape, padded_shape) + ((slab_shape, slab_shape) if send else ())
    return pl.pallas_call(
        lambda *refs: segment_kernel(steps, start_valid, halo, send, *refs),
        out_shape=out_shape,
        in_specs=[smem] + [vmem] * (2 + len(state)),
        out_specs=tuple(vmem for _ in out_shape),
        cost_estimate=pl.CostEstimate(
            flops=20 * cells * len(steps), bytes_accessed=4 * cells * 9, transcendentals=0
        ),
    )(table, op_stack, rhs, *state)


def local(viscosity, friction, base_velocity, grounded, ice_free, direction):
    layers_own, rows, cols_own = viscosity.shape
    if cols_own * lax.axis_size("my") > 256:
        return local_split(viscosity, friction, base_velocity, grounded, ice_free, direction)
    k = min(HALO, rows)
    act = (1 - ice_free).astype(jnp.float32)
    bed_coef = grounded.astype(jnp.float32) * friction
    local_stack = jnp.concatenate(
        [viscosity, act[None], bed_coef[None], base_velocity, direction[None]], axis=0
    )
    if lax.axis_size("vz") == 2 and lax.axis_size("my") == 2:
        swap = [(0, 1), (1, 0)]
        across_my = lax.ppermute(local_stack, "my", swap)
        across_vz = lax.ppermute(viscosity, "vz", swap)
        diagonal = lax.ppermute(viscosity, ("my", "vz"), [(i, 3 - i) for i in range(4)])
        first_my = lax.axis_index("my") == 0
        first_vz = lax.axis_index("vz") == 0

        def by_my(mine, other):
            return jnp.where(first_my, jnp.concatenate([mine, other], axis=2), jnp.concatenate([other, mine], axis=2))

        both = by_my(local_stack, across_my)
        other_half = by_my(across_vz, diagonal)
        mine_half = both[:layers_own]
        eta = jnp.where(
            first_vz,
            jnp.concatenate([mine_half, other_half], axis=0),
            jnp.concatenate([other_half, mine_half], axis=0),
        )
    else:
        both = gather_axis(local_stack, "my", 2)
        eta = gather_axis(both[:layers_own], "vz", 0)
    planes = both[layers_own:]
    layers = eta.shape[0]
    joined = jnp.concatenate([eta, planes], axis=0)
    zeros_halo = jnp.zeros(joined.shape[:1] + (k,) + joined.shape[2:], joined.dtype)
    joined = exchange_rows(jnp.concatenate([zeros_halo, joined, zeros_halo], axis=1), k, rows, 1)
    eta = joined[:layers]
    act, bed_coef, bv0, bv1, dir_ext = (joined[layers + i] for i in range(5))
    bv = jnp.stack([bv0, bv1])

    c_zm = weight_z * harmonic(eta, shift(eta, 0, -1))
    c_zp = weight_z * harmonic(eta, shift(eta, 0, 1))
    c_xm = harmonic(eta, shift(eta, 1, -1))
    c_xp = harmonic(eta, shift(eta, 1, 1))
    c_ym = harmonic(eta, shift(eta, 2, -1))
    c_yp = harmonic(eta, shift(eta, 2, 1))
    basal = jnp.zeros_like(eta).at[0].set(bed_coef)
    diag = c_zm + c_zp + c_xm + c_xp + c_ym + c_yp + shift_mass * eta + basal
    jacobi = 1.0 / (act * diag + 1.0 - act)

    on = act > 0
    op_stack = jnp.stack(
        [
            act * c_zm,
            act * c_zp,
            act * c_xm * shift(act, 0, -1),
            act * c_ym * shift(act, 1, -1),
            jnp.where(on, diag, 1.0),
            jacobi,
        ]
    )
    table = step_constants()

    def chebyshev(rhs):
        count = lax.axis_size("mx")
        forward = [(i, i + 1) for i in range(count - 1)]
        backward = [(i + 1, i) for i in range(count - 1)]
        state = ()
        since = 1
        start_valid = 1
        run = []
        for keep, push in table:
            if since == k:
                iterate, step_dir, up, down = run_segment(
                    tuple(run), start_valid, k, True, op_stack, rhs, state
                )
                low = lax.ppermute(up, "mx", forward)
                high = lax.ppermute(down, "mx", backward)
                state = (iterate, step_dir, low, high)
                run = []
                start_valid = 0
                since = 0
            run.append((keep, push))
            since += 1
        iterate, step_dir = run_segment(tuple(run), start_valid, k, False, op_stack, rhs, state)
        return (iterate + step_dir)[:, 1 : layers + 1]

    forcing = jnp.zeros((2,) + eta.shape, jnp.float32)
    forcing = forcing.at[:, 0].set(-(bed_coef * dir_ext)[None] * bv)
    forcing = forcing * act
    velocity_ext = chebyshev(forcing)
    column = jnp.sum(velocity_ext, axis=1) / layers
    column = exchange_rows(column, k, rows, 1)
    adjoint_rhs = obs_weight * act * jnp.broadcast_to(column[:, None], velocity_ext.shape)
    adjoint = chebyshev(adjoint_rhs)

    bed_term = bed_coef * jnp.sum(bv * adjoint[:, 0], axis=0)
    lap = (
        4.0 * dir_ext
        - shift(dir_ext, 0, -1)
        - shift(dir_ext, 0, 1)
        - shift(dir_ext, 1, -1)
        - shift(dir_ext, 1, 1)
    )
    hess_ext = -bed_term + reg_weight * lap
    col0 = lax.axis_index("my") * cols_own
    layer0 = lax.axis_index("vz") * layers_own
    hess_action = lax.dynamic_slice(hess_ext, (k, col0), (rows, cols_own))
    velocity_step = lax.dynamic_slice(
        velocity_ext, (0, layer0, k, col0), (2, layers_own, rows, cols_own)
    )
    return (hess_action, velocity_step)


def plain_harmonic(left, right):
    return 2.0 * left * right / (left + right)


def padded(block, sides, width):
    for axis, dim in sides:
        count = lax.axis_size(axis)
        forward = [(i, i + 1) for i in range(count - 1)]
        backward = [(target, source) for source, target in forward]
        low = lax.ppermute(
            lax.slice_in_dim(block, block.shape[dim] - width, None, axis=dim), axis, forward
        )
        high = lax.ppermute(lax.slice_in_dim(block, 0, width, axis=dim), axis, backward)
        block = jnp.concatenate([low, block, high], axis=dim)
    return block


def coefficients(padded_eta):
    core = padded_eta[1:-1, 1:-1, 1:-1]
    coefs = (
        weight_z * plain_harmonic(core, padded_eta[:-2, 1:-1, 1:-1]),
        weight_z * plain_harmonic(core, padded_eta[2:, 1:-1, 1:-1]),
        plain_harmonic(core, padded_eta[1:-1, :-2, 1:-1]),
        plain_harmonic(core, padded_eta[1:-1, 2:, 1:-1]),
        plain_harmonic(core, padded_eta[1:-1, 1:-1, :-2]),
        plain_harmonic(core, padded_eta[1:-1, 1:-1, 2:]),
    )
    return (core, coefs)


def stencil(pad, coefs, diag, masked, act, field):
    beside_all = coefs[0] * pad[:, :-2, 1:-1, 1:-1] + coefs[1] * pad[:, 2:, 1:-1, 1:-1]
    beside_all = beside_all + coefs[2] * pad[:, 1:-1, :-2, 1:-1] + coefs[3] * pad[:, 1:-1, 2:, 1:-1]
    beside_all = beside_all + coefs[4] * pad[:, 1:-1, 1:-1, :-2] + coefs[5] * pad[:, 1:-1, 1:-1, 2:]
    return act * (diag * masked - beside_all) + (1.0 - act) * field


def operate_split(field, coefs, diag, act):
    masked = field * act
    pad = padded(masked, (("mx", 2), ("my", 3), ("vz", 1)), 1)
    return stencil(pad, coefs, diag, masked, act, field)


def chebyshev_split(rhs, operate, jacobi):
    sigma = theta_center / delta_half
    rho = 1.0 / sigma
    keep_list = []
    push_list = []
    for inner in range(STEPS - 1):
        rho_new = 1.0 / (2.0 * sigma - rho)
        keep_list.append(rho_new * rho)
        push_list.append(2.0 * rho_new / delta_half)
        rho = rho_new
    keep_table = jnp.array(keep_list, jnp.float32)
    push_table = jnp.array(push_list, jnp.float32)

    def inner_step(position, state_pair):
        iterate, step_dir = state_pair
        iterate = iterate + step_dir
        resid = rhs - operate(iterate)
        step_dir = keep_table[position] * step_dir + push_table[position] * (jacobi * resid)
        return (iterate, step_dir)

    iterate = jnp.zeros_like(rhs)
    for sweep in range(SWEEPS):
        resid = rhs if sweep == 0 else rhs - operate(iterate)
        step_dir = jacobi * resid / theta_center
        iterate, step_dir = lax.fori_loop(0, STEPS - 1, inner_step, (iterate, step_dir))
        iterate = iterate + step_dir
    return iterate


def local_split(viscosity, friction, base_velocity, grounded, ice_free, direction):
    act = (1 - ice_free).astype(jnp.float32)
    ground = grounded.astype(jnp.float32)
    layer_index = lax.axis_index("vz")
    column_devices = lax.axis_size("vz")
    bed_coef = ground * friction
    padded_eta = padded(viscosity, (("mx", 1), ("my", 2), ("vz", 0)), 1)
    on_bed = jnp.where(layer_index == 0, 1.0, 0.0).astype(jnp.float32)
    core, coefs = coefficients(padded_eta)
    basal = jnp.zeros_like(core).at[0].set(on_bed * bed_coef)
    diag = (
        coefs[0] + coefs[1] + coefs[2] + coefs[3] + coefs[4] + coefs[5] + shift_mass * core + basal
    )
    jacobi = 1.0 / (act * diag + 1.0 - act)
    forcing = jnp.zeros((2,) + core.shape, jnp.float32)
    forcing = forcing.at[:, 0].set(-(on_bed * bed_coef * direction)[None] * base_velocity)
    forcing = forcing * act
    pad_dir = padded(direction, (("mx", 0), ("my", 1)), 1)
    lap = (
        4.0 * direction
        - pad_dir[:-2, 1:-1]
        - pad_dir[2:, 1:-1]
        - pad_dir[1:-1, :-2]
        - pad_dir[1:-1, 2:]
    )

    def operate(field):
        return operate_split(field, coefs, diag, act)

    velocity_step = chebyshev_split(forcing, operate, jacobi)
    column = lax.psum(jnp.sum(velocity_step, axis=1), "vz") / LAYERS
    adjoint_rhs = obs_weight * act * jnp.broadcast_to(column[:, None], velocity_step.shape)
    adjoint = chebyshev_split(adjoint_rhs, operate, jacobi)
    on_top = jnp.where(layer_index == column_devices - 1, 1.0, 0.0).astype(jnp.float32)
    bed_part = on_bed * bed_coef * jnp.sum(base_velocity * adjoint[:, 0], axis=0)
    own_part = on_top * (reg_weight * lap) - bed_part
    hess_action = lax.psum(own_part, "vz")
    return (hess_action, velocity_step)


def solution(mesh):
    return jax.shard_map(
        local,
        mesh=mesh,
        in_specs=(
            P("vz", "mx", "my"),
            P("mx", "my"),
            P(None, "mx", "my"),
            P("mx", "my"),
            P("mx", "my"),
            P("mx", "my"),
        ),
        out_specs=(P("mx", "my"), P(None, "vz", "mx", "my")),
        check_vma=False,
    )
```

```python
import jax
import jax.numpy as jnp
from jax import lax
from jax.experimental import pallas as pl
from jax.experimental.pallas import tpu as pltpu
from jax.sharding import PartitionSpec as P

LAYERS = 16
STEPS = 16
SWEEPS = 2
HALO = 16

weight_z = 128.0
shift_mass = 0.05
theta_center = 1.05
delta_half = 0.95
obs_weight = 200.0
reg_weight = 0.5


def step_constants():
    sigma = theta_center / delta_half
    table = []
    for sweep in range(SWEEPS):
        rho = 1.0 / sigma
        if sweep > 0:
            table.append((None, 1.0 / theta_center))
        for inner in range(STEPS - 1):
            rho_new = 1.0 / (2.0 * sigma - rho)
            table.append((rho_new * rho, 2.0 * rho_new / delta_half))
            rho = rho_new
    return table


def harmonic(left, right):
    total = left + right
    safe = jnp.where(total > 0, total, 1.0)
    return jnp.where(total > 0, 2.0 * left * right / safe, 0.0)


def exchange_rows(ext, k, rows, axis):
    count = lax.axis_size("mx")
    forward = [(i, i + 1) for i in range(count - 1)]
    backward = [(i + 1, i) for i in range(count - 1)]
    own = lax.slice_in_dim(ext, k, k + rows, axis=axis)
    low = lax.ppermute(lax.slice_in_dim(own, rows - k, rows, axis=axis), "mx", forward)
    high = lax.ppermute(lax.slice_in_dim(own, 0, k, axis=axis), "mx", backward)
    return jnp.concatenate([low, own, high], axis=axis)


def gather_axis(block, axis, dim):
    count = lax.axis_size(axis)
    me = lax.axis_index(axis)
    seq = [block]
    for s in range(1, count):
        pairs = [(j, (j - s) % count) for j in range(count)]
        seq.append(lax.ppermute(block, axis, pairs))
    size = block.shape[dim]
    doubled = jnp.concatenate(seq + seq, axis=dim)
    return lax.dynamic_slice_in_dim(doubled, ((count - me) % count) * size, count * size, axis=dim)


def shift(a, axis, offset):
    n = a.shape[axis]
    zeros_shape = list(a.shape)
    zeros_shape[axis] = 1
    z = jnp.zeros(zeros_shape, a.dtype)
    if offset > 0:
        return jnp.concatenate([lax.slice_in_dim(a, 1, n, axis=axis), z], axis=axis)
    return jnp.concatenate([z, lax.slice_in_dim(a, 0, n - 1, axis=axis)], axis=axis)


def segment_kernel(steps, start_valid, halo, send, table_ref, op_ref, rhs_ref, *refs):
    comps, layers = rhs_ref.shape[0], rhs_ref.shape[1]
    rows, cols = rhs_ref.shape[2], rhs_ref.shape[3]
    own = rows - 2 * halo
    if send:
        refs, up_ref, down_ref = refs[:-2], refs[-2], refs[-1]
    if len(refs) == 6:
        x_in, d_in, low_in, high_in, x_ref, d_ref = refs
        x_ref[...] = x_in[...]
        d_ref[...] = d_in[...]

        def place(layer, carry):
            for c in range(comps):
                for f, ref in enumerate((x_ref, d_ref)):
                    ref[c, layer + 1, pl.ds(0, halo)] = low_in[f, c, layer]
                    ref[c, layer + 1, pl.ds(halo + own, halo)] = high_in[f, c, layer]
            return carry

        lax.fori_loop(0, layers, place, 0)
    else:
        x_ref, d_ref = refs
        zero = jnp.zeros((rows, cols), jnp.float32)
        for c in range(comps):
            x_ref[c, 0] = zero
            d_ref[c, 0] = zero
            x_ref[c, layers + 1] = zero
            d_ref[c, layers + 1] = zero

        def start(layer, carry):
            for c in range(comps):
                x_ref[c, layer + 1] = zero
                d_ref[c, layer + 1] = op_ref[5, layer] * rhs_ref[c, layer] / theta_center
            return carry

        lax.fori_loop(0, layers, start, 0)

    def one_step(lo, keep, push):
        span = pl.ds(lo, rows - 2 * lo)
        height = rows - 2 * lo
        for c in range(comps):
            x_ref[c, 1, span] = x_ref[c, 1, span] + d_ref[c, 1, span]

        def update(layer, carry):
            p = layer + 1
            c_xm = op_ref[2, layer, span]
            c_ym = op_ref[3, layer, span]
            c_xp = op_ref[6, layer, span]
            c_yp = op_ref[7, layer, span]
            for c in range(comps):
                above = x_ref[c, p + 1, span] + d_ref[c, p + 1, span]
                x_ref[c, p + 1, span] = above
                centre = x_ref[c, p, span]
                beside = op_ref[0, layer, span] * x_ref[c, p - 1, span] + op_ref[1, layer, span] * above
                beside = beside + c_xm * pltpu.roll(centre, 1, 0)
                beside = beside + c_xp * pltpu.roll(centre, height - 1, 0)
                beside = beside + c_ym * pltpu.roll(centre, 1, 1)
                beside = beside + c_yp * pltpu.roll(centre, cols - 1, 1)
                resid = rhs_ref[c, layer, span] - (op_ref[4, layer, span] * centre - beside)
                if keep is None:
                    d_ref[c, p, span] = op_ref[5, layer, span] * resid / theta_center
                else:
                    d_ref[c, p, span] = keep * d_ref[c, p, span] + push * (op_ref[5, layer, span] * resid)
            return carry

        lax.fori_loop(0, layers, update, 0, unroll=True)

    def row_start(j):
        return max(min(8 * ((start_valid + j) // 8), rows // 2 - 8), 0)

    j = 0
    if steps[0][0] is None:
        one_step(row_start(0), None, None)
        j = 1
    while j < len(steps):
        lo = row_start(j)
        end = j
        while end < len(steps) and row_start(end) == lo:
            end += 1

        def body(i, carry, lo=lo):
            one_step(lo, table_ref[0, i], table_ref[1, i])
            return carry

        lax.fori_loop(j, end, body, 0)
        j = end

    if send:
        def pack(layer, carry):
            for c in range(comps):
                for f, ref in enumerate((x_ref, d_ref)):
                    up_ref[f, c, layer] = ref[c, layer + 1, pl.ds(own, halo)]
                    down_ref[f, c, layer] = ref[c, layer + 1, pl.ds(halo, halo)]
            return carry

        lax.fori_loop(0, layers, pack, 0)


def run_segment(steps, start_valid, halo, send, op_stack, rhs, state):
    comps, layers, rows, cols = rhs.shape
    vmem = pl.BlockSpec(memory_space=pltpu.VMEM)
    smem = pl.BlockSpec(memory_space=pltpu.SMEM)
    cells = comps * layers * rows * cols
    table = jnp.array(
        [[0.0 if kp is None else kp for kp, _ in steps], [0.0 if kp is None else ps for kp, ps in steps]],
        jnp.float32,
    )
    padded_shape = jax.ShapeDtypeStruct((comps, layers + 2, rows, cols), jnp.float32)
    slab_shape = jax.ShapeDtypeStruct((2, comps, layers, halo, cols), jnp.float32)
    out_shape = (padded_shape, padded_shape) + ((slab_shape, slab_shape) if send else ())
    return pl.pallas_call(
        lambda *refs: segment_kernel(steps, start_valid, halo, send, *refs),
        out_shape=out_shape,
        in_specs=[smem] + [vmem] * (2 + len(state)),
        out_specs=tuple(vmem for _ in out_shape),
        cost_estimate=pl.CostEstimate(
            flops=20 * cells * len(steps), bytes_accessed=4 * cells * 9, transcendentals=0
        ),
    )(table, op_stack, rhs, *state)


def local(viscosity, friction, base_velocity, grounded, ice_free, direction):
    layers_own, rows, cols_own = viscosity.shape
    if cols_own * lax.axis_size("my") > 256:
        return local_split(viscosity, friction, base_velocity, grounded, ice_free, direction)
    k = min(HALO, rows)
    act = (1 - ice_free).astype(jnp.float32)
    bed_coef = grounded.astype(jnp.float32) * friction
    local_stack = jnp.concatenate(
        [viscosity, act[None], bed_coef[None], base_velocity, direction[None]], axis=0
    )
    if lax.axis_size("vz") == 2 and lax.axis_size("my") == 2:
        swap = [(0, 1), (1, 0)]
        across_my = lax.ppermute(local_stack, "my", swap)
        across_vz = lax.ppermute(viscosity, "vz", swap)
        diagonal = lax.ppermute(viscosity, ("my", "vz"), [(i, 3 - i) for i in range(4)])
        first_my = lax.axis_index("my") == 0
        first_vz = lax.axis_index("vz") == 0

        def by_my(mine, other):
            return jnp.where(first_my, jnp.concatenate([mine, other], axis=2), jnp.concatenate([other, mine], axis=2))

        both = by_my(local_stack, across_my)
        other_half = by_my(across_vz, diagonal)
        mine_half = both[:layers_own]
        eta = jnp.where(
            first_vz,
            jnp.concatenate([mine_half, other_half], axis=0),
            jnp.concatenate([other_half, mine_half], axis=0),
        )
    else:
        both = gather_axis(local_stack, "my", 2)
        eta = gather_axis(both[:layers_own], "vz", 0)
    planes = both[layers_own:]
    layers = eta.shape[0]
    joined = jnp.concatenate([eta, planes], axis=0)
    zeros_halo = jnp.zeros(joined.shape[:1] + (k,) + joined.shape[2:], joined.dtype)
    joined = exchange_rows(jnp.concatenate([zeros_halo, joined, zeros_halo], axis=1), k, rows, 1)
    eta = joined[:layers]
    act, bed_coef, bv0, bv1, dir_ext = (joined[layers + i] for i in range(5))
    bv = jnp.stack([bv0, bv1])

    c_zm = weight_z * harmonic(eta, shift(eta, 0, -1))
    c_zp = weight_z * harmonic(eta, shift(eta, 0, 1))
    c_xm = harmonic(eta, shift(eta, 1, -1))
    c_xp = harmonic(eta, shift(eta, 1, 1))
    c_ym = harmonic(eta, shift(eta, 2, -1))
    c_yp = harmonic(eta, shift(eta, 2, 1))
    basal = jnp.zeros_like(eta).at[0].set(bed_coef)
    diag = c_zm + c_zp + c_xm + c_xp + c_ym + c_yp + shift_mass * eta + basal
    jacobi = 1.0 / (act * diag + 1.0 - act)

    on = act > 0
    op_stack = jnp.stack(
        [
            act * c_zm,
            act * c_zp,
            act * c_xm * shift(act, 0, -1),
            act * c_ym * shift(act, 1, -1),
            jnp.where(on, diag, 1.0),
            jacobi,
            act * c_xp * shift(act, 0, 1),
            act * c_yp * shift(act, 1, 1),
        ]
    )
    table = step_constants()

    def chebyshev(rhs):
        count = lax.axis_size("mx")
        forward = [(i, i + 1) for i in range(count - 1)]
        backward = [(i + 1, i) for i in range(count - 1)]
        state = ()
        since = 1
        start_valid = 1
        run = []
        for keep, push in table:
            if since == k:
                iterate, step_dir, up, down = run_segment(
                    tuple(run), start_valid, k, True, op_stack, rhs, state
                )
                low = lax.ppermute(up, "mx", forward)
                high = lax.ppermute(down, "mx", backward)
                state = (iterate, step_dir, low, high)
                run = []
                start_valid = 0
                since = 0
            run.append((keep, push))
            since += 1
        iterate, step_dir = run_segment(tuple(run), start_valid, k, False, op_stack, rhs, state)
        return (iterate + step_dir)[:, 1 : layers + 1]

    forcing = jnp.zeros((2,) + eta.shape, jnp.float32)
    forcing = forcing.at[:, 0].set(-(bed_coef * dir_ext)[None] * bv)
    forcing = forcing * act
    velocity_ext = chebyshev(forcing)
    column = jnp.sum(velocity_ext, axis=1) / layers
    column = exchange_rows(column, k, rows, 1)
    adjoint_rhs = obs_weight * act * jnp.broadcast_to(column[:, None], velocity_ext.shape)
    adjoint = chebyshev(adjoint_rhs)

    bed_term = bed_coef * jnp.sum(bv * adjoint[:, 0], axis=0)
    lap = (
        4.0 * dir_ext
        - shift(dir_ext, 0, -1)
        - shift(dir_ext, 0, 1)
        - shift(dir_ext, 1, -1)
        - shift(dir_ext, 1, 1)
    )
    hess_ext = -bed_term + reg_weight * lap
    col0 = lax.axis_index("my") * cols_own
    layer0 = lax.axis_index("vz") * layers_own
    hess_action = lax.dynamic_slice(hess_ext, (k, col0), (rows, cols_own))
    velocity_step = lax.dynamic_slice(
        velocity_ext, (0, layer0, k, col0), (2, layers_own, rows, cols_own)
    )
    return (hess_action, velocity_step)


def plain_harmonic(left, right):
    return 2.0 * left * right / (left + right)


def padded(block, sides, width):
    for axis, dim in sides:
        count = lax.axis_size(axis)
        forward = [(i, i + 1) for i in range(count - 1)]
        backward = [(target, source) for source, target in forward]
        low = lax.ppermute(
            lax.slice_in_dim(block, block.shape[dim] - width, None, axis=dim), axis, forward
        )
        high = lax.ppermute(lax.slice_in_dim(block, 0, width, axis=dim), axis, backward)
        block = jnp.concatenate([low, block, high], axis=dim)
    return block


def coefficients(padded_eta):
    core = padded_eta[1:-1, 1:-1, 1:-1]
    coefs = (
        weight_z * plain_harmonic(core, padded_eta[:-2, 1:-1, 1:-1]),
        weight_z * plain_harmonic(core, padded_eta[2:, 1:-1, 1:-1]),
        plain_harmonic(core, padded_eta[1:-1, :-2, 1:-1]),
        plain_harmonic(core, padded_eta[1:-1, 2:, 1:-1]),
        plain_harmonic(core, padded_eta[1:-1, 1:-1, :-2]),
        plain_harmonic(core, padded_eta[1:-1, 1:-1, 2:]),
    )
    return (core, coefs)


def stencil(pad, coefs, diag, masked, act, field):
    beside_all = coefs[0] * pad[:, :-2, 1:-1, 1:-1] + coefs[1] * pad[:, 2:, 1:-1, 1:-1]
    beside_all = beside_all + coefs[2] * pad[:, 1:-1, :-2, 1:-1] + coefs[3] * pad[:, 1:-1, 2:, 1:-1]
    beside_all = beside_all + coefs[4] * pad[:, 1:-1, 1:-1, :-2] + coefs[5] * pad[:, 1:-1, 1:-1, 2:]
    return act * (diag * masked - beside_all) + (1.0 - act) * field


def operate_split(field, coefs, diag, act):
    masked = field * act
    pad = padded(masked, (("mx", 2), ("my", 3), ("vz", 1)), 1)
    return stencil(pad, coefs, diag, masked, act, field)


def chebyshev_split(rhs, operate, jacobi):
    sigma = theta_center / delta_half
    rho = 1.0 / sigma
    keep_list = []
    push_list = []
    for inner in range(STEPS - 1):
        rho_new = 1.0 / (2.0 * sigma - rho)
        keep_list.append(rho_new * rho)
        push_list.append(2.0 * rho_new / delta_half)
        rho = rho_new
    keep_table = jnp.array(keep_list, jnp.float32)
    push_table = jnp.array(push_list, jnp.float32)

    def inner_step(position, state_pair):
        iterate, step_dir = state_pair
        iterate = iterate + step_dir
        resid = rhs - operate(iterate)
        step_dir = keep_table[position] * step_dir + push_table[position] * (jacobi * resid)
        return (iterate, step_dir)

    iterate = jnp.zeros_like(rhs)
    for sweep in range(SWEEPS):
        resid = rhs if sweep == 0 else rhs - operate(iterate)
        step_dir = jacobi * resid / theta_center
        iterate, step_dir = lax.fori_loop(0, STEPS - 1, inner_step, (iterate, step_dir))
        iterate = iterate + step_dir
    return iterate


def local_split(viscosity, friction, base_velocity, grounded, ice_free, direction):
    act = (1 - ice_free).astype(jnp.float32)
    ground = grounded.astype(jnp.float32)
    layer_index = lax.axis_index("vz")
    column_devices = lax.axis_size("vz")
    bed_coef = ground * friction
    padded_eta = padded(viscosity, (("mx", 1), ("my", 2), ("vz", 0)), 1)
    on_bed = jnp.where(layer_index == 0, 1.0, 0.0).astype(jnp.float32)
    core, coefs = coefficients(padded_eta)
    basal = jnp.zeros_like(core).at[0].set(on_bed * bed_coef)
    diag = (
        coefs[0] + coefs[1] + coefs[2] + coefs[3] + coefs[4] + coefs[5] + shift_mass * core + basal
    )
    jacobi = 1.0 / (act * diag + 1.0 - act)
    forcing = jnp.zeros((2,) + core.shape, jnp.float32)
    forcing = forcing.at[:, 0].set(-(on_bed * bed_coef * direction)[None] * base_velocity)
    forcing = forcing * act
    pad_dir = padded(direction, (("mx", 0), ("my", 1)), 1)
    lap = (
        4.0 * direction
        - pad_dir[:-2, 1:-1]
        - pad_dir[2:, 1:-1]
        - pad_dir[1:-1, :-2]
        - pad_dir[1:-1, 2:]
    )

    def operate(field):
        return operate_split(field, coefs, diag, act)

    velocity_step = chebyshev_split(forcing, operate, jacobi)
    column = lax.psum(jnp.sum(velocity_step, axis=1), "vz") / LAYERS
    adjoint_rhs = obs_weight * act * jnp.broadcast_to(column[:, None], velocity_step.shape)
    adjoint = chebyshev_split(adjoint_rhs, operate, jacobi)
    on_top = jnp.where(layer_index == column_devices - 1, 1.0, 0.0).astype(jnp.float32)
    bed_part = on_bed * bed_coef * jnp.sum(base_velocity * adjoint[:, 0], axis=0)
    own_part = on_top * (reg_weight * lap) - bed_part
    hess_action = lax.psum(own_part, "vz")
    return (hess_action, velocity_step)


def solution(mesh):
    return jax.shard_map(
        local,
        mesh=mesh,
        in_specs=(
            P("vz", "mx", "my"),
            P("mx", "my"),
            P(None, "mx", "my"),
            P("mx", "my"),
            P("mx", "my"),
            P("mx", "my"),
        ),
        out_specs=(P("mx", "my"), P(None, "vz", "mx", "my")),
        check_vma=False,
    )
```

```python
import jax
import jax.numpy as jnp
from jax import lax
from jax.experimental import pallas as pl
from jax.experimental.pallas import tpu as pltpu
from jax.sharding import PartitionSpec as P

LAYERS = 16
STEPS = 16
SWEEPS = 2
HALO = 16

weight_z = 128.0
shift_mass = 0.05
theta_center = 1.05
delta_half = 0.95
obs_weight = 200.0
reg_weight = 0.5


def step_constants():
    sigma = theta_center / delta_half
    table = []
    for sweep in range(SWEEPS):
        rho = 1.0 / sigma
        if sweep > 0:
            table.append((None, 1.0 / theta_center))
        for inner in range(STEPS - 1):
            rho_new = 1.0 / (2.0 * sigma - rho)
            table.append((rho_new * rho, 2.0 * rho_new / delta_half))
            rho = rho_new
    return table


def harmonic(left, right):
    total = left + right
    safe = jnp.where(total > 0, total, 1.0)
    return jnp.where(total > 0, 2.0 * left * right / safe, 0.0)


def exchange_rows(ext, k, rows, axis):
    count = lax.axis_size("mx")
    forward = [(i, i + 1) for i in range(count - 1)]
    backward = [(i + 1, i) for i in range(count - 1)]
    own = lax.slice_in_dim(ext, k, k + rows, axis=axis)
    low = lax.ppermute(lax.slice_in_dim(own, rows - k, rows, axis=axis), "mx", forward)
    high = lax.ppermute(lax.slice_in_dim(own, 0, k, axis=axis), "mx", backward)
    return jnp.concatenate([low, own, high], axis=axis)


def gather_axis(block, axis, dim):
    count = lax.axis_size(axis)
    me = lax.axis_index(axis)
    seq = [block]
    for s in range(1, count):
        pairs = [(j, (j - s) % count) for j in range(count)]
        seq.append(lax.ppermute(block, axis, pairs))
    size = block.shape[dim]
    doubled = jnp.concatenate(seq + seq, axis=dim)
    return lax.dynamic_slice_in_dim(doubled, ((count - me) % count) * size, count * size, axis=dim)


def shift(a, axis, offset):
    n = a.shape[axis]
    zeros_shape = list(a.shape)
    zeros_shape[axis] = 1
    z = jnp.zeros(zeros_shape, a.dtype)
    if offset > 0:
        return jnp.concatenate([lax.slice_in_dim(a, 1, n, axis=axis), z], axis=axis)
    return jnp.concatenate([z, lax.slice_in_dim(a, 0, n - 1, axis=axis)], axis=axis)


def segment_kernel(steps, start_valid, halo, send, table_ref, op_ref, rhs_ref, *refs):
    comps, layers = rhs_ref.shape[0], rhs_ref.shape[1]
    rows, cols = rhs_ref.shape[2], rhs_ref.shape[3]
    own = rows - 2 * halo
    if send:
        refs, up_ref, down_ref = refs[:-2], refs[-2], refs[-1]
    if len(refs) == 6:
        x_in, d_in, low_in, high_in, x_ref, d_ref = refs
        x_ref[...] = x_in[...]
        d_ref[...] = d_in[...]

        def place(layer, carry):
            for c in range(comps):
                for f, ref in enumerate((x_ref, d_ref)):
                    ref[c, layer + 1, pl.ds(0, halo)] = low_in[f, c, layer]
                    ref[c, layer + 1, pl.ds(halo + own, halo)] = high_in[f, c, layer]
            return carry

        lax.fori_loop(0, layers, place, 0, unroll=True)
    else:
        x_ref, d_ref = refs
        zero = jnp.zeros((rows, cols), jnp.float32)
        for c in range(comps):
            x_ref[c, 0] = zero
            d_ref[c, 0] = zero
            x_ref[c, layers + 1] = zero
            d_ref[c, layers + 1] = zero

        def start(layer, carry):
            for c in range(comps):
                x_ref[c, layer + 1] = zero
                d_ref[c, layer + 1] = op_ref[5, layer] * rhs_ref[c, layer] / theta_center
            return carry

        lax.fori_loop(0, layers, start, 0, unroll=True)

    def one_step(lo, keep, push):
        span = pl.ds(lo, rows - 2 * lo)
        height = rows - 2 * lo
        for c in range(comps):
            x_ref[c, 1, span] = x_ref[c, 1, span] + d_ref[c, 1, span]

        def update(layer, carry):
            p = layer + 1
            c_xm = op_ref[2, layer, span]
            c_ym = op_ref[3, layer, span]
            c_xp = op_ref[6, layer, span]
            c_yp = op_ref[7, layer, span]
            for c in range(comps):
                above = x_ref[c, p + 1, span] + d_ref[c, p + 1, span]
                x_ref[c, p + 1, span] = above
                centre = x_ref[c, p, span]
                beside = op_ref[0, layer, span] * x_ref[c, p - 1, span] + op_ref[1, layer, span] * above
                beside = beside + c_xm * pltpu.roll(centre, 1, 0)
                beside = beside + c_xp * pltpu.roll(centre, height - 1, 0)
                beside = beside + c_ym * pltpu.roll(centre, 1, 1)
                beside = beside + c_yp * pltpu.roll(centre, cols - 1, 1)
                resid = rhs_ref[c, layer, span] - (op_ref[4, layer, span] * centre - beside)
                if keep is None:
                    d_ref[c, p, span] = op_ref[5, layer, span] * resid / theta_center
                else:
                    d_ref[c, p, span] = keep * d_ref[c, p, span] + push * (op_ref[5, layer, span] * resid)
            return carry

        lax.fori_loop(0, layers, update, 0, unroll=True)

    def row_start(j):
        return max(min(8 * ((start_valid + j) // 8), rows // 2 - 8), 0)

    j = 0
    if steps[0][0] is None:
        one_step(row_start(0), None, None)
        j = 1
    while j < len(steps):
        lo = row_start(j)
        end = j
        while end < len(steps) and row_start(end) == lo:
            end += 1

        def body(i, carry, lo=lo):
            one_step(lo, table_ref[0, i], table_ref[1, i])
            return carry

        lax.fori_loop(j, end, body, 0)
        j = end

    if send:
        def pack(layer, carry):
            for c in range(comps):
                for f, ref in enumerate((x_ref, d_ref)):
                    up_ref[f, c, layer] = ref[c, layer + 1, pl.ds(own, halo)]
                    down_ref[f, c, layer] = ref[c, layer + 1, pl.ds(halo, halo)]
            return carry

        lax.fori_loop(0, layers, pack, 0, unroll=True)


def run_segment(steps, start_valid, halo, send, op_stack, rhs, state):
    comps, layers, rows, cols = rhs.shape
    vmem = pl.BlockSpec(memory_space=pltpu.VMEM)
    smem = pl.BlockSpec(memory_space=pltpu.SMEM)
    cells = comps * layers * rows * cols
    table = jnp.array(
        [[0.0 if kp is None else kp for kp, _ in steps], [0.0 if kp is None else ps for kp, ps in steps]],
        jnp.float32,
    )
    padded_shape = jax.ShapeDtypeStruct((comps, layers + 2, rows, cols), jnp.float32)
    slab_shape = jax.ShapeDtypeStruct((2, comps, layers, halo, cols), jnp.float32)
    out_shape = (padded_shape, padded_shape) + ((slab_shape, slab_shape) if send else ())
    return pl.pallas_call(
        lambda *refs: segment_kernel(steps, start_valid, halo, send, *refs),
        out_shape=out_shape,
        in_specs=[smem] + [vmem] * (2 + len(state)),
        out_specs=tuple(vmem for _ in out_shape),
        cost_estimate=pl.CostEstimate(
            flops=20 * cells * len(steps), bytes_accessed=4 * cells * 9, transcendentals=0
        ),
    )(table, op_stack, rhs, *state)


def local(viscosity, friction, base_velocity, grounded, ice_free, direction):
    layers_own, rows, cols_own = viscosity.shape
    if cols_own * lax.axis_size("my") > 256:
        return local_split(viscosity, friction, base_velocity, grounded, ice_free, direction)
    k = min(HALO, rows)
    act = (1 - ice_free).astype(jnp.float32)
    bed_coef = grounded.astype(jnp.float32) * friction
    local_stack = jnp.concatenate(
        [viscosity, act[None], bed_coef[None], base_velocity, direction[None]], axis=0
    )
    if lax.axis_size("vz") == 2 and lax.axis_size("my") == 2:
        swap = [(0, 1), (1, 0)]
        across_my = lax.ppermute(local_stack, "my", swap)
        across_vz = lax.ppermute(viscosity, "vz", swap)
        diagonal = lax.ppermute(viscosity, ("my", "vz"), [(i, 3 - i) for i in range(4)])
        first_my = lax.axis_index("my") == 0
        first_vz = lax.axis_index("vz") == 0

        def by_my(mine, other):
            return jnp.where(first_my, jnp.concatenate([mine, other], axis=2), jnp.concatenate([other, mine], axis=2))

        both = by_my(local_stack, across_my)
        other_half = by_my(across_vz, diagonal)
        mine_half = both[:layers_own]
        eta = jnp.where(
            first_vz,
            jnp.concatenate([mine_half, other_half], axis=0),
            jnp.concatenate([other_half, mine_half], axis=0),
        )
    else:
        both = gather_axis(local_stack, "my", 2)
        eta = gather_axis(both[:layers_own], "vz", 0)
    planes = both[layers_own:]
    layers = eta.shape[0]
    joined = jnp.concatenate([eta, planes], axis=0)
    zeros_halo = jnp.zeros(joined.shape[:1] + (k,) + joined.shape[2:], joined.dtype)
    joined = exchange_rows(jnp.concatenate([zeros_halo, joined, zeros_halo], axis=1), k, rows, 1)
    eta = joined[:layers]
    act, bed_coef, bv0, bv1, dir_ext = (joined[layers + i] for i in range(5))
    bv = jnp.stack([bv0, bv1])

    c_zm = weight_z * harmonic(eta, shift(eta, 0, -1))
    c_zp = weight_z * harmonic(eta, shift(eta, 0, 1))
    c_xm = harmonic(eta, shift(eta, 1, -1))
    c_xp = harmonic(eta, shift(eta, 1, 1))
    c_ym = harmonic(eta, shift(eta, 2, -1))
    c_yp = harmonic(eta, shift(eta, 2, 1))
    basal = jnp.zeros_like(eta).at[0].set(bed_coef)
    diag = c_zm + c_zp + c_xm + c_xp + c_ym + c_yp + shift_mass * eta + basal
    jacobi = 1.0 / (act * diag + 1.0 - act)

    on = act > 0
    op_stack = jnp.stack(
        [
            act * c_zm,
            act * c_zp,
            act * c_xm * shift(act, 0, -1),
            act * c_ym * shift(act, 1, -1),
            jnp.where(on, diag, 1.0),
            jacobi,
            act * c_xp * shift(act, 0, 1),
            act * c_yp * shift(act, 1, 1),
        ]
    )
    table = step_constants()

    def chebyshev(rhs):
        count = lax.axis_size("mx")
        forward = [(i, i + 1) for i in range(count - 1)]
        backward = [(i + 1, i) for i in range(count - 1)]
        state = ()
        since = 1
        start_valid = 1
        run = []
        for keep, push in table:
            if since == k:
                iterate, step_dir, up, down = run_segment(
                    tuple(run), start_valid, k, True, op_stack, rhs, state
                )
                low = lax.ppermute(up, "mx", forward)
                high = lax.ppermute(down, "mx", backward)
                state = (iterate, step_dir, low, high)
                run = []
                start_valid = 0
                since = 0
            run.append((keep, push))
            since += 1
        iterate, step_dir = run_segment(tuple(run), start_valid, k, False, op_stack, rhs, state)
        return (iterate + step_dir)[:, 1 : layers + 1]

    forcing = jnp.zeros((2,) + eta.shape, jnp.float32)
    forcing = forcing.at[:, 0].set(-(bed_coef * dir_ext)[None] * bv)
    forcing = forcing * act
    velocity_ext = chebyshev(forcing)
    column = jnp.sum(velocity_ext, axis=1) / layers
    column = exchange_rows(column, k, rows, 1)
    adjoint_rhs = obs_weight * act * jnp.broadcast_to(column[:, None], velocity_ext.shape)
    adjoint = chebyshev(adjoint_rhs)

    bed_term = bed_coef * jnp.sum(bv * adjoint[:, 0], axis=0)
    lap = (
        4.0 * dir_ext
        - shift(dir_ext, 0, -1)
        - shift(dir_ext, 0, 1)
        - shift(dir_ext, 1, -1)
        - shift(dir_ext, 1, 1)
    )
    hess_ext = -bed_term + reg_weight * lap
    col0 = lax.axis_index("my") * cols_own
    layer0 = lax.axis_index("vz") * layers_own
    hess_action = lax.dynamic_slice(hess_ext, (k, col0), (rows, cols_own))
    velocity_step = lax.dynamic_slice(
        velocity_ext, (0, layer0, k, col0), (2, layers_own, rows, cols_own)
    )
    return (hess_action, velocity_step)


def plain_harmonic(left, right):
    return 2.0 * left * right / (left + right)


def padded(block, sides, width):
    for axis, dim in sides:
        count = lax.axis_size(axis)
        forward = [(i, i + 1) for i in range(count - 1)]
        backward = [(target, source) for source, target in forward]
        low = lax.ppermute(
            lax.slice_in_dim(block, block.shape[dim] - width, None, axis=dim), axis, forward
        )
        high = lax.ppermute(lax.slice_in_dim(block, 0, width, axis=dim), axis, backward)
        block = jnp.concatenate([low, block, high], axis=dim)
    return block


def coefficients(padded_eta):
    core = padded_eta[1:-1, 1:-1, 1:-1]
    coefs = (
        weight_z * plain_harmonic(core, padded_eta[:-2, 1:-1, 1:-1]),
        weight_z * plain_harmonic(core, padded_eta[2:, 1:-1, 1:-1]),
        plain_harmonic(core, padded_eta[1:-1, :-2, 1:-1]),
        plain_harmonic(core, padded_eta[1:-1, 2:, 1:-1]),
        plain_harmonic(core, padded_eta[1:-1, 1:-1, :-2]),
        plain_harmonic(core, padded_eta[1:-1, 1:-1, 2:]),
    )
    return (core, coefs)


def stencil(pad, coefs, diag, masked, act, field):
    beside_all = coefs[0] * pad[:, :-2, 1:-1, 1:-1] + coefs[1] * pad[:, 2:, 1:-1, 1:-1]
    beside_all = beside_all + coefs[2] * pad[:, 1:-1, :-2, 1:-1] + coefs[3] * pad[:, 1:-1, 2:, 1:-1]
    beside_all = beside_all + coefs[4] * pad[:, 1:-1, 1:-1, :-2] + coefs[5] * pad[:, 1:-1, 1:-1, 2:]
    return act * (diag * masked - beside_all) + (1.0 - act) * field


def operate_split(field, coefs, diag, act):
    masked = field * act
    pad = padded(masked, (("mx", 2), ("my", 3), ("vz", 1)), 1)
    return stencil(pad, coefs, diag, masked, act, field)


def chebyshev_split(rhs, operate, jacobi):
    sigma = theta_center / delta_half
    rho = 1.0 / sigma
    keep_list = []
    push_list = []
    for inner in range(STEPS - 1):
        rho_new = 1.0 / (2.0 * sigma - rho)
        keep_list.append(rho_new * rho)
        push_list.append(2.0 * rho_new / delta_half)
        rho = rho_new
    keep_table = jnp.array(keep_list, jnp.float32)
    push_table = jnp.array(push_list, jnp.float32)

    def inner_step(position, state_pair):
        iterate, step_dir = state_pair
        iterate = iterate + step_dir
        resid = rhs - operate(iterate)
        step_dir = keep_table[position] * step_dir + push_table[position] * (jacobi * resid)
        return (iterate, step_dir)

    iterate = jnp.zeros_like(rhs)
    for sweep in range(SWEEPS):
        resid = rhs if sweep == 0 else rhs - operate(iterate)
        step_dir = jacobi * resid / theta_center
        iterate, step_dir = lax.fori_loop(0, STEPS - 1, inner_step, (iterate, step_dir))
        iterate = iterate + step_dir
    return iterate


def local_split(viscosity, friction, base_velocity, grounded, ice_free, direction):
    act = (1 - ice_free).astype(jnp.float32)
    ground = grounded.astype(jnp.float32)
    layer_index = lax.axis_index("vz")
    column_devices = lax.axis_size("vz")
    bed_coef = ground * friction
    padded_eta = padded(viscosity, (("mx", 1), ("my", 2), ("vz", 0)), 1)
    on_bed = jnp.where(layer_index == 0, 1.0, 0.0).astype(jnp.float32)
    core, coefs = coefficients(padded_eta)
    basal = jnp.zeros_like(core).at[0].set(on_bed * bed_coef)
    diag = (
        coefs[0] + coefs[1] + coefs[2] + coefs[3] + coefs[4] + coefs[5] + shift_mass * core + basal
    )
    jacobi = 1.0 / (act * diag + 1.0 - act)
    forcing = jnp.zeros((2,) + core.shape, jnp.float32)
    forcing = forcing.at[:, 0].set(-(on_bed * bed_coef * direction)[None] * base_velocity)
    forcing = forcing * act
    pad_dir = padded(direction, (("mx", 0), ("my", 1)), 1)
    lap = (
        4.0 * direction
        - pad_dir[:-2, 1:-1]
        - pad_dir[2:, 1:-1]
        - pad_dir[1:-1, :-2]
        - pad_dir[1:-1, 2:]
    )

    def operate(field):
        return operate_split(field, coefs, diag, act)

    velocity_step = chebyshev_split(forcing, operate, jacobi)
    column = lax.psum(jnp.sum(velocity_step, axis=1), "vz") / LAYERS
    adjoint_rhs = obs_weight * act * jnp.broadcast_to(column[:, None], velocity_step.shape)
    adjoint = chebyshev_split(adjoint_rhs, operate, jacobi)
    on_top = jnp.where(layer_index == column_devices - 1, 1.0, 0.0).astype(jnp.float32)
    bed_part = on_bed * bed_coef * jnp.sum(base_velocity * adjoint[:, 0], axis=0)
    own_part = on_top * (reg_weight * lap) - bed_part
    hess_action = lax.psum(own_part, "vz")
    return (hess_action, velocity_step)


def solution(mesh):
    return jax.shard_map(
        local,
        mesh=mesh,
        in_specs=(
            P("vz", "mx", "my"),
            P("mx", "my"),
            P(None, "mx", "my"),
            P("mx", "my"),
            P("mx", "my"),
            P("mx", "my"),
        ),
        out_specs=(P("mx", "my"), P(None, "vz", "mx", "my")),
        check_vma=False,
    )
```

```python
import jax
import jax.numpy as jnp
from jax import lax
from jax.experimental import pallas as pl
from jax.experimental.pallas import tpu as pltpu
from jax.sharding import PartitionSpec as P

LAYERS = 16
STEPS = 16
SWEEPS = 2
HALO = 16

weight_z = 128.0
shift_mass = 0.05
theta_center = 1.05
delta_half = 0.95
obs_weight = 200.0
reg_weight = 0.5


def step_constants():
    sigma = theta_center / delta_half
    table = []
    for sweep in range(SWEEPS):
        rho = 1.0 / sigma
        if sweep > 0:
            table.append((None, 1.0 / theta_center))
        for inner in range(STEPS - 1):
            rho_new = 1.0 / (2.0 * sigma - rho)
            table.append((rho_new * rho, 2.0 * rho_new / delta_half))
            rho = rho_new
    return table


def harmonic(left, right):
    total = left + right
    safe = jnp.where(total > 0, total, 1.0)
    return jnp.where(total > 0, 2.0 * left * right / safe, 0.0)


def exchange_rows(ext, k, rows, axis):
    count = lax.axis_size("mx")
    forward = [(i, i + 1) for i in range(count - 1)]
    backward = [(i + 1, i) for i in range(count - 1)]
    own = lax.slice_in_dim(ext, k, k + rows, axis=axis)
    low = lax.ppermute(lax.slice_in_dim(own, rows - k, rows, axis=axis), "mx", forward)
    high = lax.ppermute(lax.slice_in_dim(own, 0, k, axis=axis), "mx", backward)
    return jnp.concatenate([low, own, high], axis=axis)


def gather_axis(block, axis, dim):
    count = lax.axis_size(axis)
    me = lax.axis_index(axis)
    seq = [block]
    for s in range(1, count):
        pairs = [(j, (j - s) % count) for j in range(count)]
        seq.append(lax.ppermute(block, axis, pairs))
    size = block.shape[dim]
    doubled = jnp.concatenate(seq + seq, axis=dim)
    return lax.dynamic_slice_in_dim(doubled, ((count - me) % count) * size, count * size, axis=dim)


def shift(a, axis, offset):
    n = a.shape[axis]
    zeros_shape = list(a.shape)
    zeros_shape[axis] = 1
    z = jnp.zeros(zeros_shape, a.dtype)
    if offset > 0:
        return jnp.concatenate([lax.slice_in_dim(a, 1, n, axis=axis), z], axis=axis)
    return jnp.concatenate([z, lax.slice_in_dim(a, 0, n - 1, axis=axis)], axis=axis)


def segment_kernel(steps, start_valid, halo, send, table_ref, op_ref, rhs_ref, *refs):
    comps, layers = rhs_ref.shape[0], rhs_ref.shape[1]
    rows, cols = rhs_ref.shape[2], rhs_ref.shape[3]
    own = rows - 2 * halo
    if send:
        refs, up_ref, down_ref = refs[:-2], refs[-2], refs[-1]
    if len(refs) == 6:
        x_in, d_in, low_in, high_in, x_ref, d_ref = refs
        x_ref[...] = x_in[...]
        d_ref[...] = d_in[...]

        def place(layer, carry):
            for c in range(comps):
                for f, ref in enumerate((x_ref, d_ref)):
                    ref[c, layer + 1, pl.ds(0, halo)] = low_in[f, c, layer]
                    ref[c, layer + 1, pl.ds(halo + own, halo)] = high_in[f, c, layer]
            return carry

        lax.fori_loop(0, layers, place, 0, unroll=True)
    else:
        x_ref, d_ref = refs
        zero = jnp.zeros((rows, cols), jnp.float32)
        for c in range(comps):
            x_ref[c, 0] = zero
            d_ref[c, 0] = zero
            x_ref[c, layers + 1] = zero
            d_ref[c, layers + 1] = zero

        def start(layer, carry):
            for c in range(comps):
                x_ref[c, layer + 1] = zero
                d_ref[c, layer + 1] = op_ref[5, layer] * rhs_ref[c, layer] / theta_center
            return carry

        lax.fori_loop(0, layers, start, 0, unroll=True)

    def one_step(lo, keep, push):
        span = pl.ds(lo, rows - 2 * lo)
        height = rows - 2 * lo
        for c in range(comps):
            x_ref[c, 1, span] = x_ref[c, 1, span] + d_ref[c, 1, span]

        def update(layer, carry):
            p = layer + 1
            c_xm = op_ref[2, layer, span]
            c_ym = op_ref[3, layer, span]
            c_xp = op_ref[6, layer, span]
            c_yp = op_ref[7, layer, span]
            for c in range(comps):
                above = x_ref[c, p + 1, span] + d_ref[c, p + 1, span]
                x_ref[c, p + 1, span] = above
                centre = x_ref[c, p, span]
                beside = op_ref[0, layer, span] * x_ref[c, p - 1, span] + op_ref[1, layer, span] * above
                beside = beside + c_xm * pltpu.roll(centre, 1, 0)
                beside = beside + c_xp * pltpu.roll(centre, height - 1, 0)
                beside = beside + c_ym * pltpu.roll(centre, 1, 1)
                beside = beside + c_yp * pltpu.roll(centre, cols - 1, 1)
                resid = rhs_ref[c, layer, span] - (op_ref[4, layer, span] * centre - beside)
                if keep is None:
                    d_ref[c, p, span] = op_ref[5, layer, span] * resid / theta_center
                else:
                    d_ref[c, p, span] = keep * d_ref[c, p, span] + push * (op_ref[5, layer, span] * resid)
            return carry

        lax.fori_loop(0, layers, update, 0, unroll=True)

    def row_start(j):
        return max(min(8 * ((start_valid + j) // 8), rows // 2 - 8), 0)

    j = 0
    if steps[0][0] is None:
        one_step(row_start(0), None, None)
        j = 1
    while j < len(steps):
        lo = row_start(j)
        end = j
        while end < len(steps) and row_start(end) == lo:
            end += 1

        def body(i, carry, lo=lo):
            one_step(lo, table_ref[0, i], table_ref[1, i])
            return carry

        lax.fori_loop(j, end, body, 0)
        j = end

    if not send:
        def finish(layer, carry):
            for c in range(comps):
                x_ref[c, layer + 1] = x_ref[c, layer + 1] + d_ref[c, layer + 1]
            return carry

        lax.fori_loop(0, layers, finish, 0, unroll=True)

    if send:
        def pack(layer, carry):
            for c in range(comps):
                for f, ref in enumerate((x_ref, d_ref)):
                    up_ref[f, c, layer] = ref[c, layer + 1, pl.ds(own, halo)]
                    down_ref[f, c, layer] = ref[c, layer + 1, pl.ds(halo, halo)]
            return carry

        lax.fori_loop(0, layers, pack, 0, unroll=True)


def run_segment(steps, start_valid, halo, send, op_stack, rhs, state):
    comps, layers, rows, cols = rhs.shape
    vmem = pl.BlockSpec(memory_space=pltpu.VMEM)
    smem = pl.BlockSpec(memory_space=pltpu.SMEM)
    cells = comps * layers * rows * cols
    table = jnp.array(
        [[0.0 if kp is None else kp for kp, _ in steps], [0.0 if kp is None else ps for kp, ps in steps]],
        jnp.float32,
    )
    padded_shape = jax.ShapeDtypeStruct((comps, layers + 2, rows, cols), jnp.float32)
    slab_shape = jax.ShapeDtypeStruct((2, comps, layers, halo, cols), jnp.float32)
    out_shape = (padded_shape, padded_shape) + ((slab_shape, slab_shape) if send else ())
    return pl.pallas_call(
        lambda *refs: segment_kernel(steps, start_valid, halo, send, *refs),
        out_shape=out_shape,
        in_specs=[smem] + [vmem] * (2 + len(state)),
        out_specs=tuple(vmem for _ in out_shape),
        cost_estimate=pl.CostEstimate(
            flops=20 * cells * len(steps), bytes_accessed=4 * cells * 9, transcendentals=0
        ),
    )(table, op_stack, rhs, *state)


def local(viscosity, friction, base_velocity, grounded, ice_free, direction):
    layers_own, rows, cols_own = viscosity.shape
    if cols_own * lax.axis_size("my") > 256:
        return local_split(viscosity, friction, base_velocity, grounded, ice_free, direction)
    k = min(HALO, rows)
    act = (1 - ice_free).astype(jnp.float32)
    bed_coef = grounded.astype(jnp.float32) * friction
    local_stack = jnp.concatenate(
        [viscosity, act[None], bed_coef[None], base_velocity, direction[None]], axis=0
    )
    if lax.axis_size("vz") == 2 and lax.axis_size("my") == 2:
        swap = [(0, 1), (1, 0)]
        across_my = lax.ppermute(local_stack, "my", swap)
        across_vz = lax.ppermute(viscosity, "vz", swap)
        diagonal = lax.ppermute(viscosity, ("my", "vz"), [(i, 3 - i) for i in range(4)])
        first_my = lax.axis_index("my") == 0
        first_vz = lax.axis_index("vz") == 0

        def by_my(mine, other):
            return jnp.where(first_my, jnp.concatenate([mine, other], axis=2), jnp.concatenate([other, mine], axis=2))

        both = by_my(local_stack, across_my)
        other_half = by_my(across_vz, diagonal)
        mine_half = both[:layers_own]
        eta = jnp.where(
            first_vz,
            jnp.concatenate([mine_half, other_half], axis=0),
            jnp.concatenate([other_half, mine_half], axis=0),
        )
    else:
        both = gather_axis(local_stack, "my", 2)
        eta = gather_axis(both[:layers_own], "vz", 0)
    planes = both[layers_own:]
    layers = eta.shape[0]
    joined = jnp.concatenate([eta, planes], axis=0)
    zeros_halo = jnp.zeros(joined.shape[:1] + (k,) + joined.shape[2:], joined.dtype)
    joined = exchange_rows(jnp.concatenate([zeros_halo, joined, zeros_halo], axis=1), k, rows, 1)
    eta = joined[:layers]
    act, bed_coef, bv0, bv1, dir_ext = (joined[layers + i] for i in range(5))
    bv = jnp.stack([bv0, bv1])

    c_zm = weight_z * harmonic(eta, shift(eta, 0, -1))
    c_zp = weight_z * harmonic(eta, shift(eta, 0, 1))
    c_xm = harmonic(eta, shift(eta, 1, -1))
    c_xp = harmonic(eta, shift(eta, 1, 1))
    c_ym = harmonic(eta, shift(eta, 2, -1))
    c_yp = harmonic(eta, shift(eta, 2, 1))
    basal = jnp.zeros_like(eta).at[0].set(bed_coef)
    diag = c_zm + c_zp + c_xm + c_xp + c_ym + c_yp + shift_mass * eta + basal
    jacobi = 1.0 / (act * diag + 1.0 - act)

    on = act > 0
    op_stack = jnp.stack(
        [
            act * c_zm,
            act * c_zp,
            act * c_xm * shift(act, 0, -1),
            act * c_ym * shift(act, 1, -1),
            jnp.where(on, diag, 1.0),
            jacobi,
            act * c_xp * shift(act, 0, 1),
            act * c_yp * shift(act, 1, 1),
        ]
    )
    table = step_constants()

    def chebyshev(rhs):
        count = lax.axis_size("mx")
        forward = [(i, i + 1) for i in range(count - 1)]
        backward = [(i + 1, i) for i in range(count - 1)]
        state = ()
        since = 1
        start_valid = 1
        run = []
        for keep, push in table:
            if since == k:
                iterate, step_dir, up, down = run_segment(
                    tuple(run), start_valid, k, True, op_stack, rhs, state
                )
                low = lax.ppermute(up, "mx", forward)
                high = lax.ppermute(down, "mx", backward)
                state = (iterate, step_dir, low, high)
                run = []
                start_valid = 0
                since = 0
            run.append((keep, push))
            since += 1
        iterate, _ = run_segment(tuple(run), start_valid, k, False, op_stack, rhs, state)
        return iterate[:, 1 : layers + 1]

    forcing = jnp.zeros((2,) + eta.shape, jnp.float32)
    forcing = forcing.at[:, 0].set(-(bed_coef * dir_ext)[None] * bv)
    forcing = forcing * act
    velocity_ext = chebyshev(forcing)
    column = jnp.sum(velocity_ext, axis=1) / layers
    column = exchange_rows(column, k, rows, 1)
    adjoint_rhs = obs_weight * act * jnp.broadcast_to(column[:, None], velocity_ext.shape)
    adjoint = chebyshev(adjoint_rhs)

    bed_term = bed_coef * jnp.sum(bv * adjoint[:, 0], axis=0)
    lap = (
        4.0 * dir_ext
        - shift(dir_ext, 0, -1)
        - shift(dir_ext, 0, 1)
        - shift(dir_ext, 1, -1)
        - shift(dir_ext, 1, 1)
    )
    hess_ext = -bed_term + reg_weight * lap
    col0 = lax.axis_index("my") * cols_own
    layer0 = lax.axis_index("vz") * layers_own
    hess_action = lax.dynamic_slice(hess_ext, (k, col0), (rows, cols_own))
    velocity_step = lax.dynamic_slice(
        velocity_ext, (0, layer0, k, col0), (2, layers_own, rows, cols_own)
    )
    return (hess_action, velocity_step)


def plain_harmonic(left, right):
    return 2.0 * left * right / (left + right)


def padded(block, sides, width):
    for axis, dim in sides:
        count = lax.axis_size(axis)
        forward = [(i, i + 1) for i in range(count - 1)]
        backward = [(target, source) for source, target in forward]
        low = lax.ppermute(
            lax.slice_in_dim(block, block.shape[dim] - width, None, axis=dim), axis, forward
        )
        high = lax.ppermute(lax.slice_in_dim(block, 0, width, axis=dim), axis, backward)
        block = jnp.concatenate([low, block, high], axis=dim)
    return block


def coefficients(padded_eta):
    core = padded_eta[1:-1, 1:-1, 1:-1]
    coefs = (
        weight_z * plain_harmonic(core, padded_eta[:-2, 1:-1, 1:-1]),
        weight_z * plain_harmonic(core, padded_eta[2:, 1:-1, 1:-1]),
        plain_harmonic(core, padded_eta[1:-1, :-2, 1:-1]),
        plain_harmonic(core, padded_eta[1:-1, 2:, 1:-1]),
        plain_harmonic(core, padded_eta[1:-1, 1:-1, :-2]),
        plain_harmonic(core, padded_eta[1:-1, 1:-1, 2:]),
    )
    return (core, coefs)


def stencil(pad, coefs, diag, masked, act, field):
    beside_all = coefs[0] * pad[:, :-2, 1:-1, 1:-1] + coefs[1] * pad[:, 2:, 1:-1, 1:-1]
    beside_all = beside_all + coefs[2] * pad[:, 1:-1, :-2, 1:-1] + coefs[3] * pad[:, 1:-1, 2:, 1:-1]
    beside_all = beside_all + coefs[4] * pad[:, 1:-1, 1:-1, :-2] + coefs[5] * pad[:, 1:-1, 1:-1, 2:]
    return act * (diag * masked - beside_all) + (1.0 - act) * field


def operate_split(field, coefs, diag, act):
    masked = field * act
    pad = padded(masked, (("mx", 2), ("my", 3), ("vz", 1)), 1)
    return stencil(pad, coefs, diag, masked, act, field)


def chebyshev_split(rhs, operate, jacobi):
    sigma = theta_center / delta_half
    rho = 1.0 / sigma
    keep_list = []
    push_list = []
    for inner in range(STEPS - 1):
        rho_new = 1.0 / (2.0 * sigma - rho)
        keep_list.append(rho_new * rho)
        push_list.append(2.0 * rho_new / delta_half)
        rho = rho_new
    keep_table = jnp.array(keep_list, jnp.float32)
    push_table = jnp.array(push_list, jnp.float32)

    def inner_step(position, state_pair):
        iterate, step_dir = state_pair
        iterate = iterate + step_dir
        resid = rhs - operate(iterate)
        step_dir = keep_table[position] * step_dir + push_table[position] * (jacobi * resid)
        return (iterate, step_dir)

    iterate = jnp.zeros_like(rhs)
    for sweep in range(SWEEPS):
        resid = rhs if sweep == 0 else rhs - operate(iterate)
        step_dir = jacobi * resid / theta_center
        iterate, step_dir = lax.fori_loop(0, STEPS - 1, inner_step, (iterate, step_dir))
        iterate = iterate + step_dir
    return iterate


def local_split(viscosity, friction, base_velocity, grounded, ice_free, direction):
    act = (1 - ice_free).astype(jnp.float32)
    ground = grounded.astype(jnp.float32)
    layer_index = lax.axis_index("vz")
    column_devices = lax.axis_size("vz")
    bed_coef = ground * friction
    padded_eta = padded(viscosity, (("mx", 1), ("my", 2), ("vz", 0)), 1)
    on_bed = jnp.where(layer_index == 0, 1.0, 0.0).astype(jnp.float32)
    core, coefs = coefficients(padded_eta)
    basal = jnp.zeros_like(core).at[0].set(on_bed * bed_coef)
    diag = (
        coefs[0] + coefs[1] + coefs[2] + coefs[3] + coefs[4] + coefs[5] + shift_mass * core + basal
    )
    jacobi = 1.0 / (act * diag + 1.0 - act)
    forcing = jnp.zeros((2,) + core.shape, jnp.float32)
    forcing = forcing.at[:, 0].set(-(on_bed * bed_coef * direction)[None] * base_velocity)
    forcing = forcing * act
    pad_dir = padded(direction, (("mx", 0), ("my", 1)), 1)
    lap = (
        4.0 * direction
        - pad_dir[:-2, 1:-1]
        - pad_dir[2:, 1:-1]
        - pad_dir[1:-1, :-2]
        - pad_dir[1:-1, 2:]
    )

    def operate(field):
        return operate_split(field, coefs, diag, act)

    velocity_step = chebyshev_split(forcing, operate, jacobi)
    column = lax.psum(jnp.sum(velocity_step, axis=1), "vz") / LAYERS
    adjoint_rhs = obs_weight * act * jnp.broadcast_to(column[:, None], velocity_step.shape)
    adjoint = chebyshev_split(adjoint_rhs, operate, jacobi)
    on_top = jnp.where(layer_index == column_devices - 1, 1.0, 0.0).astype(jnp.float32)
    bed_part = on_bed * bed_coef * jnp.sum(base_velocity * adjoint[:, 0], axis=0)
    own_part = on_top * (reg_weight * lap) - bed_part
    hess_action = lax.psum(own_part, "vz")
    return (hess_action, velocity_step)


def solution(mesh):
    return jax.shard_map(
        local,
        mesh=mesh,
        in_specs=(
            P("vz", "mx", "my"),
            P("mx", "my"),
            P(None, "mx", "my"),
            P("mx", "my"),
            P("mx", "my"),
            P("mx", "my"),
        ),
        out_specs=(P("mx", "my"), P(None, "vz", "mx", "my")),
        check_vma=False,
    )
```

```python
import jax
import jax.numpy as jnp
from jax import lax
from jax.experimental import pallas as pl
from jax.experimental.pallas import tpu as pltpu
from jax.sharding import PartitionSpec as P

LAYERS = 16
STEPS = 16
SWEEPS = 2
HALO = 16

weight_z = 128.0
shift_mass = 0.05
theta_center = 1.05
delta_half = 0.95
obs_weight = 200.0
reg_weight = 0.5


def step_constants():
    sigma = theta_center / delta_half
    table = []
    for sweep in range(SWEEPS):
        rho = 1.0 / sigma
        if sweep > 0:
            table.append((None, 1.0 / theta_center))
        for inner in range(STEPS - 1):
            rho_new = 1.0 / (2.0 * sigma - rho)
            table.append((rho_new * rho, 2.0 * rho_new / delta_half))
            rho = rho_new
    return table


def harmonic(left, right):
    total = left + right
    safe = jnp.where(total > 0, total, 1.0)
    return jnp.where(total > 0, 2.0 * left * right / safe, 0.0)


def exchange_rows(ext, k, rows, axis):
    count = lax.axis_size("mx")
    forward = [(i, i + 1) for i in range(count - 1)]
    backward = [(i + 1, i) for i in range(count - 1)]
    own = lax.slice_in_dim(ext, k, k + rows, axis=axis)
    low = lax.ppermute(lax.slice_in_dim(own, rows - k, rows, axis=axis), "mx", forward)
    high = lax.ppermute(lax.slice_in_dim(own, 0, k, axis=axis), "mx", backward)
    return jnp.concatenate([low, own, high], axis=axis)


def gather_axis(block, axis, dim):
    count = lax.axis_size(axis)
    me = lax.axis_index(axis)
    seq = [block]
    for s in range(1, count):
        pairs = [(j, (j - s) % count) for j in range(count)]
        seq.append(lax.ppermute(block, axis, pairs))
    size = block.shape[dim]
    doubled = jnp.concatenate(seq + seq, axis=dim)
    return lax.dynamic_slice_in_dim(doubled, ((count - me) % count) * size, count * size, axis=dim)


def shift(a, axis, offset):
    n = a.shape[axis]
    zeros_shape = list(a.shape)
    zeros_shape[axis] = 1
    z = jnp.zeros(zeros_shape, a.dtype)
    if offset > 0:
        return jnp.concatenate([lax.slice_in_dim(a, 1, n, axis=axis), z], axis=axis)
    return jnp.concatenate([z, lax.slice_in_dim(a, 0, n - 1, axis=axis)], axis=axis)


def segment_kernel(steps, start_valid, halo, send, planes, table_ref, *refs):
    op_ref, rhs_ref, refs = refs[:planes], refs[planes], refs[planes + 1 :]
    comps, layers = rhs_ref.shape[0], rhs_ref.shape[1]
    rows, cols = rhs_ref.shape[2], rhs_ref.shape[3]
    own = rows - 2 * halo
    if send:
        refs, up_ref, down_ref = refs[:-2], refs[-2], refs[-1]
    if len(refs) == 6:
        x_in, d_in, low_in, high_in, x_ref, d_ref = refs
        x_ref[...] = x_in[...]
        d_ref[...] = d_in[...]

        def place(layer, carry):
            for c in range(comps):
                for f, ref in enumerate((x_ref, d_ref)):
                    ref[c, layer + 1, pl.ds(0, halo)] = low_in[f, c, layer]
                    ref[c, layer + 1, pl.ds(halo + own, halo)] = high_in[f, c, layer]
            return carry

        lax.fori_loop(0, layers, place, 0, unroll=True)
    else:
        x_ref, d_ref = refs
        zero = jnp.zeros((rows, cols), jnp.float32)
        for c in range(comps):
            x_ref[c, 0] = zero
            d_ref[c, 0] = zero
            x_ref[c, layers + 1] = zero
            d_ref[c, layers + 1] = zero

        def start(layer, carry):
            for c in range(comps):
                x_ref[c, layer + 1] = zero
                d_ref[c, layer + 1] = op_ref[5][layer] * rhs_ref[c, layer] / theta_center
            return carry

        lax.fori_loop(0, layers, start, 0, unroll=True)

    def one_step(lo, keep, push):
        span = pl.ds(lo, rows - 2 * lo)
        height = rows - 2 * lo
        for c in range(comps):
            x_ref[c, 1, span] = x_ref[c, 1, span] + d_ref[c, 1, span]

        def update(layer, carry):
            p = layer + 1
            c_xm = op_ref[2][layer, span]
            c_ym = op_ref[3][layer, span]
            c_xp = op_ref[6][layer, span]
            c_yp = op_ref[7][layer, span]
            for c in range(comps):
                above = x_ref[c, p + 1, span] + d_ref[c, p + 1, span]
                x_ref[c, p + 1, span] = above
                centre = x_ref[c, p, span]
                beside = op_ref[0][layer, span] * x_ref[c, p - 1, span] + op_ref[1][layer, span] * above
                beside = beside + c_xm * pltpu.roll(centre, 1, 0)
                beside = beside + c_xp * pltpu.roll(centre, height - 1, 0)
                beside = beside + c_ym * pltpu.roll(centre, 1, 1)
                beside = beside + c_yp * pltpu.roll(centre, cols - 1, 1)
                resid = rhs_ref[c, layer, span] - (op_ref[4][layer, span] * centre - beside)
                if keep is None:
                    d_ref[c, p, span] = op_ref[5][layer, span] * resid / theta_center
                else:
                    d_ref[c, p, span] = keep * d_ref[c, p, span] + push * (op_ref[5][layer, span] * resid)
            return carry

        lax.fori_loop(0, layers, update, 0, unroll=True)

    def row_start(j):
        return max(min(8 * ((start_valid + j) // 8), rows // 2 - 8), 0)

    j = 0
    if steps[0][0] is None:
        one_step(row_start(0), None, None)
        j = 1
    while j < len(steps):
        lo = row_start(j)
        end = j
        while end < len(steps) and row_start(end) == lo:
            end += 1

        def body(i, carry, lo=lo):
            one_step(lo, table_ref[0, i], table_ref[1, i])
            return carry

        lax.fori_loop(j, end, body, 0)
        j = end

    if not send:
        def finish(layer, carry):
            for c in range(comps):
                x_ref[c, layer + 1] = x_ref[c, layer + 1] + d_ref[c, layer + 1]
            return carry

        lax.fori_loop(0, layers, finish, 0, unroll=True)

    if send:
        def pack(layer, carry):
            for c in range(comps):
                for f, ref in enumerate((x_ref, d_ref)):
                    up_ref[f, c, layer] = ref[c, layer + 1, pl.ds(own, halo)]
                    down_ref[f, c, layer] = ref[c, layer + 1, pl.ds(halo, halo)]
            return carry

        lax.fori_loop(0, layers, pack, 0, unroll=True)


def run_segment(steps, start_valid, halo, send, op_stack, rhs, state):
    comps, layers, rows, cols = rhs.shape
    vmem = pl.BlockSpec(memory_space=pltpu.VMEM)
    smem = pl.BlockSpec(memory_space=pltpu.SMEM)
    cells = comps * layers * rows * cols
    table = jnp.array(
        [[0.0 if kp is None else kp for kp, _ in steps], [0.0 if kp is None else ps for kp, ps in steps]],
        jnp.float32,
    )
    padded_shape = jax.ShapeDtypeStruct((comps, layers + 2, rows, cols), jnp.float32)
    slab_shape = jax.ShapeDtypeStruct((2, comps, layers, halo, cols), jnp.float32)
    out_shape = (padded_shape, padded_shape) + ((slab_shape, slab_shape) if send else ())
    return pl.pallas_call(
        lambda *refs: segment_kernel(steps, start_valid, halo, send, len(op_stack), *refs),
        out_shape=out_shape,
        in_specs=[smem] + [vmem] * (len(op_stack) + 1 + len(state)),
        out_specs=tuple(vmem for _ in out_shape),
        cost_estimate=pl.CostEstimate(
            flops=20 * cells * len(steps), bytes_accessed=4 * cells * 9, transcendentals=0
        ),
    )(table, *op_stack, rhs, *state)


def local(viscosity, friction, base_velocity, grounded, ice_free, direction):
    layers_own, rows, cols_own = viscosity.shape
    if cols_own * lax.axis_size("my") > 256:
        return local_split(viscosity, friction, base_velocity, grounded, ice_free, direction)
    k = min(HALO, rows)
    act = (1 - ice_free).astype(jnp.float32)
    bed_coef = grounded.astype(jnp.float32) * friction
    local_stack = jnp.concatenate(
        [viscosity, act[None], bed_coef[None], base_velocity, direction[None]], axis=0
    )
    if lax.axis_size("vz") == 2 and lax.axis_size("my") == 2:
        swap = [(0, 1), (1, 0)]
        across_my = lax.ppermute(local_stack, "my", swap)
        across_vz = lax.ppermute(viscosity, "vz", swap)
        diagonal = lax.ppermute(viscosity, ("my", "vz"), [(i, 3 - i) for i in range(4)])
        first_my = lax.axis_index("my") == 0
        first_vz = lax.axis_index("vz") == 0

        def by_my(mine, other):
            return jnp.where(first_my, jnp.concatenate([mine, other], axis=2), jnp.concatenate([other, mine], axis=2))

        both = by_my(local_stack, across_my)
        other_half = by_my(across_vz, diagonal)
        mine_half = both[:layers_own]
        eta = jnp.where(
            first_vz,
            jnp.concatenate([mine_half, other_half], axis=0),
            jnp.concatenate([other_half, mine_half], axis=0),
        )
    else:
        both = gather_axis(local_stack, "my", 2)
        eta = gather_axis(both[:layers_own], "vz", 0)
    planes = both[layers_own:]
    layers = eta.shape[0]
    joined = jnp.concatenate([eta, planes], axis=0)
    zeros_halo = jnp.zeros(joined.shape[:1] + (k,) + joined.shape[2:], joined.dtype)
    joined = exchange_rows(jnp.concatenate([zeros_halo, joined, zeros_halo], axis=1), k, rows, 1)
    eta = joined[:layers]
    act, bed_coef, bv0, bv1, dir_ext = (joined[layers + i] for i in range(5))
    bv = jnp.stack([bv0, bv1])

    c_zm = weight_z * harmonic(eta, shift(eta, 0, -1))
    c_zp = weight_z * harmonic(eta, shift(eta, 0, 1))
    c_xm = harmonic(eta, shift(eta, 1, -1))
    c_xp = harmonic(eta, shift(eta, 1, 1))
    c_ym = harmonic(eta, shift(eta, 2, -1))
    c_yp = harmonic(eta, shift(eta, 2, 1))
    basal = jnp.zeros_like(eta).at[0].set(bed_coef)
    diag = c_zm + c_zp + c_xm + c_xp + c_ym + c_yp + shift_mass * eta + basal
    jacobi = 1.0 / (act * diag + 1.0 - act)

    on = act > 0
    op_stack = tuple(
        [
            act * c_zm,
            act * c_zp,
            act * c_xm * shift(act, 0, -1),
            act * c_ym * shift(act, 1, -1),
            jnp.where(on, diag, 1.0),
            jacobi,
            act * c_xp * shift(act, 0, 1),
            act * c_yp * shift(act, 1, 1),
        ]
    )
    table = step_constants()

    def chebyshev(rhs):
        count = lax.axis_size("mx")
        forward = [(i, i + 1) for i in range(count - 1)]
        backward = [(i + 1, i) for i in range(count - 1)]
        state = ()
        since = 1
        start_valid = 1
        run = []
        for keep, push in table:
            if since == k:
                iterate, step_dir, up, down = run_segment(
                    tuple(run), start_valid, k, True, op_stack, rhs, state
                )
                low = lax.ppermute(up, "mx", forward)
                high = lax.ppermute(down, "mx", backward)
                state = (iterate, step_dir, low, high)
                run = []
                start_valid = 0
                since = 0
            run.append((keep, push))
            since += 1
        iterate, _ = run_segment(tuple(run), start_valid, k, False, op_stack, rhs, state)
        return iterate[:, 1 : layers + 1]

    forcing = jnp.zeros((2,) + eta.shape, jnp.float32)
    forcing = forcing.at[:, 0].set(-(bed_coef * dir_ext)[None] * bv)
    forcing = forcing * act
    velocity_ext = chebyshev(forcing)
    column = jnp.sum(velocity_ext, axis=1) / layers
    column = exchange_rows(column, k, rows, 1)
    adjoint_rhs = obs_weight * act * jnp.broadcast_to(column[:, None], velocity_ext.shape)
    adjoint = chebyshev(adjoint_rhs)

    bed_term = bed_coef * jnp.sum(bv * adjoint[:, 0], axis=0)
    lap = (
        4.0 * dir_ext
        - shift(dir_ext, 0, -1)
        - shift(dir_ext, 0, 1)
        - shift(dir_ext, 1, -1)
        - shift(dir_ext, 1, 1)
    )
    hess_ext = -bed_term + reg_weight * lap
    col0 = lax.axis_index("my") * cols_own
    layer0 = lax.axis_index("vz") * layers_own
    hess_action = lax.dynamic_slice(hess_ext, (k, col0), (rows, cols_own))
    velocity_step = lax.dynamic_slice(
        velocity_ext, (0, layer0, k, col0), (2, layers_own, rows, cols_own)
    )
    return (hess_action, velocity_step)


def plain_harmonic(left, right):
    return 2.0 * left * right / (left + right)


def padded(block, sides, width):
    for axis, dim in sides:
        count = lax.axis_size(axis)
        forward = [(i, i + 1) for i in range(count - 1)]
        backward = [(target, source) for source, target in forward]
        low = lax.ppermute(
            lax.slice_in_dim(block, block.shape[dim] - width, None, axis=dim), axis, forward
        )
        high = lax.ppermute(lax.slice_in_dim(block, 0, width, axis=dim), axis, backward)
        block = jnp.concatenate([low, block, high], axis=dim)
    return block


def coefficients(padded_eta):
    core = padded_eta[1:-1, 1:-1, 1:-1]
    coefs = (
        weight_z * plain_harmonic(core, padded_eta[:-2, 1:-1, 1:-1]),
        weight_z * plain_harmonic(core, padded_eta[2:, 1:-1, 1:-1]),
        plain_harmonic(core, padded_eta[1:-1, :-2, 1:-1]),
        plain_harmonic(core, padded_eta[1:-1, 2:, 1:-1]),
        plain_harmonic(core, padded_eta[1:-1, 1:-1, :-2]),
        plain_harmonic(core, padded_eta[1:-1, 1:-1, 2:]),
    )
    return (core, coefs)


def stencil(pad, coefs, diag, masked, act, field):
    beside_all = coefs[0] * pad[:, :-2, 1:-1, 1:-1] + coefs[1] * pad[:, 2:, 1:-1, 1:-1]
    beside_all = beside_all + coefs[2] * pad[:, 1:-1, :-2, 1:-1] + coefs[3] * pad[:, 1:-1, 2:, 1:-1]
    beside_all = beside_all + coefs[4] * pad[:, 1:-1, 1:-1, :-2] + coefs[5] * pad[:, 1:-1, 1:-1, 2:]
    return act * (diag * masked - beside_all) + (1.0 - act) * field


def operate_split(field, coefs, diag, act):
    masked = field * act
    pad = padded(masked, (("mx", 2), ("my", 3), ("vz", 1)), 1)
    return stencil(pad, coefs, diag, masked, act, field)


def chebyshev_split(rhs, operate, jacobi):
    sigma = theta_center / delta_half
    rho = 1.0 / sigma
    keep_list = []
    push_list = []
    for inner in range(STEPS - 1):
        rho_new = 1.0 / (2.0 * sigma - rho)
        keep_list.append(rho_new * rho)
        push_list.append(2.0 * rho_new / delta_half)
        rho = rho_new
    keep_table = jnp.array(keep_list, jnp.float32)
    push_table = jnp.array(push_list, jnp.float32)

    def inner_step(position, state_pair):
        iterate, step_dir = state_pair
        iterate = iterate + step_dir
        resid = rhs - operate(iterate)
        step_dir = keep_table[position] * step_dir + push_table[position] * (jacobi * resid)
        return (iterate, step_dir)

    iterate = jnp.zeros_like(rhs)
    for sweep in range(SWEEPS):
        resid = rhs if sweep == 0 else rhs - operate(iterate)
        step_dir = jacobi * resid / theta_center
        iterate, step_dir = lax.fori_loop(0, STEPS - 1, inner_step, (iterate, step_dir))
        iterate = iterate + step_dir
    return iterate


def local_split(viscosity, friction, base_velocity, grounded, ice_free, direction):
    act = (1 - ice_free).astype(jnp.float32)
    ground = grounded.astype(jnp.float32)
    layer_index = lax.axis_index("vz")
    column_devices = lax.axis_size("vz")
    bed_coef = ground * friction
    padded_eta = padded(viscosity, (("mx", 1), ("my", 2), ("vz", 0)), 1)
    on_bed = jnp.where(layer_index == 0, 1.0, 0.0).astype(jnp.float32)
    core, coefs = coefficients(padded_eta)
    basal = jnp.zeros_like(core).at[0].set(on_bed * bed_coef)
    diag = (
        coefs[0] + coefs[1] + coefs[2] + coefs[3] + coefs[4] + coefs[5] + shift_mass * core + basal
    )
    jacobi = 1.0 / (act * diag + 1.0 - act)
    forcing = jnp.zeros((2,) + core.shape, jnp.float32)
    forcing = forcing.at[:, 0].set(-(on_bed * bed_coef * direction)[None] * base_velocity)
    forcing = forcing * act
    pad_dir = padded(direction, (("mx", 0), ("my", 1)), 1)
    lap = (
        4.0 * direction
        - pad_dir[:-2, 1:-1]
        - pad_dir[2:, 1:-1]
        - pad_dir[1:-1, :-2]
        - pad_dir[1:-1, 2:]
    )

    def operate(field):
        return operate_split(field, coefs, diag, act)

    velocity_step = chebyshev_split(forcing, operate, jacobi)
    column = lax.psum(jnp.sum(velocity_step, axis=1), "vz") / LAYERS
    adjoint_rhs = obs_weight * act * jnp.broadcast_to(column[:, None], velocity_step.shape)
    adjoint = chebyshev_split(adjoint_rhs, operate, jacobi)
    on_top = jnp.where(layer_index == column_devices - 1, 1.0, 0.0).astype(jnp.float32)
    bed_part = on_bed * bed_coef * jnp.sum(base_velocity * adjoint[:, 0], axis=0)
    own_part = on_top * (reg_weight * lap) - bed_part
    hess_action = lax.psum(own_part, "vz")
    return (hess_action, velocity_step)


def solution(mesh):
    return jax.shard_map(
        local,
        mesh=mesh,
        in_specs=(
            P("vz", "mx", "my"),
            P("mx", "my"),
            P(None, "mx", "my"),
            P("mx", "my"),
            P("mx", "my"),
            P("mx", "my"),
        ),
        out_specs=(P("mx", "my"), P(None, "vz", "mx", "my")),
        check_vma=False,
    )
```

```python
import jax
import jax.numpy as jnp
from jax import lax
from jax.experimental import pallas as pl
from jax.experimental.pallas import tpu as pltpu
from jax.sharding import PartitionSpec as P

LAYERS = 16
STEPS = 16
SWEEPS = 2
HALO = 16

weight_z = 128.0
shift_mass = 0.05
theta_center = 1.05
delta_half = 0.95
obs_weight = 200.0
reg_weight = 0.5


def step_constants():
    sigma = theta_center / delta_half
    table = []
    for sweep in range(SWEEPS):
        rho = 1.0 / sigma
        if sweep > 0:
            table.append((None, 1.0 / theta_center))
        for inner in range(STEPS - 1):
            rho_new = 1.0 / (2.0 * sigma - rho)
            table.append((rho_new * rho, 2.0 * rho_new / delta_half))
            rho = rho_new
    return table


def harmonic(left, right):
    total = left + right
    safe = jnp.where(total > 0, total, 1.0)
    return jnp.where(total > 0, 2.0 * left * right / safe, 0.0)


def exchange_rows(ext, k, rows, axis):
    count = lax.axis_size("mx")
    forward = [(i, i + 1) for i in range(count - 1)]
    backward = [(i + 1, i) for i in range(count - 1)]
    own = lax.slice_in_dim(ext, k, k + rows, axis=axis)
    low = lax.ppermute(lax.slice_in_dim(own, rows - k, rows, axis=axis), "mx", forward)
    high = lax.ppermute(lax.slice_in_dim(own, 0, k, axis=axis), "mx", backward)
    return jnp.concatenate([low, own, high], axis=axis)


def gather_axis(block, axis, dim):
    count = lax.axis_size(axis)
    me = lax.axis_index(axis)
    seq = [block]
    for s in range(1, count):
        pairs = [(j, (j - s) % count) for j in range(count)]
        seq.append(lax.ppermute(block, axis, pairs))
    size = block.shape[dim]
    doubled = jnp.concatenate(seq + seq, axis=dim)
    return lax.dynamic_slice_in_dim(doubled, ((count - me) % count) * size, count * size, axis=dim)


def shift(a, axis, offset):
    n = a.shape[axis]
    zeros_shape = list(a.shape)
    zeros_shape[axis] = 1
    z = jnp.zeros(zeros_shape, a.dtype)
    if offset > 0:
        return jnp.concatenate([lax.slice_in_dim(a, 1, n, axis=axis), z], axis=axis)
    return jnp.concatenate([z, lax.slice_in_dim(a, 0, n - 1, axis=axis)], axis=axis)


def segment_kernel(steps, start_valid, halo, send, planes, table_ref, *refs):
    op_ref, rhs_ref, refs = refs[:planes], refs[planes], refs[planes + 1 :]
    comps, layers = rhs_ref.shape[0], rhs_ref.shape[1]
    rows, cols = rhs_ref.shape[2], rhs_ref.shape[3]
    own = rows - 2 * halo
    if send:
        refs, up_ref, down_ref = refs[:-2], refs[-2], refs[-1]
    if len(refs) == 6:
        x_in, d_in, low_in, high_in, x_ref, d_ref = refs
        x_ref[...] = x_in[...]
        d_ref[...] = d_in[...]

        def place(layer, carry):
            for c in range(comps):
                for f, ref in enumerate((x_ref, d_ref)):
                    ref[c, layer + 1, pl.ds(0, halo)] = low_in[f, c, layer]
                    ref[c, layer + 1, pl.ds(halo + own, halo)] = high_in[f, c, layer]
            return carry

        lax.fori_loop(0, layers, place, 0, unroll=True)
    else:
        x_ref, d_ref = refs
        zero = jnp.zeros((rows, cols), jnp.float32)
        for c in range(comps):
            x_ref[c, 0] = zero
            d_ref[c, 0] = zero
            x_ref[c, layers + 1] = zero
            d_ref[c, layers + 1] = zero

        def start(layer, carry):
            for c in range(comps):
                x_ref[c, layer + 1] = zero
                d_ref[c, layer + 1] = op_ref[5][layer] * rhs_ref[c, layer] / theta_center
            return carry

        lax.fori_loop(0, layers, start, 0, unroll=True)

    def one_step(lo, keep, push):
        span = pl.ds(lo, rows - 2 * lo)
        height = rows - 2 * lo
        for c in range(comps):
            x_ref[c, 1, span] = x_ref[c, 1, span] + d_ref[c, 1, span]

        def update(layer, carry):
            p = layer + 1
            c_xm = op_ref[2][layer, span]
            c_ym = op_ref[3][layer, span]
            c_xp = op_ref[6][layer, span]
            c_yp = op_ref[7][layer, span]
            for c in range(comps):
                above = x_ref[c, p + 1, span] + d_ref[c, p + 1, span]
                x_ref[c, p + 1, span] = above
                centre = x_ref[c, p, span]
                beside = op_ref[0][layer, span] * x_ref[c, p - 1, span] + op_ref[1][layer, span] * above
                beside = beside + c_xm * pltpu.roll(centre, 1, 0)
                beside = beside + c_xp * pltpu.roll(centre, height - 1, 0)
                beside = beside + c_ym * pltpu.roll(centre, 1, 1)
                beside = beside + c_yp * pltpu.roll(centre, cols - 1, 1)
                resid = rhs_ref[c, layer, span] - (op_ref[4][layer, span] * centre - beside)
                if keep is None:
                    d_ref[c, p, span] = op_ref[5][layer, span] * resid / theta_center
                else:
                    d_ref[c, p, span] = keep * d_ref[c, p, span] + push * (op_ref[5][layer, span] * resid)
            return carry

        lax.fori_loop(0, layers, update, 0, unroll=True)

    def row_start(j):
        return max(min(8 * ((start_valid + j) // 8), rows // 2 - 8), 0)

    j = 0
    if steps[0][0] is None:
        one_step(row_start(0), None, None)
        j = 1
    while j < len(steps):
        lo = row_start(j)
        end = j
        while end < len(steps) and row_start(end) == lo:
            end += 1

        def body(i, carry, lo=lo):
            one_step(lo, table_ref[0, i], table_ref[1, i])
            return carry

        lax.fori_loop(j, end, body, 0)
        j = end

    if not send:
        def finish(layer, carry):
            for c in range(comps):
                x_ref[c, layer + 1] = x_ref[c, layer + 1] + d_ref[c, layer + 1]
            return carry

        lax.fori_loop(0, layers, finish, 0, unroll=True)

    if send:
        def pack(layer, carry):
            for c in range(comps):
                for f, ref in enumerate((x_ref, d_ref)):
                    up_ref[f, c, layer] = ref[c, layer + 1, pl.ds(own, halo)]
                    down_ref[f, c, layer] = ref[c, layer + 1, pl.ds(halo, halo)]
            return carry

        lax.fori_loop(0, layers, pack, 0, unroll=True)


def run_segment(steps, start_valid, halo, send, op_stack, rhs, state):
    comps, layers, rows, cols = rhs.shape
    vmem = pl.BlockSpec(memory_space=pltpu.VMEM)
    smem = pl.BlockSpec(memory_space=pltpu.SMEM)
    cells = comps * layers * rows * cols
    table = jnp.array(
        [[0.0 if kp is None else kp for kp, _ in steps], [0.0 if kp is None else ps for kp, ps in steps]],
        jnp.float32,
    )
    padded_shape = jax.ShapeDtypeStruct((comps, layers + 2, rows, cols), jnp.float32)
    slab_shape = jax.ShapeDtypeStruct((2, comps, layers, halo, cols), jnp.float32)
    out_shape = (padded_shape, padded_shape, slab_shape, slab_shape) if send else (padded_shape,)
    scratch = [] if send else [pltpu.VMEM(padded_shape.shape, jnp.float32)]
    return pl.pallas_call(
        lambda *refs: segment_kernel(steps, start_valid, halo, send, len(op_stack), *refs),
        out_shape=out_shape,
        in_specs=[smem] + [vmem] * (len(op_stack) + 1 + len(state)),
        out_specs=tuple(vmem for _ in out_shape),
        scratch_shapes=scratch,
        cost_estimate=pl.CostEstimate(
            flops=20 * cells * len(steps), bytes_accessed=4 * cells * 9, transcendentals=0
        ),
    )(table, *op_stack, rhs, *state)


def local(viscosity, friction, base_velocity, grounded, ice_free, direction):
    layers_own, rows, cols_own = viscosity.shape
    if cols_own * lax.axis_size("my") > 256:
        return local_split(viscosity, friction, base_velocity, grounded, ice_free, direction)
    k = min(HALO, rows)
    act = (1 - ice_free).astype(jnp.float32)
    bed_coef = grounded.astype(jnp.float32) * friction
    local_stack = jnp.concatenate(
        [viscosity, act[None], bed_coef[None], base_velocity, direction[None]], axis=0
    )
    if lax.axis_size("vz") == 2 and lax.axis_size("my") == 2:
        swap = [(0, 1), (1, 0)]
        across_my = lax.ppermute(local_stack, "my", swap)
        across_vz = lax.ppermute(viscosity, "vz", swap)
        diagonal = lax.ppermute(viscosity, ("my", "vz"), [(i, 3 - i) for i in range(4)])
        first_my = lax.axis_index("my") == 0
        first_vz = lax.axis_index("vz") == 0

        def by_my(mine, other):
            return jnp.where(first_my, jnp.concatenate([mine, other], axis=2), jnp.concatenate([other, mine], axis=2))

        both = by_my(local_stack, across_my)
        other_half = by_my(across_vz, diagonal)
        mine_half = both[:layers_own]
        eta = jnp.where(
            first_vz,
            jnp.concatenate([mine_half, other_half], axis=0),
            jnp.concatenate([other_half, mine_half], axis=0),
        )
    else:
        both = gather_axis(local_stack, "my", 2)
        eta = gather_axis(both[:layers_own], "vz", 0)
    planes = both[layers_own:]
    layers = eta.shape[0]
    joined = jnp.concatenate([eta, planes], axis=0)
    zeros_halo = jnp.zeros(joined.shape[:1] + (k,) + joined.shape[2:], joined.dtype)
    joined = exchange_rows(jnp.concatenate([zeros_halo, joined, zeros_halo], axis=1), k, rows, 1)
    eta = joined[:layers]
    act, bed_coef, bv0, bv1, dir_ext = (joined[layers + i] for i in range(5))
    bv = jnp.stack([bv0, bv1])

    c_zm = weight_z * harmonic(eta, shift(eta, 0, -1))
    c_zp = weight_z * harmonic(eta, shift(eta, 0, 1))
    c_xm = harmonic(eta, shift(eta, 1, -1))
    c_xp = harmonic(eta, shift(eta, 1, 1))
    c_ym = harmonic(eta, shift(eta, 2, -1))
    c_yp = harmonic(eta, shift(eta, 2, 1))
    basal = jnp.zeros_like(eta).at[0].set(bed_coef)
    diag = c_zm + c_zp + c_xm + c_xp + c_ym + c_yp + shift_mass * eta + basal
    jacobi = 1.0 / (act * diag + 1.0 - act)

    on = act > 0
    op_stack = tuple(
        [
            act * c_zm,
            act * c_zp,
            act * c_xm * shift(act, 0, -1),
            act * c_ym * shift(act, 1, -1),
            jnp.where(on, diag, 1.0),
            jacobi,
            act * c_xp * shift(act, 0, 1),
            act * c_yp * shift(act, 1, 1),
        ]
    )
    table = step_constants()

    def chebyshev(rhs):
        count = lax.axis_size("mx")
        forward = [(i, i + 1) for i in range(count - 1)]
        backward = [(i + 1, i) for i in range(count - 1)]
        state = ()
        since = 1
        start_valid = 1
        run = []
        for keep, push in table:
            if since == k:
                iterate, step_dir, up, down = run_segment(
                    tuple(run), start_valid, k, True, op_stack, rhs, state
                )
                low = lax.ppermute(up, "mx", forward)
                high = lax.ppermute(down, "mx", backward)
                state = (iterate, step_dir, low, high)
                run = []
                start_valid = 0
                since = 0
            run.append((keep, push))
            since += 1
        iterate = run_segment(tuple(run), start_valid, k, False, op_stack, rhs, state)[0]
        return iterate[:, 1 : layers + 1]

    forcing = jnp.zeros((2,) + eta.shape, jnp.float32)
    forcing = forcing.at[:, 0].set(-(bed_coef * dir_ext)[None] * bv)
    forcing = forcing * act
    velocity_ext = chebyshev(forcing)
    column = jnp.sum(velocity_ext, axis=1) / layers
    column = exchange_rows(column, k, rows, 1)
    adjoint_rhs = obs_weight * act * jnp.broadcast_to(column[:, None], velocity_ext.shape)
    adjoint = chebyshev(adjoint_rhs)

    bed_term = bed_coef * jnp.sum(bv * adjoint[:, 0], axis=0)
    lap = (
        4.0 * dir_ext
        - shift(dir_ext, 0, -1)
        - shift(dir_ext, 0, 1)
        - shift(dir_ext, 1, -1)
        - shift(dir_ext, 1, 1)
    )
    hess_ext = -bed_term + reg_weight * lap
    col0 = lax.axis_index("my") * cols_own
    layer0 = lax.axis_index("vz") * layers_own
    hess_action = lax.dynamic_slice(hess_ext, (k, col0), (rows, cols_own))
    velocity_step = lax.dynamic_slice(
        velocity_ext, (0, layer0, k, col0), (2, layers_own, rows, cols_own)
    )
    return (hess_action, velocity_step)


def plain_harmonic(left, right):
    return 2.0 * left * right / (left + right)


def padded(block, sides, width):
    for axis, dim in sides:
        count = lax.axis_size(axis)
        forward = [(i, i + 1) for i in range(count - 1)]
        backward = [(target, source) for source, target in forward]
        low = lax.ppermute(
            lax.slice_in_dim(block, block.shape[dim] - width, None, axis=dim), axis, forward
        )
        high = lax.ppermute(lax.slice_in_dim(block, 0, width, axis=dim), axis, backward)
        block = jnp.concatenate([low, block, high], axis=dim)
    return block


def coefficients(padded_eta):
    core = padded_eta[1:-1, 1:-1, 1:-1]
    coefs = (
        weight_z * plain_harmonic(core, padded_eta[:-2, 1:-1, 1:-1]),
        weight_z * plain_harmonic(core, padded_eta[2:, 1:-1, 1:-1]),
        plain_harmonic(core, padded_eta[1:-1, :-2, 1:-1]),
        plain_harmonic(core, padded_eta[1:-1, 2:, 1:-1]),
        plain_harmonic(core, padded_eta[1:-1, 1:-1, :-2]),
        plain_harmonic(core, padded_eta[1:-1, 1:-1, 2:]),
    )
    return (core, coefs)


def stencil(pad, coefs, diag, masked, act, field):
    beside_all = coefs[0] * pad[:, :-2, 1:-1, 1:-1] + coefs[1] * pad[:, 2:, 1:-1, 1:-1]
    beside_all = beside_all + coefs[2] * pad[:, 1:-1, :-2, 1:-1] + coefs[3] * pad[:, 1:-1, 2:, 1:-1]
    beside_all = beside_all + coefs[4] * pad[:, 1:-1, 1:-1, :-2] + coefs[5] * pad[:, 1:-1, 1:-1, 2:]
    return act * (diag * masked - beside_all) + (1.0 - act) * field


def operate_split(field, coefs, diag, act):
    masked = field * act
    pad = padded(masked, (("mx", 2), ("my", 3), ("vz", 1)), 1)
    return stencil(pad, coefs, diag, masked, act, field)


def chebyshev_split(rhs, operate, jacobi):
    sigma = theta_center / delta_half
    rho = 1.0 / sigma
    keep_list = []
    push_list = []
    for inner in range(STEPS - 1):
        rho_new = 1.0 / (2.0 * sigma - rho)
        keep_list.append(rho_new * rho)
        push_list.append(2.0 * rho_new / delta_half)
        rho = rho_new
    keep_table = jnp.array(keep_list, jnp.float32)
    push_table = jnp.array(push_list, jnp.float32)

    def inner_step(position, state_pair):
        iterate, step_dir = state_pair
        iterate = iterate + step_dir
        resid = rhs - operate(iterate)
        step_dir = keep_table[position] * step_dir + push_table[position] * (jacobi * resid)
        return (iterate, step_dir)

    iterate = jnp.zeros_like(rhs)
    for sweep in range(SWEEPS):
        resid = rhs if sweep == 0 else rhs - operate(iterate)
        step_dir = jacobi * resid / theta_center
        iterate, step_dir = lax.fori_loop(0, STEPS - 1, inner_step, (iterate, step_dir))
        iterate = iterate + step_dir
    return iterate


def local_split(viscosity, friction, base_velocity, grounded, ice_free, direction):
    act = (1 - ice_free).astype(jnp.float32)
    ground = grounded.astype(jnp.float32)
    layer_index = lax.axis_index("vz")
    column_devices = lax.axis_size("vz")
    bed_coef = ground * friction
    padded_eta = padded(viscosity, (("mx", 1), ("my", 2), ("vz", 0)), 1)
    on_bed = jnp.where(layer_index == 0, 1.0, 0.0).astype(jnp.float32)
    core, coefs = coefficients(padded_eta)
    basal = jnp.zeros_like(core).at[0].set(on_bed * bed_coef)
    diag = (
        coefs[0] + coefs[1] + coefs[2] + coefs[3] + coefs[4] + coefs[5] + shift_mass * core + basal
    )
    jacobi = 1.0 / (act * diag + 1.0 - act)
    forcing = jnp.zeros((2,) + core.shape, jnp.float32)
    forcing = forcing.at[:, 0].set(-(on_bed * bed_coef * direction)[None] * base_velocity)
    forcing = forcing * act
    pad_dir = padded(direction, (("mx", 0), ("my", 1)), 1)
    lap = (
        4.0 * direction
        - pad_dir[:-2, 1:-1]
        - pad_dir[2:, 1:-1]
        - pad_dir[1:-1, :-2]
        - pad_dir[1:-1, 2:]
    )

    def operate(field):
        return operate_split(field, coefs, diag, act)

    velocity_step = chebyshev_split(forcing, operate, jacobi)
    column = lax.psum(jnp.sum(velocity_step, axis=1), "vz") / LAYERS
    adjoint_rhs = obs_weight * act * jnp.broadcast_to(column[:, None], velocity_step.shape)
    adjoint = chebyshev_split(adjoint_rhs, operate, jacobi)
    on_top = jnp.where(layer_index == column_devices - 1, 1.0, 0.0).astype(jnp.float32)
    bed_part = on_bed * bed_coef * jnp.sum(base_velocity * adjoint[:, 0], axis=0)
    own_part = on_top * (reg_weight * lap) - bed_part
    hess_action = lax.psum(own_part, "vz")
    return (hess_action, velocity_step)


def solution(mesh):
    return jax.shard_map(
        local,
        mesh=mesh,
        in_specs=(
            P("vz", "mx", "my"),
            P("mx", "my"),
            P(None, "mx", "my"),
            P("mx", "my"),
            P("mx", "my"),
            P("mx", "my"),
        ),
        out_specs=(P("mx", "my"), P(None, "vz", "mx", "my")),
        check_vma=False,
    )
```
